32 devices in a mesh: row: 4 (over z), col: 8 (over y, x, core).
Axes of the slice: x: 2, y: 2, z: 4, core: 2. Of those that a mesh axis runs over, the one named last changes fastest.
Arguments:
- points: bfloat16 [196608, 128], P(('row', 'col')), may hold values from -6 to 6
- weights: bfloat16 [196608, 256], P(('row', 'col')), may hold values from -6 to 6
- leaf_basis: bfloat16 [196608, 128], P(('row', 'col')), may hold values from -0.75 to 0.75
- leaf_rank: int32 [768], P(('row', 'col')), may hold values from 64 to 128
- leaf_skeleton: int32 [768, 128], P(('row', 'col')), may hold values from 0 to 255, as said below
- near_list: int32 [768, 5], P(('row', 'col')), may hold values from 0 to 767, as said below
- far_list: int32 [768, 4], P(('row', 'col')), may hold values from 0 to 767, as said below
- node_basis: bfloat16 [98304, 128], P(('row', 'col')), may hold values from -0.15625 to 0.15625
- node_rank: int32 [32], P(('row', 'col')), may hold values from 64 to 128
- node_skeleton: int32 [32, 128], P(('row', 'col')), may hold values from 0 to 3071, as said below
- node_far: int32 [32, 4], P(('row', 'col')), may hold values from 0 to 31, as said below
- group_basis: bfloat16 [4096, 128], P(('row', 'col')), may hold values from -0.375 to 0.375
- group_rank: int32 [4], P('row'), may hold values from 32 to 128
- group_skeleton: int32 [4, 128], P('row'), may hold values from 0 to 1023, as said below
- group_far: int32 [4, 2], P('row'), may hold values from 0 to 3, as said below
Outputs:
- potentials: bfloat16 [196608, 256], P(('row', 'col'))
The draws below stay inside these ranges and needn't reach their ends.
Inputs may be any that keep to these rules, and one draw needn't show every extreme that they name: `near_list`: each row lists distinct leaves within 8 leaves of its own leaf; the first entry is the leaf itself. `far_list`: each row lists distinct leaves within 8 leaves of its own leaf, none of them in the same row of near_list. `leaf_skeleton`: distinct within a row. `node_skeleton`: distinct within a row. `group_skeleton`: distinct within a row. `node_far`: distinct nodes of the same group as the listing node, never itself. `group_far`: distinct groups, never the listing group itself.
All inputs are finite; a program needn't handle non-finite values.
Results may differ from the reference program's by a relative error of at most 0.0095.
Values may be sent and summed in bfloat16 or wider, within the bound.
No kernel may reach another device: no remote copies, remote signals or barrier semaphores. Data moves between devices by JAX's collectives and lax.ppermute only.
A program may use at most 192 MiB of HBM per device.

```python
import jax
import jax.numpy as jnp
from jax import lax

LEAF = 256
DIM = 128
RHS = 256
RANK = 128
NODE_RANK = 128
GROUP_RANK = 128
NEAR = 5
FAR = 4
REACH = 8
NODE_FAR = 4
GROUP_FAR = 2
LEAF_DEV = 24
NODES = 32
GROUPS = 4
GROUP_NODES = 8
LEAVES = 768
POINTS = 196608
N_COL = 8


def shared_lists(key):
    subkey = jax.random.fold_in(key, 11)
    offsets = jnp.arange(2 * REACH + 1, dtype=jnp.int32) - REACH
    targets = jnp.arange(LEAVES, dtype=jnp.int32)[:, None] + offsets[None, :]
    inside = (targets >= 0) & (targets < LEAVES)
    random_part = jax.random.randint(subkey, (LEAVES, 2 * REACH + 1), 0, 1 << 20)
    scores = random_part * 64 + (offsets + REACH)[None, :]
    scores = jnp.where(offsets[None, :] == 0, 1 << 28, scores)
    scores = jnp.where(inside, scores, -1 - (offsets + REACH)[None, :])
    top_values, ranking = lax.top_k(scores, NEAR + FAR)
    return jnp.take_along_axis(targets, ranking.astype(jnp.int32), axis=1)


def distinct_choice(key, row_total, candidates, picks):
    scores = jax.random.randint(key, (row_total, candidates), 0, (1 << 30) // candidates) * candidates
    scores = scores + jnp.arange(candidates, dtype=jnp.int32)[None, :]
    top_values, ranking = lax.top_k(scores, picks)
    return ranking.astype(jnp.int32)


def draw_near_list(key, part):
    return shared_lists(key)[:, :NEAR]


def draw_far_list(key, part):
    return shared_lists(key)[:, NEAR:]


def draw_leaf_skeleton(key, part):
    return distinct_choice(jax.random.fold_in(key, 21), LEAVES, LEAF, RANK)


def draw_node_skeleton(key, part):
    return distinct_choice(jax.random.fold_in(key, 22), NODES, LEAF_DEV * RANK, NODE_RANK)


def draw_group_skeleton(key, part):
    return distinct_choice(jax.random.fold_in(key, 23), GROUPS, GROUP_NODES * NODE_RANK, GROUP_RANK)


def draw_node_far(key, part):
    subkey = jax.random.fold_in(key, 31)
    scores = jax.random.randint(subkey, (NODES, GROUP_NODES), 0, (1 << 30) // GROUP_NODES) * GROUP_NODES
    scores = scores + jnp.arange(GROUP_NODES, dtype=jnp.int32)[None, :]
    own_column = jnp.arange(NODES, dtype=jnp.int32) % GROUP_NODES
    scores = jnp.where(jnp.arange(GROUP_NODES, dtype=jnp.int32)[None, :] == own_column[:, None], -1, scores)
    top_values, ranking = lax.top_k(scores, NODE_FAR)
    group_start = jnp.arange(NODES, dtype=jnp.int32) // GROUP_NODES * GROUP_NODES
    return (group_start[:, None] + ranking).astype(jnp.int32)


def draw_group_far(key, part):
    subkey = jax.random.fold_in(key, 32)
    scores = jax.random.randint(subkey, (GROUPS, GROUPS), 0, (1 << 30) // GROUPS) * GROUPS
    scores = scores + jnp.arange(GROUPS, dtype=jnp.int32)[None, :]
    scores = jnp.where(jnp.eye(GROUPS, dtype=jnp.bool_), -1, scores)
    top_values, ranking = lax.top_k(scores, GROUP_FAR)
    return ranking.astype(jnp.int32)


def with_ends(entries, stream_key, smallest, high):
    place = [jax.random.randint(jax.random.fold_in(stream_key, axis), (), 0, length) for axis, length in enumerate(entries.shape)]
    main_axis = entries.shape.index(max(entries.shape))
    next_to = place[:main_axis] + [(place[main_axis] + 1) % entries.shape[main_axis]] + place[main_axis + 1:]
    return entries.at[tuple(place)].set(smallest).at[tuple(next_to)].set(high)


def shard_levels(key, dims, cuts, least, top_value):
    def one(axis_at, blocks):
        heights = jax.random.uniform(jax.random.fold_in(jax.random.fold_in(key, 6), axis_at), (blocks,), jnp.float32, least / len(cuts), top_value / len(cuts))
        return jnp.repeat(jnp.exp(heights), dims[axis_at] // blocks).reshape((-1,) + (1,) * (len(dims) - axis_at - 1))

    gain = one(*cuts[0])
    for cut in cuts[1:]:
        gain = gain * one(*cut)
    return gain


def normal_values(key, extent, scale, limit, cuts=(), held_as=jnp.bfloat16):
    entries = jax.random.normal(key, extent, jnp.float32) * scale
    if len(cuts) > 0:
        entries = shard_levels(key, extent, cuts, -0.22, 0.18) * entries
    return jnp.clip(entries, min=-limit, max=limit).astype(held_as)


def setup_inputs(seed: int = 0) -> dict:
    key_of = jax.random.split(jax.random.key(seed), 16)
    return {
        "points": normal_values(key_of[0], (POINTS, DIM), 1.0, 6.0, ((0, 32),)),
        "weights": normal_values(key_of[1], (POINTS, RHS), 1.0, 6.0, ((0, 32),)),
        "leaf_basis": normal_values(key_of[2], (POINTS, RANK), (RANK // 2) ** -0.5, 0.75, ((0, 32),)),
        "leaf_rank": with_ends(jax.random.randint(key_of[3], (LEAVES,), RANK // 2, RANK + 1), jax.random.fold_in(key_of[3], 1), RANK // 2, RANK).astype(jnp.int32),
        "leaf_skeleton": draw_leaf_skeleton(jax.random.fold_in(key_of[15], 71), 0),
        "near_list": draw_near_list(jax.random.fold_in(key_of[15], 71), 0),
        "far_list": draw_far_list(jax.random.fold_in(key_of[15], 71), 0),
        "node_basis": normal_values(key_of[7], (LEAVES * RANK, NODE_RANK), (LEAF_DEV * RANK // 2) ** -0.5, 0.15625, ((0, 32),)),
        "node_rank": with_ends(jax.random.randint(key_of[8], (NODES,), NODE_RANK // 2, NODE_RANK + 1), jax.random.fold_in(key_of[8], 1), NODE_RANK // 2, NODE_RANK).astype(jnp.int32),
        "node_skeleton": draw_node_skeleton(jax.random.fold_in(key_of[15], 71), 0),
        "node_far": draw_node_far(jax.random.fold_in(key_of[15], 71), 0),
        "group_basis": normal_values(key_of[11], (NODES * NODE_RANK, GROUP_RANK), (N_COL * NODE_RANK // 4) ** -0.5, 0.375, ((0, 32),)),
        "group_rank": with_ends(jax.random.randint(key_of[12], (GROUPS,), GROUP_RANK // 4, GROUP_RANK + 1), jax.random.fold_in(key_of[12], 1), GROUP_RANK // 4, GROUP_RANK).astype(jnp.int32),
        "group_skeleton": draw_group_skeleton(jax.random.fold_in(key_of[15], 71), 0),
        "group_far": draw_group_far(jax.random.fold_in(key_of[15], 71), 0),
    }


def kernel_block(left, right):
    left_wide = left.astype(jnp.float32)
    right_wide = right.astype(jnp.float32)
    left_square = jnp.sum(left_wide * left_wide, axis=-1)
    right_square = jnp.sum(right_wide * right_wide, axis=-1)
    inner = jnp.einsum("...md,...nd->...mn", left_wide, right_wide)
    distance = left_square[..., :, None] + right_square[..., None, :] - 2.0 * inner
    return jnp.exp(distance * (-2.0 / left.shape[-1])).astype(jnp.bfloat16)


def rank_mask(ranks, width):
    return (jnp.arange(width, dtype=jnp.int32)[None, :] < ranks[:, None]).astype(jnp.float32)


def reference(points, weights, leaf_basis, leaf_rank, leaf_skeleton, near_list, far_list, node_basis, node_rank, node_skeleton, node_far, group_basis, group_rank, group_skeleton, group_far):
    leaf_points = points.reshape(LEAVES, LEAF, DIM)
    leaf_weights = weights.reshape(LEAVES, LEAF, RHS)
    leaf_bases = leaf_basis.reshape(LEAVES, LEAF, RANK)
    leaf_mask = rank_mask(leaf_rank, RANK)
    node_mask = rank_mask(node_rank, NODE_RANK)
    group_mask = rank_mask(group_rank, GROUP_RANK)

    def upward(blocks):
        bases, values, masks = blocks
        product = jnp.einsum("lpk,lpr->lkr", bases.astype(jnp.float32), values.astype(jnp.float32))
        return (product * masks[:, :, None]).astype(jnp.bfloat16)

    leaf_up = lax.map(upward, (leaf_bases.reshape(NODES, LEAF_DEV, LEAF, RANK), leaf_weights.reshape(NODES, LEAF_DEV, LEAF, RHS), leaf_mask.reshape(NODES, LEAF_DEV, RANK)))
    leaf_up = leaf_up.reshape(LEAVES, RANK, RHS)
    leaf_coords = jnp.take_along_axis(leaf_points, leaf_skeleton[:, :, None].astype(jnp.int32), axis=1)

    node_bases = node_basis.reshape(NODES, LEAF_DEV * RANK, NODE_RANK)
    stacked_up = leaf_up.reshape(NODES, LEAF_DEV * RANK, RHS)
    node_up = (jnp.einsum("nak,nar->nkr", node_bases.astype(jnp.float32), stacked_up.astype(jnp.float32)) * node_mask[:, :, None]).astype(jnp.bfloat16)
    node_coords = jnp.take_along_axis(leaf_coords.reshape(NODES, LEAF_DEV * RANK, DIM), node_skeleton[:, :, None].astype(jnp.int32), axis=1)

    group_bases = group_basis.reshape(GROUPS, GROUP_NODES * NODE_RANK, GROUP_RANK)
    group_stack = node_up.reshape(GROUPS, GROUP_NODES * NODE_RANK, RHS)
    group_up = (jnp.einsum("gak,gar->gkr", group_bases.astype(jnp.float32), group_stack.astype(jnp.float32)) * group_mask[:, :, None]).astype(jnp.bfloat16)
    group_coords = jnp.take_along_axis(node_coords.reshape(GROUPS, GROUP_NODES * NODE_RANK, DIM), group_skeleton[:, :, None].astype(jnp.int32), axis=1)

    group_sources = group_coords[group_far]
    group_targets = jnp.broadcast_to(group_coords[:, None], group_sources.shape)
    group_kernel = kernel_block(group_targets, group_sources)
    group_down = (jnp.einsum("gfab,gfbr->gar", group_kernel.astype(jnp.float32), group_up[group_far].astype(jnp.float32)) * group_mask[:, :, None]).astype(jnp.bfloat16)

    node_parts = group_basis.reshape(NODES, NODE_RANK, GROUP_RANK)
    parent_down = group_down[jnp.arange(NODES, dtype=jnp.int32) // GROUP_NODES]
    node_sources = node_coords[node_far]
    node_targets = jnp.broadcast_to(node_coords[:, None], node_sources.shape)
    node_kernel = kernel_block(node_targets, node_sources)
    node_total = jnp.einsum("nkg,ngr->nkr", node_parts.astype(jnp.float32), parent_down.astype(jnp.float32))
    node_total = node_total + jnp.einsum("nfab,nfbr->nar", node_kernel.astype(jnp.float32), node_up[node_far].astype(jnp.float32))
    node_down = (node_total * node_mask[:, :, None]).astype(jnp.bfloat16)

    def downward(blocks):
        bases_node, down_node, far_rows, near_rows, coords_node, mask_node, leaf_base_rows, points_node = blocks
        total = jnp.dot(bases_node.astype(jnp.float32), down_node.astype(jnp.float32)).reshape(LEAF_DEV, RANK, RHS)
        for position in range(FAR):
            source_coords = leaf_coords[far_rows[:, position]]
            kernel = kernel_block(coords_node, source_coords)
            total = total + jnp.einsum("lab,lbr->lar", kernel.astype(jnp.float32), leaf_up[far_rows[:, position]].astype(jnp.float32))
        down_leaf = (total * mask_node[:, :, None]).astype(jnp.bfloat16)
        result = jnp.einsum("lpk,lkr->lpr", leaf_base_rows.astype(jnp.float32), down_leaf.astype(jnp.float32))
        for position in range(NEAR):
            kernel = kernel_block(points_node, leaf_points[near_rows[:, position]])
            result = result + jnp.einsum("lpq,lqr->lpr", kernel.astype(jnp.float32), leaf_weights[near_rows[:, position]].astype(jnp.float32))
        return result.astype(jnp.bfloat16)

    outputs = lax.map(downward, (node_bases, node_down, far_list.reshape(NODES, LEAF_DEV, FAR), near_list.reshape(NODES, LEAF_DEV, NEAR), leaf_coords.reshape(NODES, LEAF_DEV, RANK, DIM), leaf_mask.reshape(NODES, LEAF_DEV, RANK), leaf_bases.reshape(NODES, LEAF_DEV, LEAF, RANK), leaf_points.reshape(NODES, LEAF_DEV, LEAF, DIM)))
    return outputs.reshape(POINTS, RHS)
```

```python
import functools

import jax
import jax.numpy as jnp
from jax import lax
from jax.experimental import pallas as pl
from jax.experimental.pallas import tpu as pltpu
from jax.sharding import PartitionSpec as P

REACH = 8


def padded(cells, sides, width):
    for axis, dim in sides:
        count = lax.axis_size(axis)
        ends = count - 1
        head = lax.slice_in_dim(cells, 0, width, axis=dim)
        tail = lax.slice_in_dim(cells, cells.shape[dim] - width, cells.shape[dim], axis=dim)
        cells = jnp.concatenate(
            [
                lax.ppermute(tail, axis, [(i, (i + 1) % count) for i in range(ends)]),
                cells,
                lax.ppermute(head, axis, [((i + 1) % count, i) for i in range(ends)]),
            ],
            axis=dim,
        )
    return cells


def kernel_block(left, right):
    left_square = jnp.sum(jnp.square(left.astype(jnp.float32)), axis=-1)
    right_square = jnp.sum(jnp.square(right.astype(jnp.float32)), axis=-1)
    inner = jnp.einsum("...md,...nd->...mn", left, right, preferred_element_type=jnp.float32)
    distance = left_square[..., :, None] + right_square[..., None, :] - 2.0 * inner
    return jnp.exp(distance * (-2.0 / left.shape[-1])).astype(jnp.bfloat16)


def near_kernel(index_ref, target_ref, *refs):
    count = (len(refs) - 1) // 3
    point_refs = refs[:count]
    weight_refs = refs[count : 2 * count]
    norm_refs = refs[2 * count : 3 * count]
    out_ref = refs[-1]
    target = target_ref[0]
    target_wide = target.astype(jnp.float32)
    target_square = jnp.sum(target_wide * target_wide, axis=-1, keepdims=True)
    scale = -2.0 / target.shape[-1]
    total = None
    for position in range(count):
        inner = lax.dot_general(
            target,
            point_refs[position][0],
            (((1,), (1,)), ((), ())),
            preferred_element_type=jnp.float32,
        )
        distance = target_square + norm_refs[position][0] - 2.0 * inner
        kernel = jnp.exp(distance * scale).astype(jnp.bfloat16)
        part = jnp.dot(kernel, weight_refs[position][0], preferred_element_type=jnp.float32)
        total = part if total is None else total + part
    out_ref[0] = total


def near_field(local_points, ext_points, ext_weights, ext_norms, near_local):
    leaves, size, dims = local_points.shape
    rhs = ext_weights.shape[-1]
    count = near_local.shape[1]
    flat_index = near_local.reshape(-1)

    def source_map(position):
        return lambda l, index: (index[l * count + position], 0, 0)

    in_specs = [pl.BlockSpec((1, size, dims), lambda l, index: (l, 0, 0))]
    in_specs += [pl.BlockSpec((1, size, dims), source_map(p)) for p in range(count)]
    in_specs += [pl.BlockSpec((1, size, rhs), source_map(p)) for p in range(count)]
    in_specs += [pl.BlockSpec((1, 1, size), source_map(p)) for p in range(count)]
    return pl.pallas_call(
        near_kernel,
        grid_spec=pltpu.PrefetchScalarGridSpec(
            num_scalar_prefetch=1,
            grid=(leaves,),
            in_specs=in_specs,
            out_specs=pl.BlockSpec((1, size, rhs), lambda l, index: (l, 0, 0)),
        ),
        out_shape=jax.ShapeDtypeStruct((leaves, size, rhs), jnp.float32),
    )(flat_index, local_points, *([ext_points] * count), *([ext_weights] * count), *([ext_norms] * count))


def select_rows(table, index):
    count = table.shape[0]
    onehot = (index[:, None] == jnp.arange(count, dtype=jnp.int32)[None, :]).astype(table.dtype)
    picked = jnp.dot(onehot, table.reshape(count, -1), preferred_element_type=jnp.float32).astype(
        table.dtype
    )
    return picked.reshape(index.shape + table.shape[1:])


def select_within(table, index):
    count = table.shape[1]
    onehot = (index[:, :, None] == jnp.arange(count, dtype=jnp.int32)[None, None, :]).astype(
        table.dtype
    )
    return jnp.einsum("bkp,bpc->bkc", onehot, table, preferred_element_type=jnp.float32).astype(
        table.dtype
    )


def body(
    points,
    weights,
    leaf_basis,
    leaf_rank,
    leaf_skeleton,
    near_list,
    far_list,
    node_basis,
    node_rank,
    node_skeleton,
    node_far,
    group_basis,
    group_rank,
    group_skeleton,
    group_far,
):
    leaf_count = leaf_rank.shape[0]
    leaf_size = points.shape[0] // leaf_count
    dim_count = points.shape[1]
    rhs_count = weights.shape[1]
    rank_count = leaf_basis.shape[1]
    node_width = node_basis.shape[1]
    group_width = group_basis.shape[1]
    local_points = points.reshape(leaf_count, leaf_size, dim_count)
    local_bases = leaf_basis.reshape(leaf_count, leaf_size, rank_count)
    local_weights = weights.reshape(leaf_count, leaf_size, rhs_count)
    leaf_mask = (
        lax.broadcasted_iota(jnp.int32, (leaf_count, rank_count), 1) < leaf_rank[:, None]
    ).astype(jnp.float32)
    leaf_up = (
        jnp.einsum("lpk,lpr->lkr", local_bases, local_weights, preferred_element_type=jnp.float32)
        * leaf_mask[:, :, None]
    ).astype(jnp.bfloat16)
    leaf_coords = select_within(local_points, leaf_skeleton)
    first_leaf = lax.axis_index(("row", "col")) * leaf_count
    offset = first_leaf - REACH
    ext_points = padded(points, ((("row", "col"), 0),), REACH * leaf_size).reshape(
        leaf_count + 2 * REACH, leaf_size, dim_count
    )
    ext_weights = padded(weights, ((("row", "col"), 0),), REACH * leaf_size).reshape(
        leaf_count + 2 * REACH, leaf_size, rhs_count
    )
    ext_wide = ext_points.astype(jnp.float32)
    ext_norms = jnp.sum(ext_wide * ext_wide, axis=-1)[:, None, :]
    own_rows = jnp.concatenate([leaf_coords, leaf_up], axis=-1).reshape(
        leaf_count * rank_count, dim_count + rhs_count
    )
    skeleton_rows = padded(own_rows, ((("row", "col"), 0),), REACH * rank_count)
    skeleton_rows = skeleton_rows.reshape(leaf_count + 2 * REACH, rank_count, dim_count + rhs_count)
    near_local = near_list - offset
    near_total = near_field(local_points, ext_points, ext_weights, ext_norms, near_local)
    node_mask = (jnp.arange(node_width, dtype=jnp.int32) < node_rank[0]).astype(jnp.float32)
    node_up = (
        jnp.einsum(
            "ak,ar->kr",
            node_basis,
            leaf_up.reshape(leaf_count * rank_count, rhs_count),
            preferred_element_type=jnp.float32,
        )
        * node_mask[:, None]
    ).astype(jnp.bfloat16)
    node_coords = select_rows(
        leaf_coords.reshape(leaf_count * rank_count, dim_count), node_skeleton[0]
    )
    column = lax.axis_index("col")
    columns = lax.axis_size("col")
    source_columns = node_far[0] % columns
    all_coords, all_up = (
        lax.all_gather(node_coords[None], "col", axis=0, tiled=True),
        lax.all_gather(node_up[None], "col", axis=0, tiled=True),
    )
    picked_coords = select_rows(all_coords, source_columns)
    picked_up = select_rows(all_up, source_columns)
    kernel = kernel_block(jnp.broadcast_to(node_coords, picked_coords.shape), picked_coords)
    node_side = jnp.einsum("fab,fbr->ar", kernel, picked_up, preferred_element_type=jnp.float32)
    group_mask = (jnp.arange(group_width, dtype=jnp.int32) < group_rank[0]).astype(jnp.float32)
    group_part = (
        jnp.einsum("ag,ar->gr", group_basis, node_up, preferred_element_type=jnp.float32)
        * group_mask[:, None]
    )
    selector = (
        group_skeleton[0][:, None]
        == column * node_width + jnp.arange(node_width, dtype=jnp.int32)[None, :]
    ).astype(jnp.bfloat16)
    coord_part = jnp.dot(selector, node_coords, preferred_element_type=jnp.float32)
    group_sum, coord_sum = lax.psum((group_part, coord_part), "col")
    group_up = group_sum.astype(jnp.bfloat16)
    group_coords = coord_sum.astype(jnp.bfloat16)
    every_group_coords, every_group_up = (
        lax.all_gather(group_coords[None], "row", axis=0, tiled=True),
        lax.all_gather(group_up[None], "row", axis=0, tiled=True),
    )
    picked_group_coords = select_rows(every_group_coords, group_far[0])
    picked_group_up = select_rows(every_group_up, group_far[0])
    group_kernel = kernel_block(
        jnp.broadcast_to(group_coords, picked_group_coords.shape), picked_group_coords
    )
    group_down = (
        jnp.einsum("fab,fbr->ar", group_kernel, picked_group_up, preferred_element_type=jnp.float32)
        * group_mask[:, None]
    ).astype(jnp.bfloat16)
    node_down = (
        (jnp.dot(group_basis, group_down, preferred_element_type=jnp.float32) + node_side)
        * node_mask[:, None]
    ).astype(jnp.bfloat16)
    far_total = jnp.dot(node_basis, node_down, preferred_element_type=jnp.float32).reshape(
        leaf_count, rank_count, rhs_count
    )
    far_local = far_list - offset
    for position in range(far_list.shape[1]):
        sources = select_rows(skeleton_rows, far_local[:, position])
        kernel = kernel_block(leaf_coords, sources[..., :dim_count])
        far_total = far_total + jnp.einsum(
            "lab,lbr->lar", kernel, sources[..., dim_count:], preferred_element_type=jnp.float32
        )
    leaf_down = (far_total * leaf_mask[:, :, None]).astype(jnp.bfloat16)
    result = (
        jnp.einsum("lpk,lkr->lpr", local_bases, leaf_down, preferred_element_type=jnp.float32)
        + near_total
    )
    return result.astype(jnp.bfloat16).reshape(leaf_count * leaf_size, rhs_count)


def solution(mesh):
    in_specs = (
        P(("row", "col"), None),
        P(("row", "col"), None),
        P(("row", "col"), None),
        P(("row", "col")),
        P(("row", "col"), None),
        P(("row", "col"), None),
        P(("row", "col"), None),
        P(("row", "col"), None),
        P(("row", "col")),
        P(("row", "col"), None),
        P(("row", "col"), None),
        P(("row", "col"), None),
        P("row"),
        P("row", None),
        P("row", None),
    )
    out_specs = P(("row", "col"), None)
    return jax.shard_map(body, mesh=mesh, in_specs=in_specs, out_specs=out_specs, check_vma=False)
```

```python
import functools

import jax
import jax.numpy as jnp
from jax import lax
from jax.experimental import pallas as pl
from jax.experimental.pallas import tpu as pltpu
from jax.sharding import PartitionSpec as P

REACH = 8


def padded(cells, sides, width):
    for axis, dim in sides:
        count = lax.axis_size(axis)
        ends = count - 1
        head = lax.slice_in_dim(cells, 0, width, axis=dim)
        tail = lax.slice_in_dim(cells, cells.shape[dim] - width, cells.shape[dim], axis=dim)
        cells = jnp.concatenate(
            [
                lax.ppermute(tail, axis, [(i, (i + 1) % count) for i in range(ends)]),
                cells,
                lax.ppermute(head, axis, [((i + 1) % count, i) for i in range(ends)]),
            ],
            axis=dim,
        )
    return cells


def kernel_block(left, right):
    left_square = jnp.sum(jnp.square(left.astype(jnp.float32)), axis=-1)
    right_square = jnp.sum(jnp.square(right.astype(jnp.float32)), axis=-1)
    inner = jnp.einsum("...md,...nd->...mn", left, right, preferred_element_type=jnp.float32)
    distance = left_square[..., :, None] + right_square[..., None, :] - 2.0 * inner
    return jnp.exp(distance * (-2.0 / left.shape[-1])).astype(jnp.bfloat16)


def near_kernel(index_ref, target_ref, *refs):
    count = (len(refs) - 1) // 3
    point_refs = refs[:count]
    weight_refs = refs[count : 2 * count]
    norm_refs = refs[2 * count : 3 * count]
    out_ref = refs[-1]
    target = target_ref[0]
    target_wide = target.astype(jnp.float32)
    target_square = jnp.sum(target_wide * target_wide, axis=-1, keepdims=True)
    scale = -2.0 / target.shape[-1]
    total = None
    for position in range(count):
        inner = lax.dot_general(
            target,
            point_refs[position][0],
            (((1,), (1,)), ((), ())),
            preferred_element_type=jnp.float32,
        )
        distance = target_square + norm_refs[position][0] - 2.0 * inner
        kernel = jnp.exp(distance * scale).astype(jnp.bfloat16)
        part = jnp.dot(kernel, weight_refs[position][0], preferred_element_type=jnp.float32)
        total = part if total is None else total + part
    out_ref[0] = total


def near_field(local_points, ext_points, ext_weights, ext_norms, near_local):
    leaves, size, dims = local_points.shape
    rhs = ext_weights.shape[-1]
    count = near_local.shape[1]
    flat_index = near_local.reshape(-1)

    def source_map(position):
        return lambda l, index: (index[l * count + position], 0, 0)

    in_specs = [pl.BlockSpec((1, size, dims), lambda l, index: (l, 0, 0))]
    in_specs += [pl.BlockSpec((1, size, dims), source_map(p)) for p in range(count)]
    in_specs += [pl.BlockSpec((1, size, rhs), source_map(p)) for p in range(count)]
    in_specs += [pl.BlockSpec((1, 1, size), source_map(p)) for p in range(count)]
    return pl.pallas_call(
        near_kernel,
        grid_spec=pltpu.PrefetchScalarGridSpec(
            num_scalar_prefetch=1,
            grid=(leaves,),
            in_specs=in_specs,
            out_specs=pl.BlockSpec((1, size, rhs), lambda l, index: (l, 0, 0)),
        ),
        out_shape=jax.ShapeDtypeStruct((leaves, size, rhs), jnp.float32),
    )(flat_index, local_points, *([ext_points] * count), *([ext_weights] * count), *([ext_norms] * count))


def far_kernel(index_ref, rank_ref, target_ref, basis_ref, down_ref, leaf_base_ref, near_ref, *refs):
    count = (len(refs) - 1) // 2
    source_refs = refs[:count]
    norm_refs = refs[count : 2 * count]
    out_ref = refs[-1]
    leaf = pl.program_id(0)
    target = target_ref[0]
    dims = target.shape[-1]
    target_wide = target.astype(jnp.float32)
    target_square = jnp.sum(target_wide * target_wide, axis=-1, keepdims=True)
    scale = -2.0 / dims
    total = jnp.dot(basis_ref[0], down_ref[...], preferred_element_type=jnp.float32)
    for position in range(count):
        source = source_refs[position][0]
        inner = lax.dot_general(
            target, source[:, :dims], (((1,), (1,)), ((), ())), preferred_element_type=jnp.float32
        )
        distance = target_square + norm_refs[position][0] - 2.0 * inner
        kernel = jnp.exp(distance * scale).astype(jnp.bfloat16)
        total = total + jnp.dot(kernel, source[:, dims:], preferred_element_type=jnp.float32)
    rows = lax.broadcasted_iota(jnp.int32, total.shape, 0)
    leaf_down = jnp.where(rows < rank_ref[leaf], total, 0.0).astype(jnp.bfloat16)
    result = jnp.dot(leaf_base_ref[0], leaf_down, preferred_element_type=jnp.float32) + near_ref[0]
    out_ref[0] = result.astype(out_ref.dtype)


def far_field(leaf_coords, skeleton_rows, skeleton_norms, far_local, leaf_rank, bases, node_down, leaf_bases, near_total):
    leaves, rank, dims = leaf_coords.shape
    width = skeleton_rows.shape[-1]
    size = leaf_bases.shape[1]
    rhs = near_total.shape[-1]
    count = far_local.shape[1]
    flat_index = far_local.reshape(-1)

    def source_map(position):
        return lambda l, index, ranks: (index[l * count + position], 0, 0)

    def own(l, index, ranks):
        return (l, 0, 0)

    in_specs = [
        pl.BlockSpec((1, rank, dims), own),
        pl.BlockSpec((1, rank, bases.shape[-1]), own),
        pl.BlockSpec(node_down.shape, lambda l, index, ranks: (0, 0)),
        pl.BlockSpec((1, size, rank), own),
        pl.BlockSpec((1, size, rhs), own),
    ]
    in_specs += [pl.BlockSpec((1, rank, width), source_map(p)) for p in range(count)]
    in_specs += [pl.BlockSpec((1, 1, rank), source_map(p)) for p in range(count)]
    return pl.pallas_call(
        far_kernel,
        grid_spec=pltpu.PrefetchScalarGridSpec(
            num_scalar_prefetch=2,
            grid=(leaves,),
            in_specs=in_specs,
            out_specs=pl.BlockSpec((1, size, rhs), own),
        ),
        out_shape=jax.ShapeDtypeStruct((leaves, size, rhs), jnp.bfloat16),
    )(
        flat_index,
        leaf_rank,
        leaf_coords,
        bases,
        node_down,
        leaf_bases,
        near_total,
        *([skeleton_rows] * count),
        *([skeleton_norms] * count),
    )


def select_rows(table, index):
    count = table.shape[0]
    onehot = (index[:, None] == jnp.arange(count, dtype=jnp.int32)[None, :]).astype(table.dtype)
    picked = jnp.dot(onehot, table.reshape(count, -1), preferred_element_type=jnp.float32).astype(
        table.dtype
    )
    return picked.reshape(index.shape + table.shape[1:])


def select_within(table, index):
    count = table.shape[1]
    onehot = (index[:, :, None] == jnp.arange(count, dtype=jnp.int32)[None, None, :]).astype(
        table.dtype
    )
    return jnp.einsum("bkp,bpc->bkc", onehot, table, preferred_element_type=jnp.float32).astype(
        table.dtype
    )


def body(
    points,
    weights,
    leaf_basis,
    leaf_rank,
    leaf_skeleton,
    near_list,
    far_list,
    node_basis,
    node_rank,
    node_skeleton,
    node_far,
    group_basis,
    group_rank,
    group_skeleton,
    group_far,
):
    leaf_count = leaf_rank.shape[0]
    leaf_size = points.shape[0] // leaf_count
    dim_count = points.shape[1]
    rhs_count = weights.shape[1]
    rank_count = leaf_basis.shape[1]
    node_width = node_basis.shape[1]
    group_width = group_basis.shape[1]
    local_points = points.reshape(leaf_count, leaf_size, dim_count)
    local_bases = leaf_basis.reshape(leaf_count, leaf_size, rank_count)
    local_weights = weights.reshape(leaf_count, leaf_size, rhs_count)
    leaf_mask = (
        lax.broadcasted_iota(jnp.int32, (leaf_count, rank_count), 1) < leaf_rank[:, None]
    ).astype(jnp.float32)
    leaf_up = (
        jnp.einsum("lpk,lpr->lkr", local_bases, local_weights, preferred_element_type=jnp.float32)
        * leaf_mask[:, :, None]
    ).astype(jnp.bfloat16)
    leaf_coords = select_within(local_points, leaf_skeleton)
    first_leaf = lax.axis_index(("row", "col")) * leaf_count
    offset = first_leaf - REACH
    ext_points = padded(points, ((("row", "col"), 0),), REACH * leaf_size).reshape(
        leaf_count + 2 * REACH, leaf_size, dim_count
    )
    ext_weights = padded(weights, ((("row", "col"), 0),), REACH * leaf_size).reshape(
        leaf_count + 2 * REACH, leaf_size, rhs_count
    )
    ext_wide = ext_points.astype(jnp.float32)
    ext_norms = jnp.sum(ext_wide * ext_wide, axis=-1)[:, None, :]
    own_rows = jnp.concatenate([leaf_coords, leaf_up], axis=-1).reshape(
        leaf_count * rank_count, dim_count + rhs_count
    )
    skeleton_rows = padded(own_rows, ((("row", "col"), 0),), REACH * rank_count)
    skeleton_rows = skeleton_rows.reshape(leaf_count + 2 * REACH, rank_count, dim_count + rhs_count)
    near_local = near_list - offset
    near_total = near_field(local_points, ext_points, ext_weights, ext_norms, near_local)
    node_mask = (jnp.arange(node_width, dtype=jnp.int32) < node_rank[0]).astype(jnp.float32)
    node_up = (
        jnp.einsum(
            "ak,ar->kr",
            node_basis,
            leaf_up.reshape(leaf_count * rank_count, rhs_count),
            preferred_element_type=jnp.float32,
        )
        * node_mask[:, None]
    ).astype(jnp.bfloat16)
    node_coords = select_rows(
        leaf_coords.reshape(leaf_count * rank_count, dim_count), node_skeleton[0]
    )
    columns = lax.axis_size("col")
    source_columns = node_far[0] % columns
    node_pack = jnp.concatenate([node_coords, node_up, group_basis], axis=1)
    gathered = lax.all_gather(node_pack[None], "col", axis=0, tiled=True)
    all_coords = gathered[:, :, :dim_count]
    all_up = gathered[:, :, dim_count : dim_count + rhs_count]
    all_parts = gathered[:, :, dim_count + rhs_count :]
    picked_coords = select_rows(all_coords, source_columns)
    picked_up = select_rows(all_up, source_columns)
    kernel = kernel_block(jnp.broadcast_to(node_coords, picked_coords.shape), picked_coords)
    node_side = jnp.einsum("fab,fbr->ar", kernel, picked_up, preferred_element_type=jnp.float32)
    group_mask = (jnp.arange(group_width, dtype=jnp.int32) < group_rank[0]).astype(jnp.float32)
    group_up = (
        jnp.einsum("nag,nar->gr", all_parts, all_up, preferred_element_type=jnp.float32)
        * group_mask[:, None]
    ).astype(jnp.bfloat16)
    group_coords = select_rows(all_coords.reshape(columns * node_width, dim_count), group_skeleton[0])
    group_pack = jnp.concatenate([group_coords, group_up], axis=1)
    every_group = lax.all_gather(group_pack[None], "row", axis=0, tiled=True)
    picked_group = select_rows(every_group, group_far[0])
    picked_group_coords = picked_group[:, :, :dim_count]
    picked_group_up = picked_group[:, :, dim_count:]
    group_kernel = kernel_block(
        jnp.broadcast_to(group_coords, picked_group_coords.shape), picked_group_coords
    )
    group_down = (
        jnp.einsum("fab,fbr->ar", group_kernel, picked_group_up, preferred_element_type=jnp.float32)
        * group_mask[:, None]
    ).astype(jnp.bfloat16)
    node_down = (
        (jnp.dot(group_basis, group_down, preferred_element_type=jnp.float32) + node_side)
        * node_mask[:, None]
    ).astype(jnp.bfloat16)
    skeleton_wide = skeleton_rows[:, :, :dim_count].astype(jnp.float32)
    skeleton_norms = jnp.sum(skeleton_wide * skeleton_wide, axis=-1)[:, None, :]
    far_local = far_list - offset
    result = far_field(
        leaf_coords,
        skeleton_rows,
        skeleton_norms,
        far_local,
        leaf_rank,
        node_basis.reshape(leaf_count, rank_count, node_width),
        node_down,
        local_bases,
        near_total,
    )
    return result.reshape(leaf_count * leaf_size, rhs_count)


def solution(mesh):
    in_specs = (
        P(("row", "col"), None),
        P(("row", "col"), None),
        P(("row", "col"), None),
        P(("row", "col")),
        P(("row", "col"), None),
        P(("row", "col"), None),
        P(("row", "col"), None),
        P(("row", "col"), None),
        P(("row", "col")),
        P(("row", "col"), None),
        P(("row", "col"), None),
        P(("row", "col"), None),
        P("row"),
        P("row", None),
        P("row", None),
    )
    out_specs = P(("row", "col"), None)
    return jax.shard_map(body, mesh=mesh, in_specs=in_specs, out_specs=out_specs, check_vma=False)
```

```python
import jax
import jax.numpy as jnp
from jax import lax
from jax.experimental import pallas as pl
from jax.experimental.pallas import tpu as pltpu
from jax.sharding import PartitionSpec as P

REACH = 8
FLAT = ("row", "col")


def halos(cells, width):
    count = lax.axis_size(FLAT)
    ends = count - 1
    head = cells[:width]
    tail = cells[cells.shape[0] - width :]
    left = lax.ppermute(tail, FLAT, [(i, i + 1) for i in range(ends)])
    right = lax.ppermute(head, FLAT, [(i + 1, i) for i in range(ends)])
    return left, right


def kernel_block(left, right):
    left_square = jnp.sum(jnp.square(left.astype(jnp.float32)), axis=-1)
    right_square = jnp.sum(jnp.square(right.astype(jnp.float32)), axis=-1)
    inner = jnp.einsum("...md,...nd->...mn", left, right, preferred_element_type=jnp.float32)
    distance = left_square[..., :, None] + right_square[..., None, :] - 2.0 * inner
    return jnp.exp(distance * (-2.0 / left.shape[-1])).astype(jnp.bfloat16)


def contract_last(a, b):
    return lax.dot_general(a, b, (((1,), (1,)), ((), ())), preferred_element_type=jnp.float32)


def scaled_kernel(target, target_square, source):
    dims = target.shape[-1]
    scale = -2.0 / dims
    wide = source.astype(jnp.float32)
    square = wide * wide
    high = square.astype(jnp.bfloat16)
    low = (square - high.astype(jnp.float32)).astype(jnp.bfloat16)
    ones = jnp.ones((8, dims), jnp.bfloat16)
    source_square = (contract_last(ones, high) + contract_last(ones, low))[0:1] * scale
    inner = contract_last(target * jnp.asarray(-2.0 * scale, target.dtype), source)
    return jnp.exp((target_square + source_square) + inner).astype(jnp.bfloat16)


def target_square_of(target):
    wide = target.astype(jnp.float32)
    return jnp.sum(wide * wide, axis=-1, keepdims=True) * (-2.0 / target.shape[-1])


def fetch_sources(index_ref, row, count, parts, buffers, sems, slot):
    for position in range(count):
        source = index_ref[row * count + position]
        for which, (left, own, right) in enumerate(parts):
            halo = left.shape[0]
            mine = own.shape[0]
            target = buffers[which].at[slot, position]
            sem = sems.at[which, slot, position]

            @pl.when(source < halo)
            def _():
                pltpu.make_async_copy(left.at[source], target, sem).start()

            @pl.when((source >= halo) & (source < halo + mine))
            def _():
                pltpu.make_async_copy(own.at[source - halo], target, sem).start()

            @pl.when(source >= halo + mine)
            def _():
                pltpu.make_async_copy(right.at[source - halo - mine], target, sem).start()


def wait_sources(count, parts, buffers, sems, slot):
    for position in range(count):
        for which, (left, own, right) in enumerate(parts):
            pltpu.make_async_copy(
                own.at[0], buffers[which].at[slot, position], sems.at[which, slot, position]
            ).wait()


def pipelined_sources(index_ref, count, parts, buffers, sems):
    leaf = pl.program_id(0)
    leaves = pl.num_programs(0)
    slot = leaf % 2

    @pl.when(leaf == 0)
    def _():
        fetch_sources(index_ref, 0, count, parts, buffers, sems, 0)

    @pl.when(leaf + 1 < leaves)
    def _():
        fetch_sources(index_ref, leaf + 1, count, parts, buffers, sems, 1 - slot)

    wait_sources(count, parts, buffers, sems, slot)
    return slot


def near_kernel(index_ref, target_ref, lp, op, rp, lw, ow, rw, out_ref, point_buf, weight_buf, sems):
    count = point_buf.shape[1]
    parts = ((lp, op, rp), (lw, ow, rw))
    slot = pipelined_sources(index_ref, count, parts, (point_buf, weight_buf), sems)
    target = target_ref[0]
    target_square = target_square_of(target)
    total = None
    for position in range(count):
        kernel = scaled_kernel(target, target_square, point_buf[slot, position])
        part = jnp.dot(kernel, weight_buf[slot, position], preferred_element_type=jnp.float32)
        total = part if total is None else total + part
    out_ref[0] = total


def near_field(local_points, left_points, right_points, local_weights, left_weights, right_weights, near_local):
    leaves, size, dims = local_points.shape
    rhs = local_weights.shape[-1]
    count = near_local.shape[1]
    anywhere = pl.BlockSpec(memory_space=pl.ANY)
    return pl.pallas_call(
        near_kernel,
        grid_spec=pltpu.PrefetchScalarGridSpec(
            num_scalar_prefetch=1,
            grid=(leaves,),
            in_specs=[pl.BlockSpec((1, size, dims), lambda l, index: (l, 0, 0))] + [anywhere] * 6,
            out_specs=pl.BlockSpec((1, size, rhs), lambda l, index: (l, 0, 0)),
            scratch_shapes=[
                pltpu.VMEM((2, count, size, dims), local_points.dtype),
                pltpu.VMEM((2, count, size, rhs), local_weights.dtype),
                pltpu.SemaphoreType.DMA((2, 2, count)),
            ],
        ),
        out_shape=jax.ShapeDtypeStruct((leaves, size, rhs), jnp.float32),
        compiler_params=pltpu.CompilerParams(dimension_semantics=("arbitrary",)),
    )(
        near_local.reshape(-1),
        local_points,
        left_points,
        local_points,
        right_points,
        left_weights,
        local_weights,
        right_weights,
    )


def far_kernel(index_ref, rank_ref, target_ref, basis_ref, down_ref, leaf_base_ref, near_ref, ls, os, rs, out_ref, source_buf, sems):
    count = source_buf.shape[1]
    slot = pipelined_sources(index_ref, count, ((ls, os, rs),), (source_buf,), sems)
    leaf = pl.program_id(0)
    target = target_ref[0]
    dims = target.shape[-1]
    target_square = target_square_of(target)
    total = jnp.dot(basis_ref[0], down_ref[...], preferred_element_type=jnp.float32)
    for position in range(count):
        source = source_buf[slot, position]
        kernel = scaled_kernel(target, target_square, source[:, :dims])
        total = total + jnp.dot(kernel, source[:, dims:], preferred_element_type=jnp.float32)
    rows = lax.broadcasted_iota(jnp.int32, total.shape, 0)
    leaf_down = jnp.where(rows < rank_ref[leaf], total, 0.0).astype(jnp.bfloat16)
    result = jnp.dot(leaf_base_ref[0], leaf_down, preferred_element_type=jnp.float32) + near_ref[0]
    out_ref[0] = result.astype(out_ref.dtype)


def far_field(leaf_coords, left_rows, own_rows, right_rows, far_local, leaf_rank, bases, node_down, leaf_bases, near_total):
    leaves, rank, dims = leaf_coords.shape
    width = own_rows.shape[-1]
    size = leaf_bases.shape[1]
    rhs = near_total.shape[-1]
    count = far_local.shape[1]

    def own(l, index, ranks):
        return (l, 0, 0)

    anywhere = pl.BlockSpec(memory_space=pl.ANY)
    in_specs = [
        pl.BlockSpec((1, rank, dims), own),
        pl.BlockSpec((1, rank, bases.shape[-1]), own),
        pl.BlockSpec(node_down.shape, lambda l, index, ranks: (0, 0)),
        pl.BlockSpec((1, size, rank), own),
        pl.BlockSpec((1, size, rhs), own),
        anywhere,
        anywhere,
        anywhere,
    ]
    return pl.pallas_call(
        far_kernel,
        grid_spec=pltpu.PrefetchScalarGridSpec(
            num_scalar_prefetch=2,
            grid=(leaves,),
            in_specs=in_specs,
            out_specs=pl.BlockSpec((1, size, rhs), own),
            scratch_shapes=[
                pltpu.VMEM((2, count, rank, width), own_rows.dtype),
                pltpu.SemaphoreType.DMA((1, 2, count)),
            ],
        ),
        out_shape=jax.ShapeDtypeStruct((leaves, size, rhs), jnp.bfloat16),
        compiler_params=pltpu.CompilerParams(dimension_semantics=("arbitrary",)),
    )(
        far_local.reshape(-1),
        leaf_rank,
        leaf_coords,
        bases,
        node_down,
        leaf_bases,
        near_total,
        left_rows,
        own_rows,
        right_rows,
    )


def select_rows(table, index):
    count = table.shape[0]
    onehot = (index[:, None] == jnp.arange(count, dtype=jnp.int32)[None, :]).astype(table.dtype)
    picked = jnp.dot(onehot, table.reshape(count, -1), preferred_element_type=jnp.float32).astype(
        table.dtype
    )
    return picked.reshape(index.shape + table.shape[1:])


def select_within(table, index):
    count = table.shape[1]
    onehot = (index[:, :, None] == jnp.arange(count, dtype=jnp.int32)[None, None, :]).astype(
        table.dtype
    )
    return jnp.einsum("bkp,bpc->bkc", onehot, table, preferred_element_type=jnp.float32).astype(
        table.dtype
    )


def body(
    points,
    weights,
    leaf_basis,
    leaf_rank,
    leaf_skeleton,
    near_list,
    far_list,
    node_basis,
    node_rank,
    node_skeleton,
    node_far,
    group_basis,
    group_rank,
    group_skeleton,
    group_far,
):
    leaf_count = leaf_rank.shape[0]
    leaf_size = points.shape[0] // leaf_count
    dim_count = points.shape[1]
    rhs_count = weights.shape[1]
    rank_count = leaf_basis.shape[1]
    node_width = node_basis.shape[1]
    group_width = group_basis.shape[1]
    local_points = points.reshape(leaf_count, leaf_size, dim_count)
    local_bases = leaf_basis.reshape(leaf_count, leaf_size, rank_count)
    local_weights = weights.reshape(leaf_count, leaf_size, rhs_count)
    first_leaf = lax.axis_index(FLAT) * leaf_count
    offset = first_leaf - REACH

    left_points, right_points = halos(points, REACH * leaf_size)
    left_weights, right_weights = halos(weights, REACH * leaf_size)

    leaf_mask = (
        lax.broadcasted_iota(jnp.int32, (leaf_count, rank_count), 1) < leaf_rank[:, None]
    ).astype(jnp.float32)
    leaf_up = (
        jnp.einsum("lpk,lpr->lkr", local_bases, local_weights, preferred_element_type=jnp.float32)
        * leaf_mask[:, :, None]
    ).astype(jnp.bfloat16)
    leaf_coords = select_within(local_points, leaf_skeleton)
    own_rows = jnp.concatenate([leaf_coords, leaf_up], axis=-1)
    skeleton_width = dim_count + rhs_count
    left_rows, right_rows = halos(
        own_rows.reshape(leaf_count * rank_count, skeleton_width), REACH * rank_count
    )

    node_mask = (jnp.arange(node_width, dtype=jnp.int32) < node_rank[0]).astype(jnp.float32)
    node_up = (
        jnp.einsum(
            "ak,ar->kr",
            node_basis,
            leaf_up.reshape(leaf_count * rank_count, rhs_count),
            preferred_element_type=jnp.float32,
        )
        * node_mask[:, None]
    ).astype(jnp.bfloat16)
    node_coords = select_rows(
        leaf_coords.reshape(leaf_count * rank_count, dim_count), node_skeleton[0]
    )
    columns = lax.axis_size("col")
    source_columns = node_far[0] % columns
    node_pack = jnp.concatenate([node_coords, node_up, group_basis], axis=1)
    gathered = lax.all_gather(node_pack[None], "col", axis=0, tiled=True)

    near_total = near_field(
        local_points,
        left_points.reshape(REACH, leaf_size, dim_count),
        right_points.reshape(REACH, leaf_size, dim_count),
        local_weights,
        left_weights.reshape(REACH, leaf_size, rhs_count),
        right_weights.reshape(REACH, leaf_size, rhs_count),
        near_list - offset,
    )

    all_coords = gathered[:, :, :dim_count]
    all_up = gathered[:, :, dim_count : dim_count + rhs_count]
    all_parts = gathered[:, :, dim_count + rhs_count :]
    picked_coords = select_rows(all_coords, source_columns)
    picked_up = select_rows(all_up, source_columns)
    kernel = kernel_block(jnp.broadcast_to(node_coords, picked_coords.shape), picked_coords)
    node_side = jnp.einsum("fab,fbr->ar", kernel, picked_up, preferred_element_type=jnp.float32)
    group_mask = (jnp.arange(group_width, dtype=jnp.int32) < group_rank[0]).astype(jnp.float32)
    group_up = (
        jnp.einsum("nag,nar->gr", all_parts, all_up, preferred_element_type=jnp.float32)
        * group_mask[:, None]
    ).astype(jnp.bfloat16)
    group_coords = select_rows(all_coords.reshape(columns * node_width, dim_count), group_skeleton[0])
    group_pack = jnp.concatenate([group_coords, group_up], axis=1)
    every_group = lax.all_gather(group_pack[None], "row", axis=0, tiled=True)
    picked_group = select_rows(every_group, group_far[0])
    picked_group_coords = picked_group[:, :, :dim_count]
    picked_group_up = picked_group[:, :, dim_count:]
    group_kernel = kernel_block(
        jnp.broadcast_to(group_coords, picked_group_coords.shape), picked_group_coords
    )
    group_down = (
        jnp.einsum("fab,fbr->ar", group_kernel, picked_group_up, preferred_element_type=jnp.float32)
        * group_mask[:, None]
    ).astype(jnp.bfloat16)
    node_down = (
        (jnp.dot(group_basis, group_down, preferred_element_type=jnp.float32) + node_side)
        * node_mask[:, None]
    ).astype(jnp.bfloat16)
    result = far_field(
        leaf_coords,
        left_rows.reshape(REACH, rank_count, skeleton_width),
        own_rows,
        right_rows.reshape(REACH, rank_count, skeleton_width),
        far_list - offset,
        leaf_rank,
        node_basis.reshape(leaf_count, rank_count, node_width),
        node_down,
        local_bases,
        near_total,
    )
    return result.reshape(leaf_count * leaf_size, rhs_count)


def solution(mesh):
    in_specs = (
        P(FLAT, None),
        P(FLAT, None),
        P(FLAT, None),
        P(FLAT),
        P(FLAT, None),
        P(FLAT, None),
        P(FLAT, None),
        P(FLAT, None),
        P(FLAT),
        P(FLAT, None),
        P(FLAT, None),
        P(FLAT, None),
        P("row"),
        P("row", None),
        P("row", None),
    )
    out_specs = P(FLAT, None)
    return jax.shard_map(body, mesh=mesh, in_specs=in_specs, out_specs=out_specs, check_vma=False)
```

```python
import jax
import jax.numpy as jnp
from jax import lax
from jax.experimental import pallas as pl
from jax.experimental.pallas import tpu as pltpu
from jax.sharding import PartitionSpec as P

REACH = 8
FLAT = ("row", "col")


def halos(cells, width):
    count = lax.axis_size(FLAT)
    ends = count - 1
    head = cells[:width]
    tail = cells[cells.shape[0] - width :]
    left = lax.ppermute(tail, FLAT, [(i, i + 1) for i in range(ends)])
    right = lax.ppermute(head, FLAT, [(i + 1, i) for i in range(ends)])
    return left, right


def kernel_block(left, right):
    left_square = jnp.sum(jnp.square(left.astype(jnp.float32)), axis=-1)
    right_square = jnp.sum(jnp.square(right.astype(jnp.float32)), axis=-1)
    inner = jnp.einsum("...md,...nd->...mn", left, right, preferred_element_type=jnp.float32)
    distance = left_square[..., :, None] + right_square[..., None, :] - 2.0 * inner
    return jnp.exp(distance * (-2.0 / left.shape[-1])).astype(jnp.bfloat16)


def contract_last(a, b):
    return lax.dot_general(a, b, (((1,), (1,)), ((), ())), preferred_element_type=jnp.float32)


def scaled_kernel(target, target_square, source, source_square):
    dims = target.shape[-1]
    inner = contract_last(target * jnp.asarray(4.0 / dims, target.dtype), source)
    return jnp.exp((target_square + source_square) + inner).astype(jnp.bfloat16)


def scaled_norms(cells):
    wide = cells.astype(jnp.float32)
    return (jnp.sum(wide * wide, axis=-1) * (-2.0 / cells.shape[-1]))[:, None, :]


def target_square_of(target):
    wide = target.astype(jnp.float32)
    return jnp.sum(wide * wide, axis=-1, keepdims=True) * (-2.0 / target.shape[-1])


def fetch_sources(index_ref, row, count, parts, buffers, sems, slot):
    for position in range(count):
        source = index_ref[row * count + position]
        for which, (left, own, right) in enumerate(parts):
            halo = left.shape[0]
            mine = own.shape[0]
            target = buffers[which](slot, position)
            sem = sems.at[which, slot, position]

            @pl.when(source < halo)
            def _():
                pltpu.make_async_copy(left.at[source], target, sem).start()

            @pl.when((source >= halo) & (source < halo + mine))
            def _():
                pltpu.make_async_copy(own.at[source - halo], target, sem).start()

            @pl.when(source >= halo + mine)
            def _():
                pltpu.make_async_copy(right.at[source - halo - mine], target, sem).start()


def wait_sources(count, parts, buffers, sems, slot):
    for position in range(count):
        for which, (left, own, right) in enumerate(parts):
            pltpu.make_async_copy(
                own.at[0], buffers[which](slot, position), sems.at[which, slot, position]
            ).wait()


def pipelined_sources(index_ref, count, parts, buffers, sems):
    leaf = pl.program_id(0)
    leaves = pl.num_programs(0)
    slot = leaf % 2

    @pl.when(leaf == 0)
    def _():
        fetch_sources(index_ref, 0, count, parts, buffers, sems, 0)

    @pl.when(leaf + 1 < leaves)
    def _():
        fetch_sources(index_ref, leaf + 1, count, parts, buffers, sems, 1 - slot)

    wait_sources(count, parts, buffers, sems, slot)
    return slot


def near_kernel(index_ref, target_ref, lp, op, rp, lw, ow, rw, ln, on, rn, out_ref, point_buf, weight_buf, norm_buf, sems):
    count, size = point_buf.shape[1], point_buf.shape[2]
    parts = ((lp, op, rp), (lw, ow, rw), (ln, on, rn))
    buffers = (
        lambda slot, position: point_buf.at[slot, position],
        lambda slot, position: weight_buf.at[slot, position],
        lambda slot, position: norm_buf.at[slot, :, pl.ds(position * size, size)],
    )
    slot = pipelined_sources(index_ref, count, parts, buffers, sems)
    target = target_ref[0]
    sources = point_buf[slot].reshape(count * size, point_buf.shape[-1])
    values = weight_buf[slot].reshape(count * size, weight_buf.shape[-1])
    kernel = scaled_kernel(target, target_square_of(target), sources, norm_buf[slot])
    out_ref[0] = jnp.dot(kernel, values, preferred_element_type=jnp.float32)


def near_field(local_points, left_points, right_points, local_weights, left_weights, right_weights, local_norms, left_norms, right_norms, near_local):
    leaves, size, dims = local_points.shape
    rhs = local_weights.shape[-1]
    count = near_local.shape[1]
    anywhere = pl.BlockSpec(memory_space=pl.ANY)
    return pl.pallas_call(
        near_kernel,
        grid_spec=pltpu.PrefetchScalarGridSpec(
            num_scalar_prefetch=1,
            grid=(leaves,),
            in_specs=[pl.BlockSpec((1, size, dims), lambda l, index: (l, 0, 0))] + [anywhere] * 9,
            out_specs=pl.BlockSpec((1, size, rhs), lambda l, index: (l, 0, 0)),
            scratch_shapes=[
                pltpu.VMEM((2, count, size, dims), local_points.dtype),
                pltpu.VMEM((2, count, size, rhs), local_weights.dtype),
                pltpu.VMEM((2, 1, count * size), jnp.float32),
                pltpu.SemaphoreType.DMA((3, 2, count)),
            ],
        ),
        out_shape=jax.ShapeDtypeStruct((leaves, size, rhs), jnp.float32),
        compiler_params=pltpu.CompilerParams(dimension_semantics=("arbitrary",)),
    )(
        near_local.reshape(-1),
        local_points,
        left_points,
        local_points,
        right_points,
        left_weights,
        local_weights,
        right_weights,
        left_norms,
        local_norms,
        right_norms,
    )


def far_kernel(index_ref, target_ref, ls, os, rs, ln, on, rn, out_ref, source_buf, norm_buf, sems):
    count, rank = source_buf.shape[1], source_buf.shape[2]
    parts = ((ls, os, rs), (ln, on, rn))
    buffers = (
        lambda slot, position: source_buf.at[slot, position],
        lambda slot, position: norm_buf.at[slot, :, pl.ds(position * rank, rank)],
    )
    slot = pipelined_sources(index_ref, count, parts, buffers, sems)
    target = target_ref[0]
    dims = target.shape[-1]
    sources = source_buf[slot].reshape(count * rank, source_buf.shape[-1])
    kernel = scaled_kernel(target, target_square_of(target), sources[:, :dims], norm_buf[slot])
    out_ref[0] = jnp.dot(kernel, sources[:, dims:], preferred_element_type=jnp.float32)


def far_field(leaf_coords, left_rows, own_rows, right_rows, left_norms, own_norms, right_norms, far_local):
    leaves, rank, dims = leaf_coords.shape
    width = own_rows.shape[-1]
    count = far_local.shape[1]
    anywhere = pl.BlockSpec(memory_space=pl.ANY)
    return pl.pallas_call(
        far_kernel,
        grid_spec=pltpu.PrefetchScalarGridSpec(
            num_scalar_prefetch=1,
            grid=(leaves,),
            in_specs=[pl.BlockSpec((1, rank, dims), lambda l, index: (l, 0, 0))] + [anywhere] * 6,
            out_specs=pl.BlockSpec((1, rank, width - dims), lambda l, index: (l, 0, 0)),
            scratch_shapes=[
                pltpu.VMEM((2, count, rank, width), own_rows.dtype),
                pltpu.VMEM((2, 1, count * rank), jnp.float32),
                pltpu.SemaphoreType.DMA((2, 2, count)),
            ],
        ),
        out_shape=jax.ShapeDtypeStruct((leaves, rank, width - dims), jnp.float32),
        compiler_params=pltpu.CompilerParams(dimension_semantics=("arbitrary",)),
    )(
        far_local.reshape(-1),
        leaf_coords,
        left_rows,
        own_rows,
        right_rows,
        left_norms,
        own_norms,
        right_norms,
    )


def final_kernel(rank_ref, basis_ref, down_ref, far_ref, leaf_base_ref, near_ref, out_ref):
    leaf = pl.program_id(0)
    total = jnp.dot(basis_ref[0], down_ref[...], preferred_element_type=jnp.float32) + far_ref[0]
    rows = lax.broadcasted_iota(jnp.int32, total.shape, 0)
    leaf_down = jnp.where(rows < rank_ref[leaf], total, 0.0).astype(jnp.bfloat16)
    result = jnp.dot(leaf_base_ref[0], leaf_down, preferred_element_type=jnp.float32) + near_ref[0]
    out_ref[0] = result.astype(out_ref.dtype)


def final_field(leaf_rank, bases, node_down, far_total, leaf_bases, near_total):
    leaves, rank, width = bases.shape
    size = leaf_bases.shape[1]
    rhs = near_total.shape[-1]

    def own(l, ranks):
        return (l, 0, 0)

    return pl.pallas_call(
        final_kernel,
        grid_spec=pltpu.PrefetchScalarGridSpec(
            num_scalar_prefetch=1,
            grid=(leaves,),
            in_specs=[
                pl.BlockSpec((1, rank, width), own),
                pl.BlockSpec(node_down.shape, lambda l, ranks: (0, 0)),
                pl.BlockSpec((1, rank, rhs), own),
                pl.BlockSpec((1, size, rank), own),
                pl.BlockSpec((1, size, rhs), own),
            ],
            out_specs=pl.BlockSpec((1, size, rhs), own),
        ),
        out_shape=jax.ShapeDtypeStruct((leaves, size, rhs), jnp.bfloat16),
    )(leaf_rank, bases, node_down, far_total, leaf_bases, near_total)


def select_rows(table, index):
    count = table.shape[0]
    onehot = (index[:, None] == jnp.arange(count, dtype=jnp.int32)[None, :]).astype(table.dtype)
    picked = jnp.dot(onehot, table.reshape(count, -1), preferred_element_type=jnp.float32).astype(
        table.dtype
    )
    return picked.reshape(index.shape + table.shape[1:])


def select_within(table, index):
    count = table.shape[1]
    onehot = (index[:, :, None] == jnp.arange(count, dtype=jnp.int32)[None, None, :]).astype(
        table.dtype
    )
    return jnp.einsum("bkp,bpc->bkc", onehot, table, preferred_element_type=jnp.float32).astype(
        table.dtype
    )


def body(
    points,
    weights,
    leaf_basis,
    leaf_rank,
    leaf_skeleton,
    near_list,
    far_list,
    node_basis,
    node_rank,
    node_skeleton,
    node_far,
    group_basis,
    group_rank,
    group_skeleton,
    group_far,
):
    leaf_count = leaf_rank.shape[0]
    leaf_size = points.shape[0] // leaf_count
    dim_count = points.shape[1]
    rhs_count = weights.shape[1]
    rank_count = leaf_basis.shape[1]
    node_width = node_basis.shape[1]
    group_width = group_basis.shape[1]
    local_points = points.reshape(leaf_count, leaf_size, dim_count)
    local_bases = leaf_basis.reshape(leaf_count, leaf_size, rank_count)
    local_weights = weights.reshape(leaf_count, leaf_size, rhs_count)
    first_leaf = lax.axis_index(FLAT) * leaf_count
    offset = first_leaf - REACH

    left_points, right_points = halos(points, REACH * leaf_size)
    left_weights, right_weights = halos(weights, REACH * leaf_size)

    leaf_mask = (
        lax.broadcasted_iota(jnp.int32, (leaf_count, rank_count), 1) < leaf_rank[:, None]
    ).astype(jnp.float32)
    leaf_up = (
        jnp.einsum("lpk,lpr->lkr", local_bases, local_weights, preferred_element_type=jnp.float32)
        * leaf_mask[:, :, None]
    ).astype(jnp.bfloat16)
    leaf_coords = select_within(local_points, leaf_skeleton)
    own_rows = jnp.concatenate([leaf_coords, leaf_up], axis=-1)
    skeleton_width = dim_count + rhs_count
    left_rows, right_rows = halos(
        own_rows.reshape(leaf_count * rank_count, skeleton_width), REACH * rank_count
    )

    node_mask = (jnp.arange(node_width, dtype=jnp.int32) < node_rank[0]).astype(jnp.float32)
    node_up = (
        jnp.einsum(
            "ak,ar->kr",
            node_basis,
            leaf_up.reshape(leaf_count * rank_count, rhs_count),
            preferred_element_type=jnp.float32,
        )
        * node_mask[:, None]
    ).astype(jnp.bfloat16)
    node_coords = select_rows(
        leaf_coords.reshape(leaf_count * rank_count, dim_count), node_skeleton[0]
    )
    columns = lax.axis_size("col")
    source_columns = node_far[0] % columns
    node_pack = jnp.concatenate([node_coords, node_up, group_basis], axis=1)
    gathered = lax.all_gather(node_pack[None], "col", axis=0, tiled=True)

    left_points = left_points.reshape(REACH, leaf_size, dim_count)
    right_points = right_points.reshape(REACH, leaf_size, dim_count)
    near_total = near_field(
        local_points,
        left_points,
        right_points,
        local_weights,
        left_weights.reshape(REACH, leaf_size, rhs_count),
        right_weights.reshape(REACH, leaf_size, rhs_count),
        scaled_norms(local_points),
        scaled_norms(left_points),
        scaled_norms(right_points),
        near_list - offset,
    )

    all_coords = gathered[:, :, :dim_count]
    all_up = gathered[:, :, dim_count : dim_count + rhs_count]
    all_parts = gathered[:, :, dim_count + rhs_count :]
    picked_coords = select_rows(all_coords, source_columns)
    picked_up = select_rows(all_up, source_columns)
    kernel = kernel_block(jnp.broadcast_to(node_coords, picked_coords.shape), picked_coords)
    node_side = jnp.einsum("fab,fbr->ar", kernel, picked_up, preferred_element_type=jnp.float32)
    group_mask = (jnp.arange(group_width, dtype=jnp.int32) < group_rank[0]).astype(jnp.float32)
    group_up = (
        jnp.einsum("nag,nar->gr", all_parts, all_up, preferred_element_type=jnp.float32)
        * group_mask[:, None]
    ).astype(jnp.bfloat16)
    group_coords = select_rows(all_coords.reshape(columns * node_width, dim_count), group_skeleton[0])
    group_pack = jnp.concatenate([group_coords, group_up], axis=1)
    every_group = lax.all_gather(group_pack[None], "row", axis=0, tiled=True)
    picked_group = select_rows(every_group, group_far[0])
    picked_group_coords = picked_group[:, :, :dim_count]
    picked_group_up = picked_group[:, :, dim_count:]
    group_kernel = kernel_block(
        jnp.broadcast_to(group_coords, picked_group_coords.shape), picked_group_coords
    )
    group_down = (
        jnp.einsum("fab,fbr->ar", group_kernel, picked_group_up, preferred_element_type=jnp.float32)
        * group_mask[:, None]
    ).astype(jnp.bfloat16)
    node_down = (
        (jnp.dot(group_basis, group_down, preferred_element_type=jnp.float32) + node_side)
        * node_mask[:, None]
    ).astype(jnp.bfloat16)
    left_rows = left_rows.reshape(REACH, rank_count, skeleton_width)
    right_rows = right_rows.reshape(REACH, rank_count, skeleton_width)
    far_total = far_field(
        leaf_coords,
        left_rows,
        own_rows,
        right_rows,
        scaled_norms(left_rows[:, :, :dim_count]),
        scaled_norms(leaf_coords),
        scaled_norms(right_rows[:, :, :dim_count]),
        far_list - offset,
    )
    result = final_field(
        leaf_rank,
        node_basis.reshape(leaf_count, rank_count, node_width),
        node_down,
        far_total,
        local_bases,
        near_total,
    )
    return result.reshape(leaf_count * leaf_size, rhs_count)


def solution(mesh):
    in_specs = (
        P(FLAT, None),
        P(FLAT, None),
        P(FLAT, None),
        P(FLAT),
        P(FLAT, None),
        P(FLAT, None),
        P(FLAT, None),
        P(FLAT, None),
        P(FLAT),
        P(FLAT, None),
        P(FLAT, None),
        P(FLAT, None),
        P("row"),
        P("row", None),
        P("row", None),
    )
    out_specs = P(FLAT, None)
    return jax.shard_map(body, mesh=mesh, in_specs=in_specs, out_specs=out_specs, check_vma=False)
```

```python
import jax
import jax.numpy as jnp
from jax import lax
from jax.experimental import pallas as pl
from jax.experimental.pallas import tpu as pltpu
from jax.sharding import PartitionSpec as P

REACH = 8
FLAT = ("row", "col")


def halos(cells, width):
    count = lax.axis_size(FLAT)
    ends = count - 1
    head = cells[:width]
    tail = cells[cells.shape[0] - width :]
    left = lax.ppermute(tail, FLAT, [(i, i + 1) for i in range(ends)])
    right = lax.ppermute(head, FLAT, [(i + 1, i) for i in range(ends)])
    return left, right


def kernel_block(left, right):
    left_square = jnp.sum(jnp.square(left.astype(jnp.float32)), axis=-1)
    right_square = jnp.sum(jnp.square(right.astype(jnp.float32)), axis=-1)
    inner = jnp.einsum("...md,...nd->...mn", left, right, preferred_element_type=jnp.float32)
    distance = left_square[..., :, None] + right_square[..., None, :] - 2.0 * inner
    return jnp.exp(distance * (-2.0 / left.shape[-1])).astype(jnp.bfloat16)


def contract_last(a, b):
    return lax.dot_general(a, b, (((1,), (1,)), ((), ())), preferred_element_type=jnp.float32)


def scaled_kernel(target, target_square, source, source_square):
    dims = target.shape[-1]
    inner = contract_last(target * jnp.asarray(4.0 / dims, target.dtype), source)
    return jnp.exp((target_square + source_square) + inner).astype(jnp.bfloat16)


def scaled_norms(cells):
    wide = cells.astype(jnp.float32)
    return (jnp.sum(wide * wide, axis=-1) * (-2.0 / cells.shape[-1]))[:, None, :]


def target_square_of(target):
    wide = target.astype(jnp.float32)
    return jnp.sum(wide * wide, axis=-1, keepdims=True) * (-2.0 / target.shape[-1])


def fetch_sources(index_ref, row, count, parts, buffers, sems, slot):
    for position in range(count):
        source = index_ref[row * count + position]
        for which, (left, own, right) in enumerate(parts):
            halo = left.shape[0]
            mine = own.shape[0]
            target = buffers[which](slot, position)
            sem = sems.at[which, slot, position]

            @pl.when(source < halo)
            def _():
                pltpu.make_async_copy(left.at[source], target, sem).start()

            @pl.when((source >= halo) & (source < halo + mine))
            def _():
                pltpu.make_async_copy(own.at[source - halo], target, sem).start()

            @pl.when(source >= halo + mine)
            def _():
                pltpu.make_async_copy(right.at[source - halo - mine], target, sem).start()


def wait_sources(count, parts, buffers, sems, slot):
    for position in range(count):
        for which, (left, own, right) in enumerate(parts):
            pltpu.make_async_copy(
                own.at[0], buffers[which](slot, position), sems.at[which, slot, position]
            ).wait()


def pipelined_sources(index_ref, count, parts, buffers, sems):
    leaf = pl.program_id(0)
    leaves = pl.num_programs(0)
    slot = leaf % 2

    @pl.when(leaf == 0)
    def _():
        fetch_sources(index_ref, 0, count, parts, buffers, sems, 0)

    @pl.when(leaf + 1 < leaves)
    def _():
        fetch_sources(index_ref, leaf + 1, count, parts, buffers, sems, 1 - slot)

    wait_sources(count, parts, buffers, sems, slot)
    return slot


def near_kernel(index_ref, target_ref, lp, op, rp, lw, ow, rw, ln, on, rn, out_ref, point_buf, weight_buf, norm_buf, sems):
    count, size = point_buf.shape[1], point_buf.shape[2]
    parts = ((lp, op, rp), (lw, ow, rw), (ln, on, rn))
    buffers = (
        lambda slot, position: point_buf.at[slot, position],
        lambda slot, position: weight_buf.at[slot, position],
        lambda slot, position: norm_buf.at[slot, :, pl.ds(position * size, size)],
    )
    slot = pipelined_sources(index_ref, count, parts, buffers, sems)
    target = target_ref[0]
    sources = point_buf[slot].reshape(count * size, point_buf.shape[-1])
    values = weight_buf[slot].reshape(count * size, weight_buf.shape[-1])
    kernel = scaled_kernel(target, target_square_of(target), sources, norm_buf[slot])
    out_ref[0] = jnp.dot(kernel, values, preferred_element_type=jnp.float32)


def near_field(local_points, left_points, right_points, local_weights, left_weights, right_weights, local_norms, left_norms, right_norms, near_local):
    leaves, size, dims = local_points.shape
    rhs = local_weights.shape[-1]
    count = near_local.shape[1]
    anywhere = pl.BlockSpec(memory_space=pl.ANY)
    return pl.pallas_call(
        near_kernel,
        grid_spec=pltpu.PrefetchScalarGridSpec(
            num_scalar_prefetch=1,
            grid=(leaves,),
            in_specs=[pl.BlockSpec((1, size, dims), lambda l, index: (l, 0, 0))] + [anywhere] * 9,
            out_specs=pl.BlockSpec((1, size, rhs), lambda l, index: (l, 0, 0)),
            scratch_shapes=[
                pltpu.VMEM((2, count, size, dims), local_points.dtype),
                pltpu.VMEM((2, count, size, rhs), local_weights.dtype),
                pltpu.VMEM((2, 1, count * size), jnp.float32),
                pltpu.SemaphoreType.DMA((3, 2, count)),
            ],
        ),
        out_shape=jax.ShapeDtypeStruct((leaves, size, rhs), jnp.float32),
        compiler_params=pltpu.CompilerParams(dimension_semantics=("arbitrary",)),
    )(
        near_local.reshape(-1),
        local_points,
        left_points,
        local_points,
        right_points,
        left_weights,
        local_weights,
        right_weights,
        left_norms,
        local_norms,
        right_norms,
    )


def far_kernel(index_ref, target_ref, ls, os, rs, ln, on, rn, after_ref, out_ref, source_buf, norm_buf, sems):
    count, rank = source_buf.shape[1], source_buf.shape[2]
    parts = ((ls, os, rs), (ln, on, rn))
    buffers = (
        lambda slot, position: source_buf.at[slot, position],
        lambda slot, position: norm_buf.at[slot, :, pl.ds(position * rank, rank)],
    )
    slot = pipelined_sources(index_ref, count, parts, buffers, sems)
    target = target_ref[0]
    dims = target.shape[-1]
    sources = source_buf[slot].reshape(count * rank, source_buf.shape[-1])
    kernel = scaled_kernel(target, target_square_of(target), sources[:, :dims], norm_buf[slot])
    out_ref[0] = jnp.dot(kernel, sources[:, dims:], preferred_element_type=jnp.float32)


def far_field(leaf_coords, left_rows, own_rows, right_rows, left_norms, own_norms, right_norms, far_local, after):
    leaves, rank, dims = leaf_coords.shape
    width = own_rows.shape[-1]
    count = far_local.shape[1]
    anywhere = pl.BlockSpec(memory_space=pl.ANY)
    return pl.pallas_call(
        far_kernel,
        grid_spec=pltpu.PrefetchScalarGridSpec(
            num_scalar_prefetch=1,
            grid=(leaves,),
            in_specs=[pl.BlockSpec((1, rank, dims), lambda l, index: (l, 0, 0))] + [anywhere] * 7,
            out_specs=pl.BlockSpec((1, rank, width - dims), lambda l, index: (l, 0, 0)),
            scratch_shapes=[
                pltpu.VMEM((2, count, rank, width), own_rows.dtype),
                pltpu.VMEM((2, 1, count * rank), jnp.float32),
                pltpu.SemaphoreType.DMA((2, 2, count)),
            ],
        ),
        out_shape=jax.ShapeDtypeStruct((leaves, rank, width - dims), jnp.float32),
        compiler_params=pltpu.CompilerParams(dimension_semantics=("arbitrary",)),
    )(
        far_local.reshape(-1),
        leaf_coords,
        left_rows,
        own_rows,
        right_rows,
        left_norms,
        own_norms,
        right_norms,
        after,
    )


def final_kernel(rank_ref, basis_ref, down_ref, far_ref, leaf_base_ref, near_ref, out_ref):
    block = basis_ref.shape[0]
    step = pl.program_id(0)
    down = down_ref[...]
    for inside in range(block):
        total = jnp.dot(basis_ref[inside], down, preferred_element_type=jnp.float32) + far_ref[inside]
        rows = lax.broadcasted_iota(jnp.int32, total.shape, 0)
        leaf_down = jnp.where(rows < rank_ref[step * block + inside], total, 0.0).astype(jnp.bfloat16)
        result = (
            jnp.dot(leaf_base_ref[inside], leaf_down, preferred_element_type=jnp.float32)
            + near_ref[inside]
        )
        out_ref[inside] = result.astype(out_ref.dtype)


def final_field(leaf_rank, bases, node_down, far_total, leaf_bases, near_total):
    leaves, rank, width = bases.shape
    size = leaf_bases.shape[1]
    rhs = near_total.shape[-1]
    block = max(b for b in (1, 2, 3, 4) if leaves % b == 0)

    def own(l, ranks):
        return (l, 0, 0)

    return pl.pallas_call(
        final_kernel,
        grid_spec=pltpu.PrefetchScalarGridSpec(
            num_scalar_prefetch=1,
            grid=(leaves // block,),
            in_specs=[
                pl.BlockSpec((block, rank, width), own),
                pl.BlockSpec(node_down.shape, lambda l, ranks: (0, 0)),
                pl.BlockSpec((block, rank, rhs), own),
                pl.BlockSpec((block, size, rank), own),
                pl.BlockSpec((block, size, rhs), own),
            ],
            out_specs=pl.BlockSpec((block, size, rhs), own),
        ),
        out_shape=jax.ShapeDtypeStruct((leaves, size, rhs), jnp.bfloat16),
    )(leaf_rank, bases, node_down, far_total, leaf_bases, near_total)


def select_rows(table, index):
    count = table.shape[0]
    onehot = (index[:, None] == jnp.arange(count, dtype=jnp.int32)[None, :]).astype(table.dtype)
    picked = jnp.dot(onehot, table.reshape(count, -1), preferred_element_type=jnp.float32).astype(
        table.dtype
    )
    return picked.reshape(index.shape + table.shape[1:])


def select_within(table, index):
    count = table.shape[1]
    onehot = (index[:, :, None] == jnp.arange(count, dtype=jnp.int32)[None, None, :]).astype(
        table.dtype
    )
    return jnp.einsum("bkp,bpc->bkc", onehot, table, preferred_element_type=jnp.float32).astype(
        table.dtype
    )


def body(
    points,
    weights,
    leaf_basis,
    leaf_rank,
    leaf_skeleton,
    near_list,
    far_list,
    node_basis,
    node_rank,
    node_skeleton,
    node_far,
    group_basis,
    group_rank,
    group_skeleton,
    group_far,
):
    leaf_count = leaf_rank.shape[0]
    leaf_size = points.shape[0] // leaf_count
    dim_count = points.shape[1]
    rhs_count = weights.shape[1]
    rank_count = leaf_basis.shape[1]
    node_width = node_basis.shape[1]
    group_width = group_basis.shape[1]
    local_points = points.reshape(leaf_count, leaf_size, dim_count)
    local_bases = leaf_basis.reshape(leaf_count, leaf_size, rank_count)
    local_weights = weights.reshape(leaf_count, leaf_size, rhs_count)
    first_leaf = lax.axis_index(FLAT) * leaf_count
    offset = first_leaf - REACH

    left_points, right_points = halos(points, REACH * leaf_size)
    left_weights, right_weights = halos(weights, REACH * leaf_size)

    leaf_mask = (
        lax.broadcasted_iota(jnp.int32, (leaf_count, rank_count), 1) < leaf_rank[:, None]
    ).astype(jnp.float32)
    leaf_up = (
        jnp.einsum("lpk,lpr->lkr", local_bases, local_weights, preferred_element_type=jnp.float32)
        * leaf_mask[:, :, None]
    ).astype(jnp.bfloat16)
    leaf_coords = select_within(local_points, leaf_skeleton)
    own_rows = jnp.concatenate([leaf_coords, leaf_up], axis=-1)
    skeleton_width = dim_count + rhs_count
    left_rows, right_rows = halos(
        own_rows.reshape(leaf_count * rank_count, skeleton_width), REACH * rank_count
    )

    node_mask = (jnp.arange(node_width, dtype=jnp.int32) < node_rank[0]).astype(jnp.float32)
    node_up = (
        jnp.einsum(
            "ak,ar->kr",
            node_basis,
            leaf_up.reshape(leaf_count * rank_count, rhs_count),
            preferred_element_type=jnp.float32,
        )
        * node_mask[:, None]
    ).astype(jnp.bfloat16)
    node_coords = select_rows(
        leaf_coords.reshape(leaf_count * rank_count, dim_count), node_skeleton[0]
    )
    columns = lax.axis_size("col")
    source_columns = node_far[0] % columns
    node_pack = jnp.concatenate([node_coords, node_up, group_basis], axis=1)
    gathered = lax.all_gather(node_pack[None], "col", axis=0, tiled=True)

    left_points = left_points.reshape(REACH, leaf_size, dim_count)
    right_points = right_points.reshape(REACH, leaf_size, dim_count)
    near_total = near_field(
        local_points,
        left_points,
        right_points,
        local_weights,
        left_weights.reshape(REACH, leaf_size, rhs_count),
        right_weights.reshape(REACH, leaf_size, rhs_count),
        scaled_norms(local_points),
        scaled_norms(left_points),
        scaled_norms(right_points),
        near_list - offset,
    )

    all_coords = gathered[:, :, :dim_count]
    all_up = gathered[:, :, dim_count : dim_count + rhs_count]
    all_parts = gathered[:, :, dim_count + rhs_count :]
    picked_coords = select_rows(all_coords, source_columns)
    picked_up = select_rows(all_up, source_columns)
    kernel = kernel_block(jnp.broadcast_to(node_coords, picked_coords.shape), picked_coords)
    node_side = jnp.einsum("fab,fbr->ar", kernel, picked_up, preferred_element_type=jnp.float32)
    group_mask = (jnp.arange(group_width, dtype=jnp.int32) < group_rank[0]).astype(jnp.float32)
    group_up = (
        jnp.einsum("nag,nar->gr", all_parts, all_up, preferred_element_type=jnp.float32)
        * group_mask[:, None]
    ).astype(jnp.bfloat16)
    group_coords = select_rows(all_coords.reshape(columns * node_width, dim_count), group_skeleton[0])
    group_pack = jnp.concatenate([group_coords, group_up], axis=1)
    left_rows = left_rows.reshape(REACH, rank_count, skeleton_width)
    right_rows = right_rows.reshape(REACH, rank_count, skeleton_width)
    far_total = far_field(
        leaf_coords,
        left_rows,
        own_rows,
        right_rows,
        scaled_norms(left_rows[:, :, :dim_count]),
        scaled_norms(leaf_coords),
        scaled_norms(right_rows[:, :, :dim_count]),
        far_list - offset,
        group_pack,
    )
    rows = lax.axis_size("row")
    received = [group_pack] + [
        lax.ppermute(group_pack, "row", [(r, (r + shift) % rows) for r in range(rows)])
        for shift in range(1, rows)
    ]
    shifts = (lax.axis_index("row") - group_far[0]) % rows
    picked_group = select_rows(jnp.stack(received), shifts)
    picked_group_coords = picked_group[:, :, :dim_count]
    picked_group_up = picked_group[:, :, dim_count:]
    group_kernel = kernel_block(
        jnp.broadcast_to(group_coords, picked_group_coords.shape), picked_group_coords
    )
    group_down = (
        jnp.einsum("fab,fbr->ar", group_kernel, picked_group_up, preferred_element_type=jnp.float32)
        * group_mask[:, None]
    ).astype(jnp.bfloat16)
    node_down = (
        (jnp.dot(group_basis, group_down, preferred_element_type=jnp.float32) + node_side)
        * node_mask[:, None]
    ).astype(jnp.bfloat16)
    result = final_field(
        leaf_rank,
        node_basis.reshape(leaf_count, rank_count, node_width),
        node_down,
        far_total,
        local_bases,
        near_total,
    )
    return result.reshape(leaf_count * leaf_size, rhs_count)


def solution(mesh):
    in_specs = (
        P(FLAT, None),
        P(FLAT, None),
        P(FLAT, None),
        P(FLAT),
        P(FLAT, None),
        P(FLAT, None),
        P(FLAT, None),
        P(FLAT, None),
        P(FLAT),
        P(FLAT, None),
        P(FLAT, None),
        P(FLAT, None),
        P("row"),
        P("row", None),
        P("row", None),
    )
    out_specs = P(FLAT, None)
    return jax.shard_map(body, mesh=mesh, in_specs=in_specs, out_specs=out_specs, check_vma=False)
```

```python
import jax
import jax.numpy as jnp
from jax import lax
from jax.experimental import pallas as pl
from jax.experimental.pallas import tpu as pltpu
from jax.sharding import PartitionSpec as P

REACH = 8
FLAT = ("row", "col")


def halos(cells, width):
    count = lax.axis_size(FLAT)
    ends = count - 1
    head = jnp.concatenate([cell[:width] for cell in cells], axis=1)
    tail = jnp.concatenate([cell[cell.shape[0] - width :] for cell in cells], axis=1)
    left = lax.ppermute(tail, FLAT, [(i, i + 1) for i in range(ends)])
    right = lax.ppermute(head, FLAT, [(i + 1, i) for i in range(ends)])
    return left, right


def kernel_block(left, right):
    left_square = jnp.sum(jnp.square(left.astype(jnp.float32)), axis=-1)
    right_square = jnp.sum(jnp.square(right.astype(jnp.float32)), axis=-1)
    inner = jnp.einsum("...md,...nd->...mn", left, right, preferred_element_type=jnp.float32)
    distance = left_square[..., :, None] + right_square[..., None, :] - 2.0 * inner
    return jnp.exp(distance * (-2.0 / left.shape[-1])).astype(jnp.bfloat16)


def contract_last(a, b):
    return lax.dot_general(a, b, (((1,), (1,)), ((), ())), preferred_element_type=jnp.float32)


def scaled_kernel(target, target_square, source, source_square):
    dims = target.shape[-1]
    inner = contract_last(target * jnp.asarray(4.0 / dims, target.dtype), source)
    return jnp.exp((target_square + source_square) + inner).astype(jnp.bfloat16)


def scaled_norms(cells):
    wide = cells.astype(jnp.float32)
    return (jnp.sum(wide * wide, axis=-1) * (-2.0 / cells.shape[-1]))[:, None, :]


def target_square_of(target):
    wide = target.astype(jnp.float32)
    return jnp.sum(wide * wide, axis=-1, keepdims=True) * (-2.0 / target.shape[-1])


def fetch_sources(index_ref, row, count, parts, buffers, sems, slot):
    for position in range(count):
        source = index_ref[row * count + position]
        for which, (halo, mine, left, own, right) in enumerate(parts):
            target = buffers[which](slot, position)
            sem = sems.at[which, slot, position]

            @pl.when(source < halo)
            def _():
                pltpu.make_async_copy(left(source), target, sem).start()

            @pl.when((source >= halo) & (source < halo + mine))
            def _():
                pltpu.make_async_copy(own(source - halo), target, sem).start()

            @pl.when(source >= halo + mine)
            def _():
                pltpu.make_async_copy(right(source - halo - mine), target, sem).start()


def wait_sources(count, parts, buffers, sems, slot):
    for position in range(count):
        for which, (halo, mine, left, own, right) in enumerate(parts):
            pltpu.make_async_copy(
                own(0), buffers[which](slot, position), sems.at[which, slot, position]
            ).wait()


def rows_of(ref):
    return lambda index: ref.at[index]


def whole_rows(left, own, right):
    return (left.shape[0], own.shape[0], rows_of(left), rows_of(own), rows_of(right))


def lane_rows(left, own, right, start, width):
    def halo_at(ref):
        return lambda index: ref.at[index, :, pl.ds(start, width)]

    return (left.shape[0], own.shape[0], halo_at(left), rows_of(own), halo_at(right))


def pipelined_sources(index_ref, count, parts, buffers, sems):
    leaf = pl.program_id(0)
    leaves = pl.num_programs(0)
    slot = leaf % 2

    @pl.when(leaf == 0)
    def _():
        fetch_sources(index_ref, 0, count, parts, buffers, sems, 0)

    @pl.when(leaf + 1 < leaves)
    def _():
        fetch_sources(index_ref, leaf + 1, count, parts, buffers, sems, 1 - slot)

    wait_sources(count, parts, buffers, sems, slot)
    return slot


def near_kernel(index_ref, target_ref, lpw, op, rpw, ow, ln, on, rn, out_ref, point_buf, weight_buf, norm_buf, sems):
    count, size, dims = point_buf.shape[1], point_buf.shape[2], point_buf.shape[3]
    parts = (
        lane_rows(lpw, op, rpw, 0, dims),
        lane_rows(lpw, ow, rpw, dims, weight_buf.shape[-1]),
        whole_rows(ln, on, rn),
    )
    buffers = (
        lambda slot, position: point_buf.at[slot, position],
        lambda slot, position: weight_buf.at[slot, position],
        lambda slot, position: norm_buf.at[slot, :, pl.ds(position * size, size)],
    )
    slot = pipelined_sources(index_ref, count, parts, buffers, sems)
    target = target_ref[0]
    sources = point_buf[slot].reshape(count * size, point_buf.shape[-1])
    values = weight_buf[slot].reshape(count * size, weight_buf.shape[-1])
    kernel = scaled_kernel(target, target_square_of(target), sources, norm_buf[slot])
    out_ref[0] = jnp.dot(kernel, values, preferred_element_type=jnp.float32)


def near_field(local_points, local_weights, left_pairs, right_pairs, local_norms, left_norms, right_norms, near_local):
    leaves, size, dims = local_points.shape
    rhs = local_weights.shape[-1]
    count = near_local.shape[1]
    anywhere = pl.BlockSpec(memory_space=pl.ANY)
    return pl.pallas_call(
        near_kernel,
        grid_spec=pltpu.PrefetchScalarGridSpec(
            num_scalar_prefetch=1,
            grid=(leaves,),
            in_specs=[pl.BlockSpec((1, size, dims), lambda l, index: (l, 0, 0))] + [anywhere] * 7,
            out_specs=pl.BlockSpec((1, size, rhs), lambda l, index: (l, 0, 0)),
            scratch_shapes=[
                pltpu.VMEM((2, count, size, dims), local_points.dtype),
                pltpu.VMEM((2, count, size, rhs), local_weights.dtype),
                pltpu.VMEM((2, 1, count * size), jnp.float32),
                pltpu.SemaphoreType.DMA((3, 2, count)),
            ],
        ),
        out_shape=jax.ShapeDtypeStruct((leaves, size, rhs), jnp.float32),
        compiler_params=pltpu.CompilerParams(dimension_semantics=("arbitrary",)),
    )(
        near_local.reshape(-1),
        local_points,
        left_pairs,
        local_points,
        right_pairs,
        local_weights,
        left_norms,
        local_norms,
        right_norms,
    )


def far_kernel(index_ref, target_ref, ls, os, rs, ln, on, rn, after_ref, out_ref, source_buf, norm_buf, sems):
    count, rank = source_buf.shape[1], source_buf.shape[2]
    parts = (whole_rows(ls, os, rs), whole_rows(ln, on, rn))
    buffers = (
        lambda slot, position: source_buf.at[slot, position],
        lambda slot, position: norm_buf.at[slot, :, pl.ds(position * rank, rank)],
    )
    slot = pipelined_sources(index_ref, count, parts, buffers, sems)
    target = target_ref[0]
    dims = target.shape[-1]
    sources = source_buf[slot].reshape(count * rank, source_buf.shape[-1])
    kernel = scaled_kernel(target, target_square_of(target), sources[:, :dims], norm_buf[slot])
    out_ref[0] = jnp.dot(kernel, sources[:, dims:], preferred_element_type=jnp.float32)


def far_field(leaf_coords, left_rows, own_rows, right_rows, left_norms, own_norms, right_norms, far_local, after):
    leaves, rank, dims = leaf_coords.shape
    width = own_rows.shape[-1]
    count = far_local.shape[1]
    anywhere = pl.BlockSpec(memory_space=pl.ANY)
    return pl.pallas_call(
        far_kernel,
        grid_spec=pltpu.PrefetchScalarGridSpec(
            num_scalar_prefetch=1,
            grid=(leaves,),
            in_specs=[pl.BlockSpec((1, rank, dims), lambda l, index: (l, 0, 0))] + [anywhere] * 7,
            out_specs=pl.BlockSpec((1, rank, width - dims), lambda l, index: (l, 0, 0)),
            scratch_shapes=[
                pltpu.VMEM((2, count, rank, width), own_rows.dtype),
                pltpu.VMEM((2, 1, count * rank), jnp.float32),
                pltpu.SemaphoreType.DMA((2, 2, count)),
            ],
        ),
        out_shape=jax.ShapeDtypeStruct((leaves, rank, width - dims), jnp.float32),
        compiler_params=pltpu.CompilerParams(dimension_semantics=("arbitrary",)),
    )(
        far_local.reshape(-1),
        leaf_coords,
        left_rows,
        own_rows,
        right_rows,
        left_norms,
        own_norms,
        right_norms,
        after,
    )


def final_kernel(rank_ref, basis_ref, down_ref, far_ref, leaf_base_ref, near_ref, out_ref):
    block = basis_ref.shape[0]
    step = pl.program_id(0)
    down = down_ref[...]
    for inside in range(block):
        total = jnp.dot(basis_ref[inside], down, preferred_element_type=jnp.float32) + far_ref[inside]
        rows = lax.broadcasted_iota(jnp.int32, total.shape, 0)
        leaf_down = jnp.where(rows < rank_ref[step * block + inside], total, 0.0).astype(jnp.bfloat16)
        result = (
            jnp.dot(leaf_base_ref[inside], leaf_down, preferred_element_type=jnp.float32)
            + near_ref[inside]
        )
        out_ref[inside] = result.astype(out_ref.dtype)


def final_field(leaf_rank, bases, node_down, far_total, leaf_bases, near_total):
    leaves, rank, width = bases.shape
    size = leaf_bases.shape[1]
    rhs = near_total.shape[-1]
    block = max(b for b in (1, 2, 3, 4) if leaves % b == 0)

    def own(l, ranks):
        return (l, 0, 0)

    return pl.pallas_call(
        final_kernel,
        grid_spec=pltpu.PrefetchScalarGridSpec(
            num_scalar_prefetch=1,
            grid=(leaves // block,),
            in_specs=[
                pl.BlockSpec((block, rank, width), own),
                pl.BlockSpec(node_down.shape, lambda l, ranks: (0, 0)),
                pl.BlockSpec((block, rank, rhs), own),
                pl.BlockSpec((block, size, rank), own),
                pl.BlockSpec((block, size, rhs), own),
            ],
            out_specs=pl.BlockSpec((block, size, rhs), own),
        ),
        out_shape=jax.ShapeDtypeStruct((leaves, size, rhs), jnp.bfloat16),
    )(leaf_rank, bases, node_down, far_total, leaf_bases, near_total)


def select_rows(table, index):
    count = table.shape[0]
    onehot = (index[:, None] == jnp.arange(count, dtype=jnp.int32)[None, :]).astype(table.dtype)
    picked = jnp.dot(onehot, table.reshape(count, -1), preferred_element_type=jnp.float32).astype(
        table.dtype
    )
    return picked.reshape(index.shape + table.shape[1:])


def select_within(table, index):
    count = table.shape[1]
    onehot = (index[:, :, None] == jnp.arange(count, dtype=jnp.int32)[None, None, :]).astype(
        table.dtype
    )
    return jnp.einsum("bkp,bpc->bkc", onehot, table, preferred_element_type=jnp.float32).astype(
        table.dtype
    )


def body(
    points,
    weights,
    leaf_basis,
    leaf_rank,
    leaf_skeleton,
    near_list,
    far_list,
    node_basis,
    node_rank,
    node_skeleton,
    node_far,
    group_basis,
    group_rank,
    group_skeleton,
    group_far,
):
    leaf_count = leaf_rank.shape[0]
    leaf_size = points.shape[0] // leaf_count
    dim_count = points.shape[1]
    rhs_count = weights.shape[1]
    rank_count = leaf_basis.shape[1]
    node_width = node_basis.shape[1]
    group_width = group_basis.shape[1]
    local_points = points.reshape(leaf_count, leaf_size, dim_count)
    local_bases = leaf_basis.reshape(leaf_count, leaf_size, rank_count)
    local_weights = weights.reshape(leaf_count, leaf_size, rhs_count)
    first_leaf = lax.axis_index(FLAT) * leaf_count
    offset = first_leaf - REACH

    left_pairs, right_pairs = halos((points, weights), REACH * leaf_size)
    left_pairs = left_pairs.reshape(REACH, leaf_size, dim_count + rhs_count)
    right_pairs = right_pairs.reshape(REACH, leaf_size, dim_count + rhs_count)

    leaf_mask = (
        lax.broadcasted_iota(jnp.int32, (leaf_count, rank_count), 1) < leaf_rank[:, None]
    ).astype(jnp.float32)
    leaf_up = (
        jnp.einsum("lpk,lpr->lkr", local_bases, local_weights, preferred_element_type=jnp.float32)
        * leaf_mask[:, :, None]
    ).astype(jnp.bfloat16)
    leaf_coords = select_within(local_points, leaf_skeleton)
    own_rows = jnp.concatenate([leaf_coords, leaf_up], axis=-1)
    skeleton_width = dim_count + rhs_count
    left_rows, right_rows = halos(
        (own_rows.reshape(leaf_count * rank_count, skeleton_width),), REACH * rank_count
    )

    node_mask = (jnp.arange(node_width, dtype=jnp.int32) < node_rank[0]).astype(jnp.float32)
    node_up = (
        jnp.einsum(
            "ak,ar->kr",
            node_basis,
            leaf_up.reshape(leaf_count * rank_count, rhs_count),
            preferred_element_type=jnp.float32,
        )
        * node_mask[:, None]
    ).astype(jnp.bfloat16)
    node_coords = select_rows(
        leaf_coords.reshape(leaf_count * rank_count, dim_count), node_skeleton[0]
    )
    columns = lax.axis_size("col")
    source_columns = node_far[0] % columns
    node_pack = jnp.concatenate([node_coords, node_up, group_basis], axis=1)
    gathered = lax.all_gather(node_pack[None], "col", axis=0, tiled=True)

    near_total = near_field(
        local_points,
        local_weights,
        left_pairs,
        right_pairs,
        scaled_norms(local_points),
        scaled_norms(left_pairs[:, :, :dim_count]),
        scaled_norms(right_pairs[:, :, :dim_count]),
        near_list - offset,
    )
    near_total, left_rows, right_rows = lax.optimization_barrier((near_total, left_rows, right_rows))

    all_coords = gathered[:, :, :dim_count]
    all_up = gathered[:, :, dim_count : dim_count + rhs_count]
    all_parts = gathered[:, :, dim_count + rhs_count :]
    picked_coords = select_rows(all_coords, source_columns)
    picked_up = select_rows(all_up, source_columns)
    kernel = kernel_block(jnp.broadcast_to(node_coords, picked_coords.shape), picked_coords)
    node_side = jnp.einsum("fab,fbr->ar", kernel, picked_up, preferred_element_type=jnp.float32)
    group_mask = (jnp.arange(group_width, dtype=jnp.int32) < group_rank[0]).astype(jnp.float32)
    group_up = (
        jnp.einsum("nag,nar->gr", all_parts, all_up, preferred_element_type=jnp.float32)
        * group_mask[:, None]
    ).astype(jnp.bfloat16)
    group_coords = select_rows(all_coords.reshape(columns * node_width, dim_count), group_skeleton[0])
    group_pack = jnp.concatenate([group_coords, group_up], axis=1)
    left_rows = left_rows.reshape(REACH, rank_count, skeleton_width)
    right_rows = right_rows.reshape(REACH, rank_count, skeleton_width)
    far_total = far_field(
        leaf_coords,
        left_rows,
        own_rows,
        right_rows,
        scaled_norms(left_rows[:, :, :dim_count]),
        scaled_norms(leaf_coords),
        scaled_norms(right_rows[:, :, :dim_count]),
        far_list - offset,
        group_pack,
    )
    rows = lax.axis_size("row")
    received = [group_pack] + [
        lax.ppermute(group_pack, "row", [(r, (r + shift) % rows) for r in range(rows)])
        for shift in range(1, rows)
    ]
    shifts = (lax.axis_index("row") - group_far[0]) % rows
    picked_group = select_rows(jnp.stack(received), shifts)
    picked_group_coords = picked_group[:, :, :dim_count]
    picked_group_up = picked_group[:, :, dim_count:]
    group_kernel = kernel_block(
        jnp.broadcast_to(group_coords, picked_group_coords.shape), picked_group_coords
    )
    group_down = (
        jnp.einsum("fab,fbr->ar", group_kernel, picked_group_up, preferred_element_type=jnp.float32)
        * group_mask[:, None]
    ).astype(jnp.bfloat16)
    node_down = (
        (jnp.dot(group_basis, group_down, preferred_element_type=jnp.float32) + node_side)
        * node_mask[:, None]
    ).astype(jnp.bfloat16)
    result = final_field(
        leaf_rank,
        node_basis.reshape(leaf_count, rank_count, node_width),
        node_down,
        far_total,
        local_bases,
        near_total,
    )
    return result.reshape(leaf_count * leaf_size, rhs_count)


def solution(mesh):
    in_specs = (
        P(FLAT, None),
        P(FLAT, None),
        P(FLAT, None),
        P(FLAT),
        P(FLAT, None),
        P(FLAT, None),
        P(FLAT, None),
        P(FLAT, None),
        P(FLAT),
        P(FLAT, None),
        P(FLAT, None),
        P(FLAT, None),
        P("row"),
        P("row", None),
        P("row", None),
    )
    out_specs = P(FLAT, None)
    return jax.shard_map(body, mesh=mesh, in_specs=in_specs, out_specs=out_specs, check_vma=False)
```

```python
import jax
import jax.numpy as jnp
from jax import lax
from jax.experimental import pallas as pl
from jax.experimental.pallas import tpu as pltpu
from jax.sharding import PartitionSpec as P

REACH = 8
FLAT = ("row", "col")


def halos(cells, width):
    count = lax.axis_size(FLAT)
    ends = count - 1
    head = jnp.concatenate([cell[:width] for cell in cells], axis=1)
    tail = jnp.concatenate([cell[cell.shape[0] - width :] for cell in cells], axis=1)
    left = lax.ppermute(tail, FLAT, [(i, i + 1) for i in range(ends)])
    right = lax.ppermute(head, FLAT, [(i + 1, i) for i in range(ends)])
    return left, right


def kernel_block(left, right):
    left_square = jnp.sum(jnp.square(left.astype(jnp.float32)), axis=-1)
    right_square = jnp.sum(jnp.square(right.astype(jnp.float32)), axis=-1)
    inner = jnp.einsum("...md,...nd->...mn", left, right, preferred_element_type=jnp.float32)
    distance = left_square[..., :, None] + right_square[..., None, :] - 2.0 * inner
    return jnp.exp(distance * (-2.0 / left.shape[-1])).astype(jnp.bfloat16)


def contract_last(a, b):
    return lax.dot_general(a, b, (((1,), (1,)), ((), ())), preferred_element_type=jnp.float32)


def scaled_kernel(target, target_square, source, source_square):
    dims = target.shape[-1]
    inner = contract_last(target * jnp.asarray(4.0 / dims, target.dtype), source)
    return jnp.exp((target_square + source_square) + inner).astype(jnp.bfloat16)


def scaled_norms(cells):
    wide = cells.astype(jnp.float32)
    return (jnp.sum(wide * wide, axis=-1) * (-2.0 / cells.shape[-1]))[:, None, :]


def target_square_of(target):
    wide = target.astype(jnp.float32)
    return jnp.sum(wide * wide, axis=-1, keepdims=True) * (-2.0 / target.shape[-1])


def fetch_sources(index_ref, row, count, parts, buffers, sems, slot):
    for position in range(count):
        source = index_ref[row * count + position]
        for which, (halo, mine, left, own, right) in enumerate(parts):
            target = buffers[which](slot, position)
            sem = sems.at[which, slot, position]
            if left is None:
                pltpu.make_async_copy(own(source - halo), target, sem).start()
                continue

            @pl.when(source < halo)
            def _():
                pltpu.make_async_copy(left(source), target, sem).start()

            @pl.when((source >= halo) & (source < halo + mine))
            def _():
                pltpu.make_async_copy(own(source - halo), target, sem).start()

            @pl.when(source >= halo + mine)
            def _():
                pltpu.make_async_copy(right(source - halo - mine), target, sem).start()


def wait_sources(count, parts, buffers, sems, slot):
    for position in range(count):
        for which, (halo, mine, left, own, right) in enumerate(parts):
            pltpu.make_async_copy(
                own(0), buffers[which](slot, position), sems.at[which, slot, position]
            ).wait()


def rows_of(ref):
    return lambda index: ref.at[index]


def whole_rows(left, own, right):
    return (left.shape[0], own.shape[0], rows_of(left), rows_of(own), rows_of(right))


def own_rows_only(own):
    return (REACH, own.shape[0], None, rows_of(own), None)


def lane_rows(left, own, right, start, width):
    def halo_at(ref):
        return lambda index: ref.at[index, :, pl.ds(start, width)]

    return (left.shape[0], own.shape[0], halo_at(left), rows_of(own), halo_at(right))


def pipelined_sources(index_ref, count, parts, buffers, sems, leaf_of):
    step = pl.program_id(0)
    steps = pl.num_programs(0)
    slot = step % 2

    @pl.when(step == 0)
    def _():
        fetch_sources(index_ref, leaf_of(0), count, parts, buffers, sems, 0)

    @pl.when(step + 1 < steps)
    def _():
        fetch_sources(index_ref, leaf_of(step + 1), count, parts, buffers, sems, 1 - slot)

    wait_sources(count, parts, buffers, sems, slot)
    return slot


def leaf_order(leaves, edges):
    low, high = REACH, leaves - REACH
    if high <= low:
        return (lambda step: step), leaves, None
    if not edges:
        return (lambda step: step + low), high - low, None
    gap = high - low
    return (lambda step: step + gap * jnp.asarray(step >= low, jnp.int32)), leaves - gap, gap


def near_kernel(leaf_of, halo, index_ref, target_ref, *refs):
    inputs = 8 if halo else 3
    out_ref = refs[inputs]
    point_buf, weight_buf, norm_buf, sems = refs[inputs + 1 :]
    count, size, dims = point_buf.shape[1], point_buf.shape[2], point_buf.shape[3]
    if halo:
        lpw, op, rpw, ow, ln, on, rn = refs[:7]
        parts = (
            lane_rows(lpw, op, rpw, 0, dims),
            lane_rows(lpw, ow, rpw, dims, weight_buf.shape[-1]),
            whole_rows(ln, on, rn),
        )
    else:
        parts = tuple(own_rows_only(ref) for ref in refs[:3])
    buffers = (
        lambda slot, position: point_buf.at[slot, position],
        lambda slot, position: weight_buf.at[slot, position],
        lambda slot, position: norm_buf.at[slot, :, pl.ds(position * size, size)],
    )
    slot = pipelined_sources(index_ref, count, parts, buffers, sems, leaf_of)
    target = target_ref[0]
    sources = point_buf[slot].reshape(count * size, dims)
    values = weight_buf[slot].reshape(count * size, weight_buf.shape[-1])
    kernel = scaled_kernel(target, target_square_of(target), sources, norm_buf[slot])
    out_ref[0] = jnp.dot(kernel, values, preferred_element_type=jnp.float32)


def near_field(local_points, local_weights, local_norms, near_local, halo_inputs=None, previous=None):
    leaves, size, dims = local_points.shape
    rhs = local_weights.shape[-1]
    count = near_local.shape[1]
    halo = halo_inputs is not None
    leaf_of, steps, gap = leaf_order(leaves, halo)
    anywhere = pl.BlockSpec(memory_space=pl.ANY)
    if halo:
        left_pairs, right_pairs, left_norms, right_norms = halo_inputs
        inputs = (left_pairs, local_points, right_pairs, local_weights, left_norms, local_norms, right_norms, previous)
    else:
        inputs = (local_points, local_weights, local_norms)
    aliases = {len(inputs) + 1: 0} if previous is not None else {}
    by_leaf = lambda step, index: (leaf_of(step), 0, 0)
    return pl.pallas_call(
        lambda *refs: near_kernel(leaf_of, halo, *refs),
        grid_spec=pltpu.PrefetchScalarGridSpec(
            num_scalar_prefetch=1,
            grid=(steps,),
            in_specs=[pl.BlockSpec((1, size, dims), by_leaf)] + [anywhere] * len(inputs),
            out_specs=pl.BlockSpec((1, size, rhs), by_leaf),
            scratch_shapes=[
                pltpu.VMEM((2, count, size, dims), local_points.dtype),
                pltpu.VMEM((2, count, size, rhs), local_weights.dtype),
                pltpu.VMEM((2, 1, count * size), jnp.float32),
                pltpu.SemaphoreType.DMA((3, 2, count)),
            ],
        ),
        out_shape=jax.ShapeDtypeStruct((leaves, size, rhs), jnp.float32),
        input_output_aliases=aliases,
        compiler_params=pltpu.CompilerParams(dimension_semantics=("arbitrary",)),
    )(near_local.reshape(-1), local_points, *inputs)


def far_kernel(leaf_of, halo, index_ref, target_ref, *refs):
    inputs = 8 if halo else 2
    out_ref = refs[inputs]
    source_buf, norm_buf, sems = refs[inputs + 1 :]
    count, rank = source_buf.shape[1], source_buf.shape[2]
    if halo:
        ls, os, rs, ln, on, rn = refs[:6]
        parts = (whole_rows(ls, os, rs), whole_rows(ln, on, rn))
    else:
        parts = tuple(own_rows_only(ref) for ref in refs[:2])
    buffers = (
        lambda slot, position: source_buf.at[slot, position],
        lambda slot, position: norm_buf.at[slot, :, pl.ds(position * rank, rank)],
    )
    slot = pipelined_sources(index_ref, count, parts, buffers, sems, leaf_of)
    target = target_ref[0]
    dims = target.shape[-1]
    sources = source_buf[slot].reshape(count * rank, source_buf.shape[-1])
    kernel = scaled_kernel(target, target_square_of(target), sources[:, :dims], norm_buf[slot])
    out_ref[0] = jnp.dot(kernel, sources[:, dims:], preferred_element_type=jnp.float32)


def far_field(leaf_coords, own_rows, own_norms, far_local, halo_inputs=None, previous=None, after=None):
    leaves, rank, dims = leaf_coords.shape
    width = own_rows.shape[-1]
    count = far_local.shape[1]
    halo = halo_inputs is not None
    leaf_of, steps, gap = leaf_order(leaves, halo)
    anywhere = pl.BlockSpec(memory_space=pl.ANY)
    if halo:
        left_rows, right_rows, left_norms, right_norms = halo_inputs
        inputs = (left_rows, own_rows, right_rows, left_norms, own_norms, right_norms, after, previous)
    else:
        inputs = (own_rows, own_norms)
    aliases = {len(inputs) + 1: 0} if previous is not None else {}
    by_leaf = lambda step, index: (leaf_of(step), 0, 0)
    return pl.pallas_call(
        lambda *refs: far_kernel(leaf_of, halo, *refs),
        grid_spec=pltpu.PrefetchScalarGridSpec(
            num_scalar_prefetch=1,
            grid=(steps,),
            in_specs=[pl.BlockSpec((1, rank, dims), by_leaf)] + [anywhere] * len(inputs),
            out_specs=pl.BlockSpec((1, rank, width - dims), by_leaf),
            scratch_shapes=[
                pltpu.VMEM((2, count, rank, width), own_rows.dtype),
                pltpu.VMEM((2, 1, count * rank), jnp.float32),
                pltpu.SemaphoreType.DMA((2, 2, count)),
            ],
        ),
        out_shape=jax.ShapeDtypeStruct((leaves, rank, width - dims), jnp.float32),
        input_output_aliases=aliases,
        compiler_params=pltpu.CompilerParams(dimension_semantics=("arbitrary",)),
    )(far_local.reshape(-1), leaf_coords, *inputs)


def final_kernel(rank_ref, basis_ref, down_ref, far_ref, leaf_base_ref, near_ref, out_ref):
    block = basis_ref.shape[0]
    step = pl.program_id(0)
    down = down_ref[...]
    for inside in range(block):
        total = jnp.dot(basis_ref[inside], down, preferred_element_type=jnp.float32) + far_ref[inside]
        rows = lax.broadcasted_iota(jnp.int32, total.shape, 0)
        leaf_down = jnp.where(rows < rank_ref[step * block + inside], total, 0.0).astype(jnp.bfloat16)
        result = (
            jnp.dot(leaf_base_ref[inside], leaf_down, preferred_element_type=jnp.float32)
            + near_ref[inside]
        )
        out_ref[inside] = result.astype(out_ref.dtype)


def final_field(leaf_rank, bases, node_down, far_total, leaf_bases, near_total):
    leaves, rank, width = bases.shape
    size = leaf_bases.shape[1]
    rhs = near_total.shape[-1]
    block = max(b for b in (1, 2, 3, 4) if leaves % b == 0)

    def own(l, ranks):
        return (l, 0, 0)

    return pl.pallas_call(
        final_kernel,
        grid_spec=pltpu.PrefetchScalarGridSpec(
            num_scalar_prefetch=1,
            grid=(leaves // block,),
            in_specs=[
                pl.BlockSpec((block, rank, width), own),
                pl.BlockSpec(node_down.shape, lambda l, ranks: (0, 0)),
                pl.BlockSpec((block, rank, rhs), own),
                pl.BlockSpec((block, size, rank), own),
                pl.BlockSpec((block, size, rhs), own),
            ],
            out_specs=pl.BlockSpec((block, size, rhs), own),
        ),
        out_shape=jax.ShapeDtypeStruct((leaves, size, rhs), jnp.bfloat16),
    )(leaf_rank, bases, node_down, far_total, leaf_bases, near_total)


def select_rows(table, index):
    count = table.shape[0]
    onehot = (index[:, None] == jnp.arange(count, dtype=jnp.int32)[None, :]).astype(table.dtype)
    picked = jnp.dot(onehot, table.reshape(count, -1), preferred_element_type=jnp.float32).astype(
        table.dtype
    )
    return picked.reshape(index.shape + table.shape[1:])


def select_within(table, index):
    count = table.shape[1]
    onehot = (index[:, :, None] == jnp.arange(count, dtype=jnp.int32)[None, None, :]).astype(
        table.dtype
    )
    return jnp.einsum("bkp,bpc->bkc", onehot, table, preferred_element_type=jnp.float32).astype(
        table.dtype
    )


def body(
    points,
    weights,
    leaf_basis,
    leaf_rank,
    leaf_skeleton,
    near_list,
    far_list,
    node_basis,
    node_rank,
    node_skeleton,
    node_far,
    group_basis,
    group_rank,
    group_skeleton,
    group_far,
):
    leaf_count = leaf_rank.shape[0]
    leaf_size = points.shape[0] // leaf_count
    dim_count = points.shape[1]
    rhs_count = weights.shape[1]
    rank_count = leaf_basis.shape[1]
    node_width = node_basis.shape[1]
    group_width = group_basis.shape[1]
    local_points = points.reshape(leaf_count, leaf_size, dim_count)
    local_bases = leaf_basis.reshape(leaf_count, leaf_size, rank_count)
    local_weights = weights.reshape(leaf_count, leaf_size, rhs_count)
    first_leaf = lax.axis_index(FLAT) * leaf_count
    offset = first_leaf - REACH

    left_pairs, right_pairs = halos((points, weights), REACH * leaf_size)
    left_pairs = left_pairs.reshape(REACH, leaf_size, dim_count + rhs_count)
    right_pairs = right_pairs.reshape(REACH, leaf_size, dim_count + rhs_count)

    leaf_mask = (
        lax.broadcasted_iota(jnp.int32, (leaf_count, rank_count), 1) < leaf_rank[:, None]
    ).astype(jnp.float32)
    leaf_up = (
        jnp.einsum("lpk,lpr->lkr", local_bases, local_weights, preferred_element_type=jnp.float32)
        * leaf_mask[:, :, None]
    ).astype(jnp.bfloat16)
    leaf_coords = select_within(local_points, leaf_skeleton)
    own_rows = jnp.concatenate([leaf_coords, leaf_up], axis=-1)
    skeleton_width = dim_count + rhs_count
    left_rows, right_rows = halos(
        (own_rows.reshape(leaf_count * rank_count, skeleton_width),), REACH * rank_count
    )

    node_mask = (jnp.arange(node_width, dtype=jnp.int32) < node_rank[0]).astype(jnp.float32)
    node_up = (
        jnp.einsum(
            "ak,ar->kr",
            node_basis,
            leaf_up.reshape(leaf_count * rank_count, rhs_count),
            preferred_element_type=jnp.float32,
        )
        * node_mask[:, None]
    ).astype(jnp.bfloat16)
    node_coords = select_rows(
        leaf_coords.reshape(leaf_count * rank_count, dim_count), node_skeleton[0]
    )
    columns = lax.axis_size("col")
    source_columns = node_far[0] % columns
    node_pack = jnp.concatenate([node_coords, node_up, group_basis], axis=1)
    gathered = lax.all_gather(node_pack[None], "col", axis=0, tiled=True)

    near_local = near_list - offset
    local_norms = scaled_norms(local_points)
    near_inner = near_field(local_points, local_weights, local_norms, near_local)
    near_total = near_field(
        local_points,
        local_weights,
        local_norms,
        near_local,
        (
            left_pairs,
            right_pairs,
            scaled_norms(left_pairs[:, :, :dim_count]),
            scaled_norms(right_pairs[:, :, :dim_count]),
        ),
        near_inner,
    )
    near_total, left_rows, right_rows = lax.optimization_barrier((near_total, left_rows, right_rows))

    all_coords = gathered[:, :, :dim_count]
    all_up = gathered[:, :, dim_count : dim_count + rhs_count]
    all_parts = gathered[:, :, dim_count + rhs_count :]
    picked_coords = select_rows(all_coords, source_columns)
    picked_up = select_rows(all_up, source_columns)
    kernel = kernel_block(jnp.broadcast_to(node_coords, picked_coords.shape), picked_coords)
    node_side = jnp.einsum("fab,fbr->ar", kernel, picked_up, preferred_element_type=jnp.float32)
    group_mask = (jnp.arange(group_width, dtype=jnp.int32) < group_rank[0]).astype(jnp.float32)
    group_up = (
        jnp.einsum("nag,nar->gr", all_parts, all_up, preferred_element_type=jnp.float32)
        * group_mask[:, None]
    ).astype(jnp.bfloat16)
    group_coords = select_rows(all_coords.reshape(columns * node_width, dim_count), group_skeleton[0])
    group_pack = jnp.concatenate([group_coords, group_up], axis=1)
    left_rows = left_rows.reshape(REACH, rank_count, skeleton_width)
    right_rows = right_rows.reshape(REACH, rank_count, skeleton_width)
    far_local = far_list - offset
    coord_norms = scaled_norms(leaf_coords)
    far_inner = far_field(leaf_coords, own_rows, coord_norms, far_local)
    far_total = far_field(
        leaf_coords,
        own_rows,
        coord_norms,
        far_local,
        (
            left_rows,
            right_rows,
            scaled_norms(left_rows[:, :, :dim_count]),
            scaled_norms(right_rows[:, :, :dim_count]),
        ),
        far_inner,
        group_pack,
    )
    rows = lax.axis_size("row")
    received = [group_pack] + [
        lax.ppermute(group_pack, "row", [(r, (r + shift) % rows) for r in range(rows)])
        for shift in range(1, rows)
    ]
    shifts = (lax.axis_index("row") - group_far[0]) % rows
    picked_group = select_rows(jnp.stack(received), shifts)
    picked_group_coords = picked_group[:, :, :dim_count]
    picked_group_up = picked_group[:, :, dim_count:]
    group_kernel = kernel_block(
        jnp.broadcast_to(group_coords, picked_group_coords.shape), picked_group_coords
    )
    group_down = (
        jnp.einsum("fab,fbr->ar", group_kernel, picked_group_up, preferred_element_type=jnp.float32)
        * group_mask[:, None]
    ).astype(jnp.bfloat16)
    node_down = (
        (jnp.dot(group_basis, group_down, preferred_element_type=jnp.float32) + node_side)
        * node_mask[:, None]
    ).astype(jnp.bfloat16)
    result = final_field(
        leaf_rank,
        node_basis.reshape(leaf_count, rank_count, node_width),
        node_down,
        far_total,
        local_bases,
        near_total,
    )
    return result.reshape(leaf_count * leaf_size, rhs_count)


def solution(mesh):
    in_specs = (
        P(FLAT, None),
        P(FLAT, None),
        P(FLAT, None),
        P(FLAT),
        P(FLAT, None),
        P(FLAT, None),
        P(FLAT, None),
        P(FLAT, None),
        P(FLAT),
        P(FLAT, None),
        P(FLAT, None),
        P(FLAT, None),
        P("row"),
        P("row", None),
        P("row", None),
    )
    out_specs = P(FLAT, None)
    return jax.shard_map(body, mesh=mesh, in_specs=in_specs, out_specs=out_specs, check_vma=False)
```

```python
import jax
import jax.numpy as jnp
from jax import lax
from jax.experimental import pallas as pl
from jax.experimental.pallas import tpu as pltpu
from jax.sharding import PartitionSpec as P


REACH = 8
FLAT = ("row", "col")


def halos(cells, width):
    count = lax.axis_size(FLAT)
    ends = count - 1
    head = jnp.concatenate([cell[:width] for cell in cells], axis=1)
    tail = jnp.concatenate([cell[cell.shape[0] - width :] for cell in cells], axis=1)
    left = lax.ppermute(tail, FLAT, [(i, i + 1) for i in range(ends)])
    right = lax.ppermute(head, FLAT, [(i + 1, i) for i in range(ends)])
    return left, right


def kernel_block(left, right):
    left_square = jnp.sum(jnp.square(left.astype(jnp.float32)), axis=-1)
    right_square = jnp.sum(jnp.square(right.astype(jnp.float32)), axis=-1)
    inner = jnp.einsum("...md,...nd->...mn", left, right, preferred_element_type=jnp.float32)
    distance = left_square[..., :, None] + right_square[..., None, :] - 2.0 * inner
    return jnp.exp(distance * (-2.0 / left.shape[-1])).astype(jnp.bfloat16)


def contract_last(a, b):
    return lax.dot_general(a, b, (((1,), (1,)), ((), ())), preferred_element_type=jnp.float32)


def scaled_kernel(target, target_square, source, source_square):
    dims = target.shape[-1]
    inner = contract_last(target * jnp.asarray(4.0 / dims, target.dtype), source)
    return jnp.exp((target_square + source_square) + inner).astype(jnp.bfloat16)


def scaled_norms(cells):
    wide = cells.astype(jnp.float32)
    return (jnp.sum(wide * wide, axis=-1) * (-2.0 / cells.shape[-1]))[:, None, :]


def target_square_of(target):
    wide = target.astype(jnp.float32)
    return jnp.sum(wide * wide, axis=-1, keepdims=True) * (-2.0 / target.shape[-1])


def fetch_sources(index_ref, row, count, parts, buffers, sems, slot):
    for position in range(count):
        source = index_ref[row * count + position]
        for which, (halo, mine, left, own, right) in enumerate(parts):
            target = buffers[which](slot, position)
            sem = sems.at[which, slot, position]
            if left is None:
                pltpu.make_async_copy(own(source - halo), target, sem).start()
                continue

            @pl.when(source < halo)
            def _():
                pltpu.make_async_copy(left(source), target, sem).start()

            @pl.when((source >= halo) & (source < halo + mine))
            def _():
                pltpu.make_async_copy(own(source - halo), target, sem).start()

            @pl.when(source >= halo + mine)
            def _():
                pltpu.make_async_copy(right(source - halo - mine), target, sem).start()


def wait_sources(count, parts, buffers, sems, slot):
    for position in range(count):
        for which, (halo, mine, left, own, right) in enumerate(parts):
            pltpu.make_async_copy(
                own(0), buffers[which](slot, position), sems.at[which, slot, position]
            ).wait()


def rows_of(ref):
    return lambda index: ref.at[index]


def whole_rows(left, own, right):
    return (left.shape[0], own.shape[0], rows_of(left), rows_of(own), rows_of(right))


def own_rows_only(own):
    return (REACH, own.shape[0], None, rows_of(own), None)


def lane_rows(left, own, right, start, width):
    def halo_at(ref):
        return lambda index: ref.at[index, :, pl.ds(start, width)]

    return (left.shape[0], own.shape[0], halo_at(left), rows_of(own), halo_at(right))


def pipelined_sources(index_ref, count, parts, buffers, sems, leaf_of):
    step = pl.program_id(0)
    steps = pl.num_programs(0)
    slot = step % 2

    @pl.when(step == 0)
    def _():
        fetch_sources(index_ref, leaf_of(0), count, parts, buffers, sems, 0)

    @pl.when(step + 1 < steps)
    def _():
        fetch_sources(index_ref, leaf_of(step + 1), count, parts, buffers, sems, 1 - slot)

    wait_sources(count, parts, buffers, sems, slot)
    return slot


def leaf_order(leaves, edges):
    low, high = REACH, leaves - REACH
    if high <= low:
        return (lambda step: step), leaves, None
    if not edges:
        return (lambda step: step + low), high - low, None
    gap = high - low
    return (lambda step: step + gap * jnp.asarray(step >= low, jnp.int32)), leaves - gap, gap


def near_kernel(leaf_of, halo, index_ref, target_ref, *refs):
    inputs = 8 if halo else 3
    out_ref = refs[inputs]
    point_buf, weight_buf, norm_buf, sems = refs[inputs + 1 :]
    count, size, dims = point_buf.shape[1], point_buf.shape[2], point_buf.shape[3]
    if halo:
        lpw, op, rpw, ow, ln, on, rn = refs[:7]
        parts = (
            lane_rows(lpw, op, rpw, 0, dims),
            lane_rows(lpw, ow, rpw, dims, weight_buf.shape[-1]),
            whole_rows(ln, on, rn),
        )
    else:
        parts = tuple(own_rows_only(ref) for ref in refs[:3])
    buffers = (
        lambda slot, position: point_buf.at[slot, position],
        lambda slot, position: weight_buf.at[slot, position],
        lambda slot, position: norm_buf.at[slot, :, pl.ds(position * size, size)],
    )
    slot = pipelined_sources(index_ref, count, parts, buffers, sems, leaf_of)
    target = target_ref[0]
    sources = point_buf[slot].reshape(count * size, dims)
    values = weight_buf[slot].reshape(count * size, weight_buf.shape[-1])
    kernel = scaled_kernel(target, target_square_of(target), sources, norm_buf[slot])
    out_ref[0] = jnp.dot(kernel, values, preferred_element_type=jnp.float32)


def near_field(local_points, local_weights, local_norms, near_local, halo_inputs=None, previous=None):
    leaves, size, dims = local_points.shape
    rhs = local_weights.shape[-1]
    count = near_local.shape[1]
    halo = halo_inputs is not None
    leaf_of, steps, _ = leaf_order(leaves, halo)
    anywhere = pl.BlockSpec(memory_space=pl.ANY)
    if halo:
        left_pairs, right_pairs, left_norms, right_norms = halo_inputs
        inputs = (left_pairs, local_points, right_pairs, local_weights, left_norms, local_norms, right_norms, previous)
    else:
        inputs = (local_points, local_weights, local_norms)
    aliases = {len(inputs) + 1: 0} if previous is not None else {}
    by_leaf = lambda step, index: (leaf_of(step), 0, 0)
    return pl.pallas_call(
        lambda *refs: near_kernel(leaf_of, halo, *refs),
        grid_spec=pltpu.PrefetchScalarGridSpec(
            num_scalar_prefetch=1,
            grid=(steps,),
            in_specs=[pl.BlockSpec((1, size, dims), by_leaf)] + [anywhere] * len(inputs),
            out_specs=pl.BlockSpec((1, size, rhs), by_leaf),
            scratch_shapes=[
                pltpu.VMEM((2, count, size, dims), local_points.dtype),
                pltpu.VMEM((2, count, size, rhs), local_weights.dtype),
                pltpu.VMEM((2, 1, count * size), jnp.float32),
                pltpu.SemaphoreType.DMA((3, 2, count)),
            ],
        ),
        out_shape=jax.ShapeDtypeStruct((leaves, size, rhs), jnp.float32),
        input_output_aliases=aliases,
        compiler_params=pltpu.CompilerParams(dimension_semantics=("arbitrary",)),
    )(near_local.reshape(-1), local_points, *inputs)


def far_kernel(leaf_of, halo, index_ref, target_ref, *refs):
    inputs = 8 if halo else 2
    out_ref = refs[inputs]
    source_buf, norm_buf, sems = refs[inputs + 1 :]
    count, rank = source_buf.shape[1], source_buf.shape[2]
    if halo:
        ls, os, rs, ln, on, rn = refs[:6]
        parts = (whole_rows(ls, os, rs), whole_rows(ln, on, rn))
    else:
        parts = tuple(own_rows_only(ref) for ref in refs[:2])
    buffers = (
        lambda slot, position: source_buf.at[slot, position],
        lambda slot, position: norm_buf.at[slot, :, pl.ds(position * rank, rank)],
    )
    slot = pipelined_sources(index_ref, count, parts, buffers, sems, leaf_of)
    target = target_ref[0]
    dims = target.shape[-1]
    sources = source_buf[slot].reshape(count * rank, source_buf.shape[-1])
    kernel = scaled_kernel(target, target_square_of(target), sources[:, :dims], norm_buf[slot])
    out_ref[0] = jnp.dot(kernel, sources[:, dims:], preferred_element_type=jnp.float32)


def far_field(leaf_coords, own_rows, own_norms, far_local, halo_inputs=None, previous=None, after=None):
    leaves, rank, dims = leaf_coords.shape
    width = own_rows.shape[-1]
    count = far_local.shape[1]
    halo = halo_inputs is not None
    leaf_of, steps, _ = leaf_order(leaves, halo)
    anywhere = pl.BlockSpec(memory_space=pl.ANY)
    if halo:
        left_rows, right_rows, left_norms, right_norms = halo_inputs
        inputs = (left_rows, own_rows, right_rows, left_norms, own_norms, right_norms, after, previous)
    else:
        inputs = (own_rows, own_norms)
    aliases = {len(inputs) + 1: 0} if previous is not None else {}
    by_leaf = lambda step, index: (leaf_of(step), 0, 0)
    return pl.pallas_call(
        lambda *refs: far_kernel(leaf_of, halo, *refs),
        grid_spec=pltpu.PrefetchScalarGridSpec(
            num_scalar_prefetch=1,
            grid=(steps,),
            in_specs=[pl.BlockSpec((1, rank, dims), by_leaf)] + [anywhere] * len(inputs),
            out_specs=pl.BlockSpec((1, rank, width - dims), by_leaf),
            scratch_shapes=[
                pltpu.VMEM((2, count, rank, width), own_rows.dtype),
                pltpu.VMEM((2, 1, count * rank), jnp.float32),
                pltpu.SemaphoreType.DMA((2, 2, count)),
            ],
        ),
        out_shape=jax.ShapeDtypeStruct((leaves, rank, width - dims), jnp.float32),
        input_output_aliases=aliases,
        compiler_params=pltpu.CompilerParams(dimension_semantics=("arbitrary",)),
    )(far_local.reshape(-1), leaf_coords, *inputs)


def final_kernel(rank_ref, basis_ref, down_ref, far_ref, leaf_base_ref, near_ref, out_ref):
    block = basis_ref.shape[0]
    step = pl.program_id(0)
    down = down_ref[...]
    for inside in range(block):
        total = jnp.dot(basis_ref[inside], down, preferred_element_type=jnp.float32) + far_ref[inside]
        rows = lax.broadcasted_iota(jnp.int32, total.shape, 0)
        leaf_down = jnp.where(rows < rank_ref[step * block + inside], total, 0.0).astype(jnp.bfloat16)
        result = (
            jnp.dot(leaf_base_ref[inside], leaf_down, preferred_element_type=jnp.float32)
            + near_ref[inside]
        )
        out_ref[inside] = result.astype(out_ref.dtype)


def final_field(leaf_rank, bases, node_down, far_total, leaf_bases, near_total):
    leaves, rank, width = bases.shape
    size = leaf_bases.shape[1]
    rhs = near_total.shape[-1]
    block = max(b for b in (1, 2, 3, 4) if leaves % b == 0)

    def own(l, ranks):
        return (l, 0, 0)

    return pl.pallas_call(
        final_kernel,
        grid_spec=pltpu.PrefetchScalarGridSpec(
            num_scalar_prefetch=1,
            grid=(leaves // block,),
            in_specs=[
                pl.BlockSpec((block, rank, width), own),
                pl.BlockSpec(node_down.shape, lambda l, ranks: (0, 0)),
                pl.BlockSpec((block, rank, rhs), own),
                pl.BlockSpec((block, size, rank), own),
                pl.BlockSpec((block, size, rhs), own),
            ],
            out_specs=pl.BlockSpec((block, size, rhs), own),
        ),
        out_shape=jax.ShapeDtypeStruct((leaves, size, rhs), jnp.bfloat16),
    )(leaf_rank, bases, node_down, far_total, leaf_bases, near_total)


def select_rows(table, index):
    count = table.shape[0]
    onehot = (index[:, None] == jnp.arange(count, dtype=jnp.int32)[None, :]).astype(table.dtype)
    picked = jnp.dot(onehot, table.reshape(count, -1), preferred_element_type=jnp.float32).astype(
        table.dtype
    )
    return picked.reshape(index.shape + table.shape[1:])


def select_within(table, index):
    count = table.shape[1]
    onehot = (index[:, :, None] == jnp.arange(count, dtype=jnp.int32)[None, None, :]).astype(
        table.dtype
    )
    return jnp.einsum("bkp,bpc->bkc", onehot, table, preferred_element_type=jnp.float32).astype(
        table.dtype
    )


def body(
    points,
    weights,
    leaf_basis,
    leaf_rank,
    leaf_skeleton,
    near_list,
    far_list,
    node_basis,
    node_rank,
    node_skeleton,
    node_far,
    group_basis,
    group_rank,
    group_skeleton,
    group_far,
):
    leaf_count = leaf_rank.shape[0]
    leaf_size = points.shape[0] // leaf_count
    dim_count = points.shape[1]
    rhs_count = weights.shape[1]
    rank_count = leaf_basis.shape[1]
    node_width = node_basis.shape[1]
    group_width = group_basis.shape[1]
    local_points = points.reshape(leaf_count, leaf_size, dim_count)
    local_bases = leaf_basis.reshape(leaf_count, leaf_size, rank_count)
    local_weights = weights.reshape(leaf_count, leaf_size, rhs_count)
    first_leaf = lax.axis_index(FLAT) * leaf_count
    offset = first_leaf - REACH

    left_pairs, right_pairs = halos((points, weights), REACH * leaf_size)
    left_pairs = left_pairs.reshape(REACH, leaf_size, dim_count + rhs_count)
    right_pairs = right_pairs.reshape(REACH, leaf_size, dim_count + rhs_count)

    leaf_mask = (lax.broadcasted_iota(jnp.int32, (leaf_count, rank_count), 1) < leaf_rank[:, None]).astype(jnp.float32)
    leaf_up = (
        jnp.einsum("lpk,lpr->lkr", local_bases, local_weights, preferred_element_type=jnp.float32)
        * leaf_mask[:, :, None]
    ).astype(jnp.bfloat16)
    leaf_coords = select_within(local_points, leaf_skeleton)
    own_rows = jnp.concatenate([leaf_coords, leaf_up], axis=-1)
    skeleton_width = dim_count + rhs_count
    left_rows, right_rows = halos(
        (own_rows.reshape(leaf_count * rank_count, skeleton_width),), REACH * rank_count
    )

    node_mask = (jnp.arange(node_width, dtype=jnp.int32) < node_rank[0]).astype(jnp.float32)
    node_up = (
        jnp.einsum(
            "ak,ar->kr",
            node_basis,
            leaf_up.reshape(leaf_count * rank_count, rhs_count),
            preferred_element_type=jnp.float32,
        )
        * node_mask[:, None]
    ).astype(jnp.bfloat16)
    node_coords = select_rows(
        leaf_coords.reshape(leaf_count * rank_count, dim_count), node_skeleton[0]
    )
    columns = lax.axis_size("col")
    source_columns = node_far[0] % columns
    node_pack = jnp.concatenate([node_coords, node_up, group_basis], axis=1)
    gathered = lax.all_gather(node_pack[None], "col", axis=0, tiled=True)

    near_local = near_list - offset
    local_norms = scaled_norms(local_points)
    near_inner = near_field(local_points, local_weights, local_norms, near_local)
    near_total = near_field(
        local_points,
        local_weights,
        local_norms,
        near_local,
        (
            left_pairs,
            right_pairs,
            scaled_norms(left_pairs[:, :, :dim_count]),
            scaled_norms(right_pairs[:, :, :dim_count]),
        ),
        near_inner,
    )
    near_total, left_rows, right_rows = lax.optimization_barrier((near_total, left_rows, right_rows))

    all_coords = gathered[:, :, :dim_count]
    all_up = gathered[:, :, dim_count : dim_count + rhs_count]
    all_parts = gathered[:, :, dim_count + rhs_count :]
    picked_coords = select_rows(all_coords, source_columns)
    picked_up = select_rows(all_up, source_columns)
    kernel = kernel_block(jnp.broadcast_to(node_coords, picked_coords.shape), picked_coords)
    node_side = jnp.einsum("fab,fbr->ar", kernel, picked_up, preferred_element_type=jnp.float32)
    group_mask = (jnp.arange(group_width, dtype=jnp.int32) < group_rank[0]).astype(jnp.float32)
    group_up = (
        jnp.einsum("nag,nar->gr", all_parts, all_up, preferred_element_type=jnp.float32)
        * group_mask[:, None]
    ).astype(jnp.bfloat16)
    group_coords = select_rows(all_coords.reshape(columns * node_width, dim_count), group_skeleton[0])
    group_pack = jnp.concatenate([group_coords, group_up], axis=1)
    left_rows = left_rows.reshape(REACH, rank_count, skeleton_width)
    right_rows = right_rows.reshape(REACH, rank_count, skeleton_width)
    far_local = far_list - offset
    coord_norms = scaled_norms(leaf_coords)
    far_inner = far_field(leaf_coords, own_rows, coord_norms, far_local)
    far_total = far_field(
        leaf_coords,
        own_rows,
        coord_norms,
        far_local,
        (
            left_rows,
            right_rows,
            scaled_norms(left_rows[:, :, :dim_count]),
            scaled_norms(right_rows[:, :, :dim_count]),
        ),
        far_inner,
        group_pack,
    )
    rows = lax.axis_size("row")
    received = [group_pack] + [
        lax.ppermute(group_pack, "row", [(r, (r + shift) % rows) for r in range(rows)])
        for shift in range(1, rows)
    ]
    shifts = (lax.axis_index("row") - group_far[0]) % rows
    picked_group = select_rows(jnp.stack(received), shifts)
    picked_group_coords = picked_group[:, :, :dim_count]
    picked_group_up = picked_group[:, :, dim_count:]
    group_kernel = kernel_block(
        jnp.broadcast_to(group_coords, picked_group_coords.shape), picked_group_coords
    )
    group_down = (
        jnp.einsum("fab,fbr->ar", group_kernel, picked_group_up, preferred_element_type=jnp.float32)
        * group_mask[:, None]
    ).astype(jnp.bfloat16)
    node_down = (
        (jnp.dot(group_basis, group_down, preferred_element_type=jnp.float32) + node_side)
        * node_mask[:, None]
    ).astype(jnp.bfloat16)
    result = final_field(
        leaf_rank,
        node_basis.reshape(leaf_count, rank_count, node_width),
        node_down,
        far_total,
        local_bases,
        near_total,
    )
    return result.reshape(leaf_count * leaf_size, rhs_count)


def solution(mesh):
    in_specs = (
        P(FLAT, None),
        P(FLAT, None),
        P(FLAT, None),
        P(FLAT),
        P(FLAT, None),
        P(FLAT, None),
        P(FLAT, None),
        P(FLAT, None),
        P(FLAT),
        P(FLAT, None),
        P(FLAT, None),
        P(FLAT, None),
        P("row"),
        P("row", None),
        P("row", None),
    )
    out_specs = P(FLAT, None)

    return jax.shard_map(body, mesh=mesh, in_specs=in_specs, out_specs=out_specs, check_vma=False)
```

```python
import jax
import jax.numpy as jnp
from jax import lax
from jax.experimental import pallas as pl
from jax.experimental.pallas import tpu as pltpu
from jax.sharding import PartitionSpec as P


REACH = 8
FLAT = ("row", "col")


def halos(cells, width):
    count = lax.axis_size(FLAT)
    ends = count - 1
    head = jnp.concatenate([cell[:width] for cell in cells], axis=1)
    tail = jnp.concatenate([cell[cell.shape[0] - width :] for cell in cells], axis=1)
    left = lax.ppermute(tail, FLAT, [(i, i + 1) for i in range(ends)])
    right = lax.ppermute(head, FLAT, [(i + 1, i) for i in range(ends)])
    return left, right


def kernel_block(left, right):
    left_square = jnp.sum(jnp.square(left.astype(jnp.float32)), axis=-1)
    right_square = jnp.sum(jnp.square(right.astype(jnp.float32)), axis=-1)
    inner = jnp.einsum("...md,...nd->...mn", left, right, preferred_element_type=jnp.float32)
    distance = left_square[..., :, None] + right_square[..., None, :] - 2.0 * inner
    return jnp.exp(distance * (-2.0 / left.shape[-1])).astype(jnp.bfloat16)


def contract_last(a, b):
    return lax.dot_general(a, b, (((1,), (1,)), ((), ())), preferred_element_type=jnp.float32)


def scaled_kernel(target, target_square, source, source_square):
    dims = target.shape[-1]
    inner = contract_last(target * jnp.asarray(4.0 / dims, target.dtype), source)
    return jnp.exp((target_square + source_square) + inner).astype(jnp.bfloat16)


def scaled_norms(cells):
    wide = cells.astype(jnp.float32)
    return (jnp.sum(wide * wide, axis=-1) * (-2.0 / cells.shape[-1]))[:, None, :]


def target_square_of(target):
    wide = target.astype(jnp.float32)
    return jnp.sum(wide * wide, axis=-1, keepdims=True) * (-2.0 / target.shape[-1])


def fetch_sources(index_ref, row, count, parts, buffers, sems, slot):
    for position in range(count):
        source = index_ref[row * count + position]
        for which, (halo, mine, left, own, right) in enumerate(parts):
            target = buffers[which](slot, position)
            sem = sems.at[which, slot, position]
            if left is None:
                pltpu.make_async_copy(own(source - halo), target, sem).start()
                continue

            @pl.when(source < halo)
            def _():
                pltpu.make_async_copy(left(source), target, sem).start()

            @pl.when((source >= halo) & (source < halo + mine))
            def _():
                pltpu.make_async_copy(own(source - halo), target, sem).start()

            @pl.when(source >= halo + mine)
            def _():
                pltpu.make_async_copy(right(source - halo - mine), target, sem).start()


def wait_sources(count, parts, buffers, sems, slot):
    for position in range(count):
        for which, (halo, mine, left, own, right) in enumerate(parts):
            pltpu.make_async_copy(
                own(0), buffers[which](slot, position), sems.at[which, slot, position]
            ).wait()


def rows_of(ref):
    return lambda index: ref.at[index]


def whole_rows(left, own, right):
    return (left.shape[0], own.shape[0], rows_of(left), rows_of(own), rows_of(right))


def own_rows_only(own):
    return (REACH, own.shape[0], None, rows_of(own), None)


def lane_rows(left, own, right, start, width):
    def halo_at(ref):
        return lambda index: ref.at[index, :, pl.ds(start, width)]

    return (left.shape[0], own.shape[0], halo_at(left), rows_of(own), halo_at(right))


def pipelined_sources(index_ref, count, parts, buffers, sems, leaf_of):
    step = pl.program_id(0)
    steps = pl.num_programs(0)
    slot = step % 2

    @pl.when(step == 0)
    def _():
        fetch_sources(index_ref, leaf_of(0), count, parts, buffers, sems, 0)

    @pl.when(step + 1 < steps)
    def _():
        fetch_sources(index_ref, leaf_of(step + 1), count, parts, buffers, sems, 1 - slot)

    wait_sources(count, parts, buffers, sems, slot)
    return slot


def leaf_order(leaves, edges):
    low, high = REACH, leaves - REACH
    if high <= low:
        return (lambda step: step), leaves, None
    if not edges:
        return (lambda step: step + low), high - low, None
    gap = high - low
    return (lambda step: step + gap * jnp.asarray(step >= low, jnp.int32)), leaves - gap, gap


def near_kernel(leaf_of, halo, index_ref, target_ref, *refs):
    inputs = 9 if halo else 3
    out_ref = refs[inputs]
    point_buf, weight_buf, norm_buf, sems = refs[inputs + 1 :]
    count, size, dims = point_buf.shape[1], point_buf.shape[2], point_buf.shape[3]
    if halo:
        lpw, op, rpw, ow, ln, on, rn = refs[:7]
        parts = (
            lane_rows(lpw, op, rpw, 0, dims),
            lane_rows(lpw, ow, rpw, dims, weight_buf.shape[-1]),
            whole_rows(ln, on, rn),
        )
    else:
        parts = tuple(own_rows_only(ref) for ref in refs[:3])
    buffers = (
        lambda slot, position: point_buf.at[slot, position],
        lambda slot, position: weight_buf.at[slot, position],
        lambda slot, position: norm_buf.at[slot, :, pl.ds(position * size, size)],
    )
    slot = pipelined_sources(index_ref, count, parts, buffers, sems, leaf_of)
    target = target_ref[0]
    sources = point_buf[slot].reshape(count * size, dims)
    values = weight_buf[slot].reshape(count * size, weight_buf.shape[-1])
    kernel = scaled_kernel(target, target_square_of(target), sources, norm_buf[slot])
    out_ref[0] = jnp.dot(kernel, values, preferred_element_type=jnp.float32)


def near_field(local_points, local_weights, local_norms, near_local, halo_inputs=None, previous=None, after=None):
    leaves, size, dims = local_points.shape
    rhs = local_weights.shape[-1]
    count = near_local.shape[1]
    halo = halo_inputs is not None
    leaf_of, steps, _ = leaf_order(leaves, halo)
    anywhere = pl.BlockSpec(memory_space=pl.ANY)
    if halo:
        left_pairs, right_pairs, left_norms, right_norms = halo_inputs
        inputs = (left_pairs, local_points, right_pairs, local_weights, left_norms, local_norms, right_norms, after, previous)
    else:
        inputs = (local_points, local_weights, local_norms)
    aliases = {len(inputs) + 1: 0} if previous is not None else {}
    by_leaf = lambda step, index: (leaf_of(step), 0, 0)
    return pl.pallas_call(
        lambda *refs: near_kernel(leaf_of, halo, *refs),
        grid_spec=pltpu.PrefetchScalarGridSpec(
            num_scalar_prefetch=1,
            grid=(steps,),
            in_specs=[pl.BlockSpec((1, size, dims), by_leaf)] + [anywhere] * len(inputs),
            out_specs=pl.BlockSpec((1, size, rhs), by_leaf),
            scratch_shapes=[
                pltpu.VMEM((2, count, size, dims), local_points.dtype),
                pltpu.VMEM((2, count, size, rhs), local_weights.dtype),
                pltpu.VMEM((2, 1, count * size), jnp.float32),
                pltpu.SemaphoreType.DMA((3, 2, count)),
            ],
        ),
        out_shape=jax.ShapeDtypeStruct((leaves, size, rhs), jnp.float32),
        input_output_aliases=aliases,
        compiler_params=pltpu.CompilerParams(dimension_semantics=("arbitrary",)),
    )(near_local.reshape(-1), local_points, *inputs)


def far_kernel(leaf_of, halo, index_ref, target_ref, *refs):
    inputs = 7 if halo else 2
    out_ref = refs[inputs]
    source_buf, norm_buf, sems = refs[inputs + 1 :]
    count, rank = source_buf.shape[1], source_buf.shape[2]
    if halo:
        ls, os, rs, ln, on, rn = refs[:6]
        parts = (whole_rows(ls, os, rs), whole_rows(ln, on, rn))
    else:
        parts = tuple(own_rows_only(ref) for ref in refs[:2])
    buffers = (
        lambda slot, position: source_buf.at[slot, position],
        lambda slot, position: norm_buf.at[slot, :, pl.ds(position * rank, rank)],
    )
    slot = pipelined_sources(index_ref, count, parts, buffers, sems, leaf_of)
    target = target_ref[0]
    dims = target.shape[-1]
    sources = source_buf[slot].reshape(count * rank, source_buf.shape[-1])
    kernel = scaled_kernel(target, target_square_of(target), sources[:, :dims], norm_buf[slot])
    out_ref[0] = jnp.dot(kernel, sources[:, dims:], preferred_element_type=jnp.float32)


def far_field(leaf_coords, own_rows, own_norms, far_local, halo_inputs=None, previous=None):
    leaves, rank, dims = leaf_coords.shape
    width = own_rows.shape[-1]
    count = far_local.shape[1]
    halo = halo_inputs is not None
    leaf_of, steps, _ = leaf_order(leaves, halo)
    anywhere = pl.BlockSpec(memory_space=pl.ANY)
    if halo:
        left_rows, right_rows, left_norms, right_norms = halo_inputs
        inputs = (left_rows, own_rows, right_rows, left_norms, own_norms, right_norms, previous)
    else:
        inputs = (own_rows, own_norms)
    aliases = {len(inputs) + 1: 0} if previous is not None else {}
    by_leaf = lambda step, index: (leaf_of(step), 0, 0)
    return pl.pallas_call(
        lambda *refs: far_kernel(leaf_of, halo, *refs),
        grid_spec=pltpu.PrefetchScalarGridSpec(
            num_scalar_prefetch=1,
            grid=(steps,),
            in_specs=[pl.BlockSpec((1, rank, dims), by_leaf)] + [anywhere] * len(inputs),
            out_specs=pl.BlockSpec((1, rank, width - dims), by_leaf),
            scratch_shapes=[
                pltpu.VMEM((2, count, rank, width), own_rows.dtype),
                pltpu.VMEM((2, 1, count * rank), jnp.float32),
                pltpu.SemaphoreType.DMA((2, 2, count)),
            ],
        ),
        out_shape=jax.ShapeDtypeStruct((leaves, rank, width - dims), jnp.float32),
        input_output_aliases=aliases,
        compiler_params=pltpu.CompilerParams(dimension_semantics=("arbitrary",)),
    )(far_local.reshape(-1), leaf_coords, *inputs)


def final_kernel(rank_ref, basis_ref, down_ref, far_ref, leaf_base_ref, near_ref, out_ref):
    block = basis_ref.shape[0]
    step = pl.program_id(0)
    down = down_ref[...]
    for inside in range(block):
        total = jnp.dot(basis_ref[inside], down, preferred_element_type=jnp.float32) + far_ref[inside]
        rows = lax.broadcasted_iota(jnp.int32, total.shape, 0)
        leaf_down = jnp.where(rows < rank_ref[step * block + inside], total, 0.0).astype(jnp.bfloat16)
        result = (
            jnp.dot(leaf_base_ref[inside], leaf_down, preferred_element_type=jnp.float32)
            + near_ref[inside]
        )
        out_ref[inside] = result.astype(out_ref.dtype)


def final_field(leaf_rank, bases, node_down, far_total, leaf_bases, near_total):
    leaves, rank, width = bases.shape
    size = leaf_bases.shape[1]
    rhs = near_total.shape[-1]
    block = max(b for b in (1, 2, 3, 4) if leaves % b == 0)

    def own(l, ranks):
        return (l, 0, 0)

    return pl.pallas_call(
        final_kernel,
        grid_spec=pltpu.PrefetchScalarGridSpec(
            num_scalar_prefetch=1,
            grid=(leaves // block,),
            in_specs=[
                pl.BlockSpec((block, rank, width), own),
                pl.BlockSpec(node_down.shape, lambda l, ranks: (0, 0)),
                pl.BlockSpec((block, rank, rhs), own),
                pl.BlockSpec((block, size, rank), own),
                pl.BlockSpec((block, size, rhs), own),
            ],
            out_specs=pl.BlockSpec((block, size, rhs), own),
        ),
        out_shape=jax.ShapeDtypeStruct((leaves, size, rhs), jnp.bfloat16),
    )(leaf_rank, bases, node_down, far_total, leaf_bases, near_total)


def select_rows(table, index):
    count = table.shape[0]
    onehot = (index[:, None] == jnp.arange(count, dtype=jnp.int32)[None, :]).astype(table.dtype)
    picked = jnp.dot(onehot, table.reshape(count, -1), preferred_element_type=jnp.float32).astype(
        table.dtype
    )
    return picked.reshape(index.shape + table.shape[1:])


def select_within(table, index):
    count = table.shape[1]
    onehot = (index[:, :, None] == jnp.arange(count, dtype=jnp.int32)[None, None, :]).astype(
        table.dtype
    )
    return jnp.einsum("bkp,bpc->bkc", onehot, table, preferred_element_type=jnp.float32).astype(
        table.dtype
    )


def body(
    points,
    weights,
    leaf_basis,
    leaf_rank,
    leaf_skeleton,
    near_list,
    far_list,
    node_basis,
    node_rank,
    node_skeleton,
    node_far,
    group_basis,
    group_rank,
    group_skeleton,
    group_far,
):
    leaf_count = leaf_rank.shape[0]
    leaf_size = points.shape[0] // leaf_count
    dim_count = points.shape[1]
    rhs_count = weights.shape[1]
    rank_count = leaf_basis.shape[1]
    node_width = node_basis.shape[1]
    group_width = group_basis.shape[1]
    local_points = points.reshape(leaf_count, leaf_size, dim_count)
    local_bases = leaf_basis.reshape(leaf_count, leaf_size, rank_count)
    local_weights = weights.reshape(leaf_count, leaf_size, rhs_count)
    first_leaf = lax.axis_index(FLAT) * leaf_count
    offset = first_leaf - REACH

    left_pairs, right_pairs = halos((points, weights), REACH * leaf_size)
    left_pairs = left_pairs.reshape(REACH, leaf_size, dim_count + rhs_count)
    right_pairs = right_pairs.reshape(REACH, leaf_size, dim_count + rhs_count)

    leaf_mask = (
        lax.broadcasted_iota(jnp.int32, (leaf_count, rank_count), 1) < leaf_rank[:, None]
    ).astype(jnp.float32)
    leaf_up = (
        jnp.einsum("lpk,lpr->lkr", local_bases, local_weights, preferred_element_type=jnp.float32)
        * leaf_mask[:, :, None]
    ).astype(jnp.bfloat16)
    leaf_coords = select_within(local_points, leaf_skeleton)
    own_rows = jnp.concatenate([leaf_coords, leaf_up], axis=-1)
    skeleton_width = dim_count + rhs_count
    left_rows, right_rows = halos(
        (own_rows.reshape(leaf_count * rank_count, skeleton_width),), REACH * rank_count
    )

    node_mask = (jnp.arange(node_width, dtype=jnp.int32) < node_rank[0]).astype(jnp.float32)
    node_up = (
        jnp.einsum(
            "ak,ar->kr",
            node_basis,
            leaf_up.reshape(leaf_count * rank_count, rhs_count),
            preferred_element_type=jnp.float32,
        )
        * node_mask[:, None]
    ).astype(jnp.bfloat16)
    node_coords = select_rows(
        leaf_coords.reshape(leaf_count * rank_count, dim_count), node_skeleton[0]
    )
    columns = lax.axis_size("col")
    source_columns = node_far[0] % columns
    node_pack = jnp.concatenate([node_coords, node_up, group_basis], axis=1)
    gathered = lax.all_gather(node_pack[None], "col", axis=0, tiled=True)

    near_local = near_list - offset
    local_norms = scaled_norms(local_points)
    near_inner = near_field(local_points, local_weights, local_norms, near_local)
    all_coords = gathered[:, :, :dim_count]
    all_up = gathered[:, :, dim_count : dim_count + rhs_count]
    all_parts = gathered[:, :, dim_count + rhs_count :]
    picked_coords = select_rows(all_coords, source_columns)
    picked_up = select_rows(all_up, source_columns)
    kernel = kernel_block(jnp.broadcast_to(node_coords, picked_coords.shape), picked_coords)
    node_side = jnp.einsum("fab,fbr->ar", kernel, picked_up, preferred_element_type=jnp.float32)
    group_mask = (jnp.arange(group_width, dtype=jnp.int32) < group_rank[0]).astype(jnp.float32)
    group_up = (
        jnp.einsum("nag,nar->gr", all_parts, all_up, preferred_element_type=jnp.float32)
        * group_mask[:, None]
    ).astype(jnp.bfloat16)
    group_coords = select_rows(all_coords.reshape(columns * node_width, dim_count), group_skeleton[0])
    group_pack = jnp.concatenate([group_coords, group_up], axis=1)
    near_total = near_field(
        local_points,
        local_weights,
        local_norms,
        near_local,
        (
            left_pairs,
            right_pairs,
            scaled_norms(left_pairs[:, :, :dim_count]),
            scaled_norms(right_pairs[:, :, :dim_count]),
        ),
        near_inner,
        group_pack,
    )
    near_total, left_rows, right_rows = lax.optimization_barrier((near_total, left_rows, right_rows))

    left_rows = left_rows.reshape(REACH, rank_count, skeleton_width)
    right_rows = right_rows.reshape(REACH, rank_count, skeleton_width)
    far_local = far_list - offset
    coord_norms = scaled_norms(leaf_coords)
    far_inner = far_field(leaf_coords, own_rows, coord_norms, far_local)
    far_total = far_field(
        leaf_coords,
        own_rows,
        coord_norms,
        far_local,
        (
            left_rows,
            right_rows,
            scaled_norms(left_rows[:, :, :dim_count]),
            scaled_norms(right_rows[:, :, :dim_count]),
        ),
        far_inner,
    )
    rows = lax.axis_size("row")
    received = [group_pack] + [
        lax.ppermute(group_pack, "row", [(r, (r + shift) % rows) for r in range(rows)])
        for shift in range(1, rows)
    ]
    shifts = (lax.axis_index("row") - group_far[0]) % rows
    picked_group = select_rows(jnp.stack(received), shifts)
    picked_group_coords = picked_group[:, :, :dim_count]
    picked_group_up = picked_group[:, :, dim_count:]
    group_kernel = kernel_block(
        jnp.broadcast_to(group_coords, picked_group_coords.shape), picked_group_coords
    )
    group_down = (
        jnp.einsum("fab,fbr->ar", group_kernel, picked_group_up, preferred_element_type=jnp.float32)
        * group_mask[:, None]
    ).astype(jnp.bfloat16)
    node_down = (
        (jnp.dot(group_basis, group_down, preferred_element_type=jnp.float32) + node_side)
        * node_mask[:, None]
    ).astype(jnp.bfloat16)
    result = final_field(
        leaf_rank,
        node_basis.reshape(leaf_count, rank_count, node_width),
        node_down,
        far_total,
        local_bases,
        near_total,
    )
    return result.reshape(leaf_count * leaf_size, rhs_count)


def solution(mesh):
    in_specs = (
        P(FLAT, None),
        P(FLAT, None),
        P(FLAT, None),
        P(FLAT),
        P(FLAT, None),
        P(FLAT, None),
        P(FLAT, None),
        P(FLAT, None),
        P(FLAT),
        P(FLAT, None),
        P(FLAT, None),
        P(FLAT, None),
        P("row"),
        P("row", None),
        P("row", None),
    )
    out_specs = P(FLAT, None)

    return jax.shard_map(body, mesh=mesh, in_specs=in_specs, out_specs=out_specs, check_vma=False)
```

```python
import jax
import jax.numpy as jnp
from jax import lax
from jax.experimental import pallas as pl
from jax.experimental.pallas import tpu as pltpu
from jax.sharding import PartitionSpec as P


REACH = 8
FLAT = ("row", "col")


def halos(cells, width):
    count = lax.axis_size(FLAT)
    ends = count - 1
    head = jnp.concatenate([cell[:width] for cell in cells], axis=1)
    tail = jnp.concatenate([cell[cell.shape[0] - width :] for cell in cells], axis=1)
    left = lax.ppermute(tail, FLAT, [(i, i + 1) for i in range(ends)])
    right = lax.ppermute(head, FLAT, [(i + 1, i) for i in range(ends)])
    return left, right


def kernel_block(left, right):
    left_square = jnp.sum(jnp.square(left.astype(jnp.float32)), axis=-1)
    right_square = jnp.sum(jnp.square(right.astype(jnp.float32)), axis=-1)
    inner = jnp.einsum("...md,...nd->...mn", left, right, preferred_element_type=jnp.float32)
    distance = left_square[..., :, None] + right_square[..., None, :] - 2.0 * inner
    return jnp.exp(distance * (-2.0 / left.shape[-1])).astype(jnp.bfloat16)


def contract_last(a, b):
    return lax.dot_general(a, b, (((1,), (1,)), ((), ())), preferred_element_type=jnp.float32)


def scaled_kernel(target, target_square, source, source_square):
    dims = target.shape[-1]
    inner = contract_last(target * jnp.asarray(4.0 / dims, target.dtype), source)
    return jnp.exp((target_square + source_square) + inner).astype(jnp.bfloat16)


def scaled_norms(cells):
    wide = cells.astype(jnp.float32)
    return (jnp.sum(wide * wide, axis=-1) * (-2.0 / cells.shape[-1]))[:, None, :]


def target_square_of(target):
    wide = target.astype(jnp.float32)
    return jnp.sum(wide * wide, axis=-1, keepdims=True) * (-2.0 / target.shape[-1])


def fetch_sources(index_ref, row, count, parts, buffers, sems, slot):
    for position in range(count):
        source = index_ref[row * count + position]
        for which, (halo, mine, left, own, right) in enumerate(parts):
            target = buffers[which](slot, position)
            sem = sems.at[which, slot, position]
            if left is None:
                pltpu.make_async_copy(own(source - halo), target, sem).start()
                continue

            @pl.when(source < halo)
            def _():
                pltpu.make_async_copy(left(source), target, sem).start()

            @pl.when((source >= halo) & (source < halo + mine))
            def _():
                pltpu.make_async_copy(own(source - halo), target, sem).start()

            @pl.when(source >= halo + mine)
            def _():
                pltpu.make_async_copy(right(source - halo - mine), target, sem).start()


def wait_sources(count, parts, buffers, sems, slot):
    for position in range(count):
        for which, (halo, mine, left, own, right) in enumerate(parts):
            pltpu.make_async_copy(
                own(0), buffers[which](slot, position), sems.at[which, slot, position]
            ).wait()


def rows_of(ref):
    return lambda index: ref.at[index]


def whole_rows(left, own, right):
    return (left.shape[0], own.shape[0], rows_of(left), rows_of(own), rows_of(right))


def own_rows_only(own):
    return (REACH, own.shape[0], None, rows_of(own), None)


def lane_rows(left, own, right, start, width):
    def halo_at(ref):
        return lambda index: ref.at[index, :, pl.ds(start, width)]

    return (left.shape[0], own.shape[0], halo_at(left), rows_of(own), halo_at(right))


def pipelined_sources(index_ref, count, parts, buffers, sems, leaf_of):
    step = pl.program_id(0)
    steps = pl.num_programs(0)
    slot = step % 2

    @pl.when(step == 0)
    def _():
        fetch_sources(index_ref, leaf_of(0), count, parts, buffers, sems, 0)

    @pl.when(step + 1 < steps)
    def _():
        fetch_sources(index_ref, leaf_of(step + 1), count, parts, buffers, sems, 1 - slot)

    wait_sources(count, parts, buffers, sems, slot)
    return slot


def leaf_order(leaves, edges):
    low, high = REACH, leaves - REACH
    if high <= low:
        return (lambda step: step), leaves, None
    if not edges:
        return (lambda step: step + low), high - low, None
    gap = high - low
    return (lambda step: step + gap * jnp.asarray(step >= low, jnp.int32)), leaves - gap, gap


def near_kernel(leaf_of, halo, index_ref, target_ref, *refs):
    inputs = 9 if halo else 3
    out_ref = refs[inputs]
    point_buf, weight_buf, norm_buf, sems = refs[inputs + 1 :]
    count, size, dims = point_buf.shape[1], point_buf.shape[2], point_buf.shape[3]
    if halo:
        lpw, op, rpw, ow, ln, on, rn = refs[:7]
        parts = (
            lane_rows(lpw, op, rpw, 0, dims),
            lane_rows(lpw, ow, rpw, dims, weight_buf.shape[-1]),
            whole_rows(ln, on, rn),
        )
    else:
        parts = tuple(own_rows_only(ref) for ref in refs[:3])
    buffers = (
        lambda slot, position: point_buf.at[slot, position],
        lambda slot, position: weight_buf.at[slot, position],
        lambda slot, position: norm_buf.at[slot, :, pl.ds(position * size, size)],
    )
    slot = pipelined_sources(index_ref, count, parts, buffers, sems, leaf_of)
    target = target_ref[0]
    sources = point_buf[slot].reshape(count * size, dims)
    values = weight_buf[slot].reshape(count * size, weight_buf.shape[-1])
    kernel = scaled_kernel(target, target_square_of(target), sources, norm_buf[slot])
    out_ref[0] = jnp.dot(kernel, values, preferred_element_type=jnp.float32)


def near_field(local_points, local_weights, local_norms, near_local, halo_inputs=None, previous=None, after=None):
    leaves, size, dims = local_points.shape
    rhs = local_weights.shape[-1]
    count = near_local.shape[1]
    halo = halo_inputs is not None
    leaf_of, steps, _ = leaf_order(leaves, halo)
    anywhere = pl.BlockSpec(memory_space=pl.ANY)
    if halo:
        left_pairs, right_pairs, left_norms, right_norms = halo_inputs
        inputs = (left_pairs, local_points, right_pairs, local_weights, left_norms, local_norms, right_norms, after, previous)
    else:
        inputs = (local_points, local_weights, local_norms)
    aliases = {len(inputs) + 1: 0} if previous is not None else {}
    by_leaf = lambda step, index: (leaf_of(step), 0, 0)
    return pl.pallas_call(
        lambda *refs: near_kernel(leaf_of, halo, *refs),
        grid_spec=pltpu.PrefetchScalarGridSpec(
            num_scalar_prefetch=1,
            grid=(steps,),
            in_specs=[pl.BlockSpec((1, size, dims), by_leaf)] + [anywhere] * len(inputs),
            out_specs=pl.BlockSpec((1, size, rhs), by_leaf),
            scratch_shapes=[
                pltpu.VMEM((2, count, size, dims), local_points.dtype),
                pltpu.VMEM((2, count, size, rhs), local_weights.dtype),
                pltpu.VMEM((2, 1, count * size), jnp.float32),
                pltpu.SemaphoreType.DMA((3, 2, count)),
            ],
        ),
        out_shape=jax.ShapeDtypeStruct((leaves, size, rhs), jnp.float32),
        input_output_aliases=aliases,
        compiler_params=pltpu.CompilerParams(dimension_semantics=("arbitrary",)),
    )(near_local.reshape(-1), local_points, *inputs)


def far_kernel(leaf_of, halo, index_ref, target_ref, *refs):
    inputs = 7 if halo else 3
    out_ref = refs[inputs]
    source_buf, norm_buf, sems = refs[inputs + 1 :]
    count, rank = source_buf.shape[1], source_buf.shape[2]
    if halo:
        ls, os, rs, ln, on, rn = refs[:6]
        parts = (whole_rows(ls, os, rs), whole_rows(ln, on, rn))
    else:
        parts = tuple(own_rows_only(ref) for ref in refs[:2])
    buffers = (
        lambda slot, position: source_buf.at[slot, position],
        lambda slot, position: norm_buf.at[slot, :, pl.ds(position * rank, rank)],
    )
    slot = pipelined_sources(index_ref, count, parts, buffers, sems, leaf_of)
    target = target_ref[0]
    dims = target.shape[-1]
    sources = source_buf[slot].reshape(count * rank, source_buf.shape[-1])
    kernel = scaled_kernel(target, target_square_of(target), sources[:, :dims], norm_buf[slot])
    out_ref[0] = jnp.dot(kernel, sources[:, dims:], preferred_element_type=jnp.float32)


def far_field(leaf_coords, own_rows, own_norms, far_local, halo_inputs=None, previous=None, after=None):
    leaves, rank, dims = leaf_coords.shape
    width = own_rows.shape[-1]
    count = far_local.shape[1]
    halo = halo_inputs is not None
    leaf_of, steps, _ = leaf_order(leaves, halo)
    anywhere = pl.BlockSpec(memory_space=pl.ANY)
    if halo:
        left_rows, right_rows, left_norms, right_norms = halo_inputs
        inputs = (left_rows, own_rows, right_rows, left_norms, own_norms, right_norms, previous)
    else:
        inputs = (own_rows, own_norms, after)
    aliases = {len(inputs) + 1: 0} if previous is not None else {}
    by_leaf = lambda step, index: (leaf_of(step), 0, 0)
    return pl.pallas_call(
        lambda *refs: far_kernel(leaf_of, halo, *refs),
        grid_spec=pltpu.PrefetchScalarGridSpec(
            num_scalar_prefetch=1,
            grid=(steps,),
            in_specs=[pl.BlockSpec((1, rank, dims), by_leaf)] + [anywhere] * len(inputs),
            out_specs=pl.BlockSpec((1, rank, width - dims), by_leaf),
            scratch_shapes=[
                pltpu.VMEM((2, count, rank, width), own_rows.dtype),
                pltpu.VMEM((2, 1, count * rank), jnp.float32),
                pltpu.SemaphoreType.DMA((2, 2, count)),
            ],
        ),
        out_shape=jax.ShapeDtypeStruct((leaves, rank, width - dims), jnp.float32),
        input_output_aliases=aliases,
        compiler_params=pltpu.CompilerParams(dimension_semantics=("arbitrary",)),
    )(far_local.reshape(-1), leaf_coords, *inputs)


def final_kernel(rank_ref, basis_ref, down_ref, far_ref, leaf_base_ref, near_ref, out_ref):
    block = basis_ref.shape[0]
    step = pl.program_id(0)
    down = down_ref[...]
    for inside in range(block):
        total = jnp.dot(basis_ref[inside], down, preferred_element_type=jnp.float32) + far_ref[inside]
        rows = lax.broadcasted_iota(jnp.int32, total.shape, 0)
        leaf_down = jnp.where(rows < rank_ref[step * block + inside], total, 0.0).astype(jnp.bfloat16)
        result = (
            jnp.dot(leaf_base_ref[inside], leaf_down, preferred_element_type=jnp.float32)
            + near_ref[inside]
        )
        out_ref[inside] = result.astype(out_ref.dtype)


def final_field(leaf_rank, bases, node_down, far_total, leaf_bases, near_total):
    leaves, rank, width = bases.shape
    size = leaf_bases.shape[1]
    rhs = near_total.shape[-1]
    block = max(b for b in (1, 2, 3, 4) if leaves % b == 0)

    def own(l, ranks):
        return (l, 0, 0)

    return pl.pallas_call(
        final_kernel,
        grid_spec=pltpu.PrefetchScalarGridSpec(
            num_scalar_prefetch=1,
            grid=(leaves // block,),
            in_specs=[
                pl.BlockSpec((block, rank, width), own),
                pl.BlockSpec(node_down.shape, lambda l, ranks: (0, 0)),
                pl.BlockSpec((block, rank, rhs), own),
                pl.BlockSpec((block, size, rank), own),
                pl.BlockSpec((block, size, rhs), own),
            ],
            out_specs=pl.BlockSpec((block, size, rhs), own),
        ),
        out_shape=jax.ShapeDtypeStruct((leaves, size, rhs), jnp.bfloat16),
    )(leaf_rank, bases, node_down, far_total, leaf_bases, near_total)


def select_rows(table, index):
    count = table.shape[0]
    onehot = (index[:, None] == jnp.arange(count, dtype=jnp.int32)[None, :]).astype(table.dtype)
    picked = jnp.dot(onehot, table.reshape(count, -1), preferred_element_type=jnp.float32).astype(
        table.dtype
    )
    return picked.reshape(index.shape + table.shape[1:])


def select_within(table, index):
    count = table.shape[1]
    onehot = (index[:, :, None] == jnp.arange(count, dtype=jnp.int32)[None, None, :]).astype(
        table.dtype
    )
    return jnp.einsum("bkp,bpc->bkc", onehot, table, preferred_element_type=jnp.float32).astype(
        table.dtype
    )


def body(
    points,
    weights,
    leaf_basis,
    leaf_rank,
    leaf_skeleton,
    near_list,
    far_list,
    node_basis,
    node_rank,
    node_skeleton,
    node_far,
    group_basis,
    group_rank,
    group_skeleton,
    group_far,
):
    leaf_count = leaf_rank.shape[0]
    leaf_size = points.shape[0] // leaf_count
    dim_count = points.shape[1]
    rhs_count = weights.shape[1]
    rank_count = leaf_basis.shape[1]
    node_width = node_basis.shape[1]
    group_width = group_basis.shape[1]
    local_points = points.reshape(leaf_count, leaf_size, dim_count)
    local_bases = leaf_basis.reshape(leaf_count, leaf_size, rank_count)
    local_weights = weights.reshape(leaf_count, leaf_size, rhs_count)
    first_leaf = lax.axis_index(FLAT) * leaf_count
    offset = first_leaf - REACH

    left_pairs, right_pairs = halos((points, weights), REACH * leaf_size)
    left_pairs = left_pairs.reshape(REACH, leaf_size, dim_count + rhs_count)
    right_pairs = right_pairs.reshape(REACH, leaf_size, dim_count + rhs_count)

    leaf_mask = (
        lax.broadcasted_iota(jnp.int32, (leaf_count, rank_count), 1) < leaf_rank[:, None]
    ).astype(jnp.float32)
    leaf_up = (
        jnp.einsum("lpk,lpr->lkr", local_bases, local_weights, preferred_element_type=jnp.float32)
        * leaf_mask[:, :, None]
    ).astype(jnp.bfloat16)
    leaf_coords = select_within(local_points, leaf_skeleton)
    own_rows = jnp.concatenate([leaf_coords, leaf_up], axis=-1)
    skeleton_width = dim_count + rhs_count
    left_rows, right_rows = halos(
        (own_rows.reshape(leaf_count * rank_count, skeleton_width),), REACH * rank_count
    )

    node_mask = (jnp.arange(node_width, dtype=jnp.int32) < node_rank[0]).astype(jnp.float32)
    node_up = (
        jnp.einsum(
            "ak,ar->kr",
            node_basis,
            leaf_up.reshape(leaf_count * rank_count, rhs_count),
            preferred_element_type=jnp.float32,
        )
        * node_mask[:, None]
    ).astype(jnp.bfloat16)
    node_coords = select_rows(
        leaf_coords.reshape(leaf_count * rank_count, dim_count), node_skeleton[0]
    )
    columns = lax.axis_size("col")
    source_columns = node_far[0] % columns
    node_pack = jnp.concatenate([node_coords, node_up, group_basis], axis=1)
    gathered = lax.all_gather(node_pack[None], "col", axis=0, tiled=True)

    near_local = near_list - offset
    local_norms = scaled_norms(local_points)
    near_inner = near_field(local_points, local_weights, local_norms, near_local)
    all_coords = gathered[:, :, :dim_count]
    all_up = gathered[:, :, dim_count : dim_count + rhs_count]
    all_parts = gathered[:, :, dim_count + rhs_count :]
    picked_coords = select_rows(all_coords, source_columns)
    picked_up = select_rows(all_up, source_columns)
    kernel = kernel_block(jnp.broadcast_to(node_coords, picked_coords.shape), picked_coords)
    node_side = jnp.einsum("fab,fbr->ar", kernel, picked_up, preferred_element_type=jnp.float32)
    group_mask = (jnp.arange(group_width, dtype=jnp.int32) < group_rank[0]).astype(jnp.float32)
    group_up = (
        jnp.einsum("nag,nar->gr", all_parts, all_up, preferred_element_type=jnp.float32)
        * group_mask[:, None]
    ).astype(jnp.bfloat16)
    group_coords = select_rows(all_coords.reshape(columns * node_width, dim_count), group_skeleton[0])
    group_pack = jnp.concatenate([group_coords, group_up], axis=1)
    far_local = far_list - offset
    coord_norms = scaled_norms(leaf_coords)
    far_inner = far_field(leaf_coords, own_rows, coord_norms, far_local, after=group_pack)
    near_total = near_field(
        local_points,
        local_weights,
        local_norms,
        near_local,
        (
            left_pairs,
            right_pairs,
            scaled_norms(left_pairs[:, :, :dim_count]),
            scaled_norms(right_pairs[:, :, :dim_count]),
        ),
        near_inner,
        group_pack,
    )
    near_total, left_rows, right_rows = lax.optimization_barrier((near_total, left_rows, right_rows))

    left_rows = left_rows.reshape(REACH, rank_count, skeleton_width)
    right_rows = right_rows.reshape(REACH, rank_count, skeleton_width)
    far_total = far_field(
        leaf_coords,
        own_rows,
        coord_norms,
        far_local,
        (
            left_rows,
            right_rows,
            scaled_norms(left_rows[:, :, :dim_count]),
            scaled_norms(right_rows[:, :, :dim_count]),
        ),
        far_inner,
    )
    rows = lax.axis_size("row")
    received = [group_pack] + [
        lax.ppermute(group_pack, "row", [(r, (r + shift) % rows) for r in range(rows)])
        for shift in range(1, rows)
    ]
    shifts = (lax.axis_index("row") - group_far[0]) % rows
    picked_group = select_rows(jnp.stack(received), shifts)
    picked_group_coords = picked_group[:, :, :dim_count]
    picked_group_up = picked_group[:, :, dim_count:]
    group_kernel = kernel_block(
        jnp.broadcast_to(group_coords, picked_group_coords.shape), picked_group_coords
    )
    group_down = (
        jnp.einsum("fab,fbr->ar", group_kernel, picked_group_up, preferred_element_type=jnp.float32)
        * group_mask[:, None]
    ).astype(jnp.bfloat16)
    node_down = (
        (jnp.dot(group_basis, group_down, preferred_element_type=jnp.float32) + node_side)
        * node_mask[:, None]
    ).astype(jnp.bfloat16)
    result = final_field(
        leaf_rank,
        node_basis.reshape(leaf_count, rank_count, node_width),
        node_down,
        far_total,
        local_bases,
        near_total,
    )
    return result.reshape(leaf_count * leaf_size, rhs_count)


def solution(mesh):
    in_specs = (
        P(FLAT, None),
        P(FLAT, None),
        P(FLAT, None),
        P(FLAT),
        P(FLAT, None),
        P(FLAT, None),
        P(FLAT, None),
        P(FLAT, None),
        P(FLAT),
        P(FLAT, None),
        P(FLAT, None),
        P(FLAT, None),
        P("row"),
        P("row", None),
        P("row", None),
    )
    out_specs = P(FLAT, None)

    return jax.shard_map(body, mesh=mesh, in_specs=in_specs, out_specs=out_specs, check_vma=False)
```

```python
import jax
import jax.numpy as jnp
from jax import lax
from jax.experimental import pallas as pl
from jax.experimental.pallas import tpu as pltpu
from jax.sharding import PartitionSpec as P


REACH = 8
FLAT = ("row", "col")


def halos(cells, width):
    count = lax.axis_size(FLAT)
    ends = count - 1
    head = jnp.concatenate([cell[:width] for cell in cells], axis=1)
    tail = jnp.concatenate([cell[cell.shape[0] - width :] for cell in cells], axis=1)
    left = lax.ppermute(tail, FLAT, [(i, i + 1) for i in range(ends)])
    right = lax.ppermute(head, FLAT, [(i + 1, i) for i in range(ends)])
    return left, right


def kernel_block(left, right):
    left_square = jnp.sum(jnp.square(left.astype(jnp.float32)), axis=-1)
    right_square = jnp.sum(jnp.square(right.astype(jnp.float32)), axis=-1)
    inner = jnp.einsum("...md,...nd->...mn", left, right, preferred_element_type=jnp.float32)
    distance = left_square[..., :, None] + right_square[..., None, :] - 2.0 * inner
    return jnp.exp(distance * (-2.0 / left.shape[-1])).astype(jnp.bfloat16)


def contract_last(a, b):
    return lax.dot_general(a, b, (((1,), (1,)), ((), ())), preferred_element_type=jnp.float32)


def scaled_kernel(target, target_square, source, source_square):
    dims = target.shape[-1]
    inner = contract_last(target * jnp.asarray(4.0 / dims, target.dtype), source)
    return jnp.exp((target_square + source_square) + inner).astype(jnp.bfloat16)


def scaled_norms(cells):
    factor = (2.0 / cells.shape[-1]) ** 0.5
    assert factor * factor == 2.0 / cells.shape[-1]
    wide = cells.astype(jnp.float32) * factor
    return jnp.sum(wide * -wide, axis=-1)


def target_square_of(target):
    wide = target.astype(jnp.float32)
    return jnp.sum(wide * wide, axis=-1, keepdims=True) * (-2.0 / target.shape[-1])


def fetch_sources(index_ref, row, count, parts, buffers, sems, slot):
    for position in range(count):
        source = index_ref[row * count + position]
        for which, (halo, mine, left, own, right) in enumerate(parts):
            target = buffers[which](slot, position)
            sem = sems.at[which, slot, position]
            if left is None:
                pltpu.make_async_copy(own(source - halo), target, sem).start()
                continue

            @pl.when(source < halo)
            def _():
                pltpu.make_async_copy(left(source), target, sem).start()

            @pl.when((source >= halo) & (source < halo + mine))
            def _():
                pltpu.make_async_copy(own(source - halo), target, sem).start()

            @pl.when(source >= halo + mine)
            def _():
                pltpu.make_async_copy(right(source - halo - mine), target, sem).start()


def wait_sources(count, parts, buffers, sems, slot):
    for position in range(count):
        for which, (halo, mine, left, own, right) in enumerate(parts):
            pltpu.make_async_copy(
                own(0), buffers[which](slot, position), sems.at[which, slot, position]
            ).wait()


def rows_of(ref):
    return lambda index: ref.at[index]


def row_of(ref):
    return lambda index: ref.at[pl.ds(index, 1)]


def norm_rows(left, own, right):
    return (left.shape[0], own.shape[0], row_of(left), row_of(own), row_of(right))


def own_norms_only(own):
    return (REACH, own.shape[0], None, row_of(own), None)


def whole_rows(left, own, right):
    return (left.shape[0], own.shape[0], rows_of(left), rows_of(own), rows_of(right))


def own_rows_only(own):
    return (REACH, own.shape[0], None, rows_of(own), None)


def lane_rows(left, own, right, start, width):
    def halo_at(ref):
        return lambda index: ref.at[index, :, pl.ds(start, width)]

    return (left.shape[0], own.shape[0], halo_at(left), rows_of(own), halo_at(right))


def pipelined_sources(index_ref, count, parts, buffers, sems, leaf_of):
    step = pl.program_id(0)
    steps = pl.num_programs(0)
    slot = step % 2

    @pl.when(step == 0)
    def _():
        fetch_sources(index_ref, leaf_of(0), count, parts, buffers, sems, 0)

    @pl.when(step + 1 < steps)
    def _():
        fetch_sources(index_ref, leaf_of(step + 1), count, parts, buffers, sems, 1 - slot)

    wait_sources(count, parts, buffers, sems, slot)
    return slot


def leaf_order(leaves, edges):
    low, high = REACH, leaves - REACH
    if high <= low:
        return (lambda step: step), leaves, None
    if not edges:
        return (lambda step: step + low), high - low, None
    gap = high - low
    return (lambda step: step + gap * jnp.asarray(step >= low, jnp.int32)), leaves - gap, gap


def near_kernel(leaf_of, halo, index_ref, target_ref, *refs):
    inputs = 9 if halo else 3
    out_ref = refs[inputs]
    point_buf, weight_buf, norm_buf, sems = refs[inputs + 1 :]
    count, size, dims = point_buf.shape[1], point_buf.shape[2], point_buf.shape[3]
    if halo:
        lpw, op, rpw, ow, ln, on, rn = refs[:7]
        parts = (
            lane_rows(lpw, op, rpw, 0, dims),
            lane_rows(lpw, ow, rpw, dims, weight_buf.shape[-1]),
            norm_rows(ln, on, rn),
        )
    else:
        parts = (own_rows_only(refs[0]), own_rows_only(refs[1]), own_norms_only(refs[2]))
    buffers = (
        lambda slot, position: point_buf.at[slot, position],
        lambda slot, position: weight_buf.at[slot, position],
        lambda slot, position: norm_buf.at[slot, :, pl.ds(position * size, size)],
    )
    slot = pipelined_sources(index_ref, count, parts, buffers, sems, leaf_of)
    target = target_ref[0]
    sources = point_buf[slot].reshape(count * size, dims)
    values = weight_buf[slot].reshape(count * size, weight_buf.shape[-1])
    kernel = scaled_kernel(target, target_square_of(target), sources, norm_buf[slot])
    out_ref[0] = jnp.dot(kernel, values, preferred_element_type=jnp.float32)


def near_field(local_points, local_weights, local_norms, near_local, halo_inputs=None, previous=None, after=None):
    leaves, size, dims = local_points.shape
    rhs = local_weights.shape[-1]
    count = near_local.shape[1]
    halo = halo_inputs is not None
    leaf_of, steps, _ = leaf_order(leaves, halo)
    anywhere = pl.BlockSpec(memory_space=pl.ANY)
    if halo:
        left_pairs, right_pairs, left_norms, right_norms = halo_inputs
        inputs = (left_pairs, local_points, right_pairs, local_weights, left_norms, local_norms, right_norms, after, previous)
    else:
        inputs = (local_points, local_weights, local_norms)
    aliases = {len(inputs) + 1: 0} if previous is not None else {}
    by_leaf = lambda step, index: (leaf_of(step), 0, 0)
    return pl.pallas_call(
        lambda *refs: near_kernel(leaf_of, halo, *refs),
        grid_spec=pltpu.PrefetchScalarGridSpec(
            num_scalar_prefetch=1,
            grid=(steps,),
            in_specs=[pl.BlockSpec((1, size, dims), by_leaf)] + [anywhere] * len(inputs),
            out_specs=pl.BlockSpec((1, size, rhs), by_leaf),
            scratch_shapes=[
                pltpu.VMEM((2, count, size, dims), local_points.dtype),
                pltpu.VMEM((2, count, size, rhs), local_weights.dtype),
                pltpu.VMEM((2, 1, count * size), jnp.float32),
                pltpu.SemaphoreType.DMA((3, 2, count)),
            ],
        ),
        out_shape=jax.ShapeDtypeStruct((leaves, size, rhs), jnp.float32),
        input_output_aliases=aliases,
        compiler_params=pltpu.CompilerParams(dimension_semantics=("arbitrary",)),
    )(near_local.reshape(-1), local_points, *inputs)


def far_kernel(leaf_of, halo, index_ref, target_ref, *refs):
    inputs = 7 if halo else 2
    out_ref = refs[inputs]
    source_buf, norm_buf, sems = refs[inputs + 1 :]
    count, rank = source_buf.shape[1], source_buf.shape[2]
    if halo:
        ls, os, rs, ln, on, rn = refs[:6]
        parts = (whole_rows(ls, os, rs), norm_rows(ln, on, rn))
    else:
        parts = (own_rows_only(refs[0]), own_norms_only(refs[1]))
    buffers = (
        lambda slot, position: source_buf.at[slot, position],
        lambda slot, position: norm_buf.at[slot, :, pl.ds(position * rank, rank)],
    )
    slot = pipelined_sources(index_ref, count, parts, buffers, sems, leaf_of)
    target = target_ref[0]
    dims = target.shape[-1]
    sources = source_buf[slot].reshape(count * rank, source_buf.shape[-1])
    kernel = scaled_kernel(target, target_square_of(target), sources[:, :dims], norm_buf[slot])
    out_ref[0] = jnp.dot(kernel, sources[:, dims:], preferred_element_type=jnp.float32)


def far_field(leaf_coords, own_rows, own_norms, far_local, halo_inputs=None, previous=None):
    leaves, rank, dims = leaf_coords.shape
    width = own_rows.shape[-1]
    count = far_local.shape[1]
    halo = halo_inputs is not None
    leaf_of, steps, _ = leaf_order(leaves, halo)
    anywhere = pl.BlockSpec(memory_space=pl.ANY)
    if halo:
        left_rows, right_rows, left_norms, right_norms = halo_inputs
        inputs = (left_rows, own_rows, right_rows, left_norms, own_norms, right_norms, previous)
    else:
        inputs = (own_rows, own_norms)
    aliases = {len(inputs) + 1: 0} if previous is not None else {}
    by_leaf = lambda step, index: (leaf_of(step), 0, 0)
    return pl.pallas_call(
        lambda *refs: far_kernel(leaf_of, halo, *refs),
        grid_spec=pltpu.PrefetchScalarGridSpec(
            num_scalar_prefetch=1,
            grid=(steps,),
            in_specs=[pl.BlockSpec((1, rank, dims), by_leaf)] + [anywhere] * len(inputs),
            out_specs=pl.BlockSpec((1, rank, width - dims), by_leaf),
            scratch_shapes=[
                pltpu.VMEM((2, count, rank, width), own_rows.dtype),
                pltpu.VMEM((2, 1, count * rank), jnp.float32),
                pltpu.SemaphoreType.DMA((2, 2, count)),
            ],
        ),
        out_shape=jax.ShapeDtypeStruct((leaves, rank, width - dims), jnp.float32),
        input_output_aliases=aliases,
        compiler_params=pltpu.CompilerParams(dimension_semantics=("arbitrary",)),
    )(far_local.reshape(-1), leaf_coords, *inputs)


def final_kernel(rank_ref, basis_ref, down_ref, far_ref, leaf_base_ref, near_ref, out_ref):
    block = basis_ref.shape[0]
    step = pl.program_id(0)
    down = down_ref[...]
    for inside in range(block):
        total = jnp.dot(basis_ref[inside], down, preferred_element_type=jnp.float32) + far_ref[inside]
        rows = lax.broadcasted_iota(jnp.int32, total.shape, 0)
        leaf_down = jnp.where(rows < rank_ref[step * block + inside], total, 0.0).astype(jnp.bfloat16)
        result = (
            jnp.dot(leaf_base_ref[inside], leaf_down, preferred_element_type=jnp.float32)
            + near_ref[inside]
        )
        out_ref[inside] = result.astype(out_ref.dtype)


def final_field(leaf_rank, bases, node_down, far_total, leaf_bases, near_total):
    leaves, rank, width = bases.shape
    size = leaf_bases.shape[1]
    rhs = near_total.shape[-1]
    block = max(b for b in (1, 2, 3, 4) if leaves % b == 0)

    def own(l, ranks):
        return (l, 0, 0)

    return pl.pallas_call(
        final_kernel,
        grid_spec=pltpu.PrefetchScalarGridSpec(
            num_scalar_prefetch=1,
            grid=(leaves // block,),
            in_specs=[
                pl.BlockSpec((block, rank, width), own),
                pl.BlockSpec(node_down.shape, lambda l, ranks: (0, 0)),
                pl.BlockSpec((block, rank, rhs), own),
                pl.BlockSpec((block, size, rank), own),
                pl.BlockSpec((block, size, rhs), own),
            ],
            out_specs=pl.BlockSpec((block, size, rhs), own),
        ),
        out_shape=jax.ShapeDtypeStruct((leaves, size, rhs), jnp.bfloat16),
    )(leaf_rank, bases, node_down, far_total, leaf_bases, near_total)


def select_rows(table, index):
    count = table.shape[0]
    onehot = (index[:, None] == jnp.arange(count, dtype=jnp.int32)[None, :]).astype(table.dtype)
    picked = jnp.dot(onehot, table.reshape(count, -1), preferred_element_type=jnp.float32).astype(
        table.dtype
    )
    return picked.reshape(index.shape + table.shape[1:])


def select_within(table, index):
    count = table.shape[1]
    onehot = (index[:, :, None] == jnp.arange(count, dtype=jnp.int32)[None, None, :]).astype(
        table.dtype
    )
    return jnp.einsum("bkp,bpc->bkc", onehot, table, preferred_element_type=jnp.float32).astype(
        table.dtype
    )


def body(
    points,
    weights,
    leaf_basis,
    leaf_rank,
    leaf_skeleton,
    near_list,
    far_list,
    node_basis,
    node_rank,
    node_skeleton,
    node_far,
    group_basis,
    group_rank,
    group_skeleton,
    group_far,
):
    leaf_count = leaf_rank.shape[0]
    leaf_size = points.shape[0] // leaf_count
    dim_count = points.shape[1]
    rhs_count = weights.shape[1]
    rank_count = leaf_basis.shape[1]
    node_width = node_basis.shape[1]
    group_width = group_basis.shape[1]
    local_points = points.reshape(leaf_count, leaf_size, dim_count)
    local_bases = leaf_basis.reshape(leaf_count, leaf_size, rank_count)
    local_weights = weights.reshape(leaf_count, leaf_size, rhs_count)
    first_leaf = lax.axis_index(FLAT) * leaf_count
    offset = first_leaf - REACH

    left_pairs, right_pairs = halos((points, weights), REACH * leaf_size)
    left_pairs = left_pairs.reshape(REACH, leaf_size, dim_count + rhs_count)
    right_pairs = right_pairs.reshape(REACH, leaf_size, dim_count + rhs_count)

    leaf_mask = (
        lax.broadcasted_iota(jnp.int32, (leaf_count, rank_count), 1) < leaf_rank[:, None]
    ).astype(jnp.float32)
    leaf_up = (
        jnp.einsum("lpk,lpr->lkr", local_bases, local_weights, preferred_element_type=jnp.float32)
        * leaf_mask[:, :, None]
    ).astype(jnp.bfloat16)
    leaf_coords = select_within(local_points, leaf_skeleton)
    own_rows = jnp.concatenate([leaf_coords, leaf_up], axis=-1)
    skeleton_width = dim_count + rhs_count
    left_rows, right_rows = halos(
        (own_rows.reshape(leaf_count * rank_count, skeleton_width),), REACH * rank_count
    )

    node_mask = (jnp.arange(node_width, dtype=jnp.int32) < node_rank[0]).astype(jnp.float32)
    node_up = (
        jnp.einsum(
            "ak,ar->kr",
            node_basis,
            leaf_up.reshape(leaf_count * rank_count, rhs_count),
            preferred_element_type=jnp.float32,
        )
        * node_mask[:, None]
    ).astype(jnp.bfloat16)
    node_coords = select_rows(
        leaf_coords.reshape(leaf_count * rank_count, dim_count), node_skeleton[0]
    )
    columns = lax.axis_size("col")
    source_columns = node_far[0] % columns
    node_pack = jnp.concatenate([node_coords, node_up, group_basis], axis=1)
    gathered = lax.all_gather(node_pack[None], "col", axis=0, tiled=True)

    near_local = near_list - offset
    local_norms = scaled_norms(local_points)
    near_inner = near_field(local_points, local_weights, local_norms, near_local)
    all_coords = gathered[:, :, :dim_count]
    all_up = gathered[:, :, dim_count : dim_count + rhs_count]
    all_parts = gathered[:, :, dim_count + rhs_count :]
    picked_coords = select_rows(all_coords, source_columns)
    picked_up = select_rows(all_up, source_columns)
    kernel = kernel_block(jnp.broadcast_to(node_coords, picked_coords.shape), picked_coords)
    node_side = jnp.einsum("fab,fbr->ar", kernel, picked_up, preferred_element_type=jnp.float32)
    group_mask = (jnp.arange(group_width, dtype=jnp.int32) < group_rank[0]).astype(jnp.float32)
    group_up = (
        jnp.einsum("nag,nar->gr", all_parts, all_up, preferred_element_type=jnp.float32)
        * group_mask[:, None]
    ).astype(jnp.bfloat16)
    group_coords = select_rows(all_coords.reshape(columns * node_width, dim_count), group_skeleton[0])
    group_pack = jnp.concatenate([group_coords, group_up], axis=1)
    near_total = near_field(
        local_points,
        local_weights,
        local_norms,
        near_local,
        (
            left_pairs,
            right_pairs,
            scaled_norms(left_pairs[:, :, :dim_count]),
            scaled_norms(right_pairs[:, :, :dim_count]),
        ),
        near_inner,
        group_pack,
    )
    near_total, left_rows, right_rows = lax.optimization_barrier((near_total, left_rows, right_rows))

    left_rows = left_rows.reshape(REACH, rank_count, skeleton_width)
    right_rows = right_rows.reshape(REACH, rank_count, skeleton_width)
    far_local = far_list - offset
    coord_norms = scaled_norms(leaf_coords)
    far_inner = far_field(leaf_coords, own_rows, coord_norms, far_local)
    far_total = far_field(
        leaf_coords,
        own_rows,
        coord_norms,
        far_local,
        (
            left_rows,
            right_rows,
            scaled_norms(left_rows[:, :, :dim_count]),
            scaled_norms(right_rows[:, :, :dim_count]),
        ),
        far_inner,
    )
    rows = lax.axis_size("row")
    received = [group_pack] + [
        lax.ppermute(group_pack, "row", [(r, (r + shift) % rows) for r in range(rows)])
        for shift in range(1, rows)
    ]
    shifts = (lax.axis_index("row") - group_far[0]) % rows
    picked_group = select_rows(jnp.stack(received), shifts)
    picked_group_coords = picked_group[:, :, :dim_count]
    picked_group_up = picked_group[:, :, dim_count:]
    group_kernel = kernel_block(
        jnp.broadcast_to(group_coords, picked_group_coords.shape), picked_group_coords
    )
    group_down = (
        jnp.einsum("fab,fbr->ar", group_kernel, picked_group_up, preferred_element_type=jnp.float32)
        * group_mask[:, None]
    ).astype(jnp.bfloat16)
    node_down = (
        (jnp.dot(group_basis, group_down, preferred_element_type=jnp.float32) + node_side)
        * node_mask[:, None]
    ).astype(jnp.bfloat16)
    result = final_field(
        leaf_rank,
        node_basis.reshape(leaf_count, rank_count, node_width),
        node_down,
        far_total,
        local_bases,
        near_total,
    )
    return result.reshape(leaf_count * leaf_size, rhs_count)


def solution(mesh):
    in_specs = (
        P(FLAT, None),
        P(FLAT, None),
        P(FLAT, None),
        P(FLAT),
        P(FLAT, None),
        P(FLAT, None),
        P(FLAT, None),
        P(FLAT, None),
        P(FLAT),
        P(FLAT, None),
        P(FLAT, None),
        P(FLAT, None),
        P("row"),
        P("row", None),
        P("row", None),
    )
    out_specs = P(FLAT, None)

    return jax.shard_map(body, mesh=mesh, in_specs=in_specs, out_specs=out_specs, check_vma=False)
```

```python
import jax
import jax.numpy as jnp
from jax import lax
from jax.experimental import pallas as pl
from jax.experimental.pallas import tpu as pltpu
from jax.sharding import PartitionSpec as P


REACH = 8
FLAT = ("row", "col")


def halos(cells, width):
    count = lax.axis_size(FLAT)
    ends = count - 1
    head = jnp.concatenate([cell[:width] for cell in cells], axis=1)
    tail = jnp.concatenate([cell[cell.shape[0] - width :] for cell in cells], axis=1)
    left = lax.ppermute(tail, FLAT, [(i, i + 1) for i in range(ends)])
    right = lax.ppermute(head, FLAT, [(i + 1, i) for i in range(ends)])
    return left, right


def doubling_gather(block, axis):
    count = lax.axis_size(axis)
    assert count & (count - 1) == 0
    me = lax.axis_index(axis)
    distance = 1
    while distance < count:
        other = lax.ppermute(block, axis, [(i, i ^ distance) for i in range(count)])
        upper = (me & distance) != 0
        block = jnp.where(
            upper, jnp.concatenate([other, block], axis=0), jnp.concatenate([block, other], axis=0)
        )
        distance *= 2
    return block


def kernel_block(left, right):
    left_square = jnp.sum(jnp.square(left.astype(jnp.float32)), axis=-1)
    right_square = jnp.sum(jnp.square(right.astype(jnp.float32)), axis=-1)
    inner = jnp.einsum("...md,...nd->...mn", left, right, preferred_element_type=jnp.float32)
    distance = left_square[..., :, None] + right_square[..., None, :] - 2.0 * inner
    return jnp.exp(distance * (-2.0 / left.shape[-1])).astype(jnp.bfloat16)


def contract_last(a, b):
    return lax.dot_general(a, b, (((1,), (1,)), ((), ())), preferred_element_type=jnp.float32)


def scaled_kernel(target, target_square, source, source_square):
    dims = target.shape[-1]
    inner = contract_last(target * jnp.asarray(4.0 / dims, target.dtype), source)
    return jnp.exp((target_square + source_square) + inner).astype(jnp.bfloat16)


def scaled_norms(cells):
    factor = (2.0 / cells.shape[-1]) ** 0.5
    assert factor * factor == 2.0 / cells.shape[-1]
    wide = cells.astype(jnp.float32) * factor
    return jnp.sum(wide * -wide, axis=-1)


def target_square_of(target):
    wide = target.astype(jnp.float32)
    return jnp.sum(wide * wide, axis=-1, keepdims=True) * (-2.0 / target.shape[-1])


def fetch_sources(index_ref, row, count, parts, buffers, sems, slot):
    for position in range(count):
        source = index_ref[row * count + position]
        for which, (halo, mine, left, own, right) in enumerate(parts):
            target = buffers[which](slot, position)
            sem = sems.at[which, slot, position]
            if left is None:
                pltpu.make_async_copy(own(source - halo), target, sem).start()
                continue

            @pl.when(source < halo)
            def _():
                pltpu.make_async_copy(left(source), target, sem).start()

            @pl.when((source >= halo) & (source < halo + mine))
            def _():
                pltpu.make_async_copy(own(source - halo), target, sem).start()

            @pl.when(source >= halo + mine)
            def _():
                pltpu.make_async_copy(right(source - halo - mine), target, sem).start()


def wait_sources(count, parts, buffers, sems, slot):
    for position in range(count):
        for which, (halo, mine, left, own, right) in enumerate(parts):
            pltpu.make_async_copy(
                own(0), buffers[which](slot, position), sems.at[which, slot, position]
            ).wait()


def rows_of(ref):
    return lambda index: ref.at[index]


def row_of(ref):
    return lambda index: ref.at[pl.ds(index, 1)]


def norm_rows(left, own, right):
    return (left.shape[0], own.shape[0], row_of(left), row_of(own), row_of(right))


def own_norms_only(own):
    return (REACH, own.shape[0], None, row_of(own), None)


def whole_rows(left, own, right):
    return (left.shape[0], own.shape[0], rows_of(left), rows_of(own), rows_of(right))


def own_rows_only(own):
    return (REACH, own.shape[0], None, rows_of(own), None)


def lane_rows(left, own, right, start, width):
    def halo_at(ref):
        return lambda index: ref.at[index, :, pl.ds(start, width)]

    return (left.shape[0], own.shape[0], halo_at(left), rows_of(own), halo_at(right))


def pipelined_sources(index_ref, count, parts, buffers, sems, leaf_of):
    step = pl.program_id(0)
    steps = pl.num_programs(0)
    slot = step % 2

    @pl.when(step == 0)
    def _():
        fetch_sources(index_ref, leaf_of(0), count, parts, buffers, sems, 0)

    @pl.when(step + 1 < steps)
    def _():
        fetch_sources(index_ref, leaf_of(step + 1), count, parts, buffers, sems, 1 - slot)

    wait_sources(count, parts, buffers, sems, slot)
    return slot


def leaf_order(leaves, edges):
    low, high = REACH, leaves - REACH
    if high <= low:
        return (lambda step: step), leaves, None
    if not edges:
        return (lambda step: step + low), high - low, None
    gap = high - low
    return (lambda step: step + gap * jnp.asarray(step >= low, jnp.int32)), leaves - gap, gap


def near_kernel(leaf_of, halo, index_ref, target_ref, *refs):
    inputs = 9 if halo else 3
    out_ref = refs[inputs]
    point_buf, weight_buf, norm_buf, sems = refs[inputs + 1 :]
    count, size, dims = point_buf.shape[1], point_buf.shape[2], point_buf.shape[3]
    if halo:
        lpw, op, rpw, ow, ln, on, rn = refs[:7]
        parts = (
            lane_rows(lpw, op, rpw, 0, dims),
            lane_rows(lpw, ow, rpw, dims, weight_buf.shape[-1]),
            norm_rows(ln, on, rn),
        )
    else:
        parts = (own_rows_only(refs[0]), own_rows_only(refs[1]), own_norms_only(refs[2]))
    buffers = (
        lambda slot, position: point_buf.at[slot, position],
        lambda slot, position: weight_buf.at[slot, position],
        lambda slot, position: norm_buf.at[slot, :, pl.ds(position * size, size)],
    )
    slot = pipelined_sources(index_ref, count, parts, buffers, sems, leaf_of)
    target = target_ref[0]
    sources = point_buf[slot].reshape(count * size, dims)
    values = weight_buf[slot].reshape(count * size, weight_buf.shape[-1])
    kernel = scaled_kernel(target, target_square_of(target), sources, norm_buf[slot])
    out_ref[0] = jnp.dot(kernel, values, preferred_element_type=jnp.float32)


def near_field(local_points, local_weights, local_norms, near_local, halo_inputs=None, previous=None, after=None):
    leaves, size, dims = local_points.shape
    rhs = local_weights.shape[-1]
    count = near_local.shape[1]
    halo = halo_inputs is not None
    leaf_of, steps, _ = leaf_order(leaves, halo)
    anywhere = pl.BlockSpec(memory_space=pl.ANY)
    if halo:
        left_pairs, right_pairs, left_norms, right_norms = halo_inputs
        inputs = (left_pairs, local_points, right_pairs, local_weights, left_norms, local_norms, right_norms, after, previous)
    else:
        inputs = (local_points, local_weights, local_norms)
    aliases = {len(inputs) + 1: 0} if previous is not None else {}
    by_leaf = lambda step, index: (leaf_of(step), 0, 0)
    return pl.pallas_call(
        lambda *refs: near_kernel(leaf_of, halo, *refs),
        grid_spec=pltpu.PrefetchScalarGridSpec(
            num_scalar_prefetch=1,
            grid=(steps,),
            in_specs=[pl.BlockSpec((1, size, dims), by_leaf)] + [anywhere] * len(inputs),
            out_specs=pl.BlockSpec((1, size, rhs), by_leaf),
            scratch_shapes=[
                pltpu.VMEM((2, count, size, dims), local_points.dtype),
                pltpu.VMEM((2, count, size, rhs), local_weights.dtype),
                pltpu.VMEM((2, 1, count * size), jnp.float32),
                pltpu.SemaphoreType.DMA((3, 2, count)),
            ],
        ),
        out_shape=jax.ShapeDtypeStruct((leaves, size, rhs), jnp.float32),
        input_output_aliases=aliases,
        compiler_params=pltpu.CompilerParams(dimension_semantics=("arbitrary",)),
    )(near_local.reshape(-1), local_points, *inputs)


def far_kernel(leaf_of, halo, index_ref, target_ref, *refs):
    inputs = 7 if halo else 2
    out_ref = refs[inputs]
    source_buf, norm_buf, sems = refs[inputs + 1 :]
    count, rank = source_buf.shape[1], source_buf.shape[2]
    if halo:
        ls, os, rs, ln, on, rn = refs[:6]
        parts = (whole_rows(ls, os, rs), norm_rows(ln, on, rn))
    else:
        parts = (own_rows_only(refs[0]), own_norms_only(refs[1]))
    buffers = (
        lambda slot, position: source_buf.at[slot, position],
        lambda slot, position: norm_buf.at[slot, :, pl.ds(position * rank, rank)],
    )
    slot = pipelined_sources(index_ref, count, parts, buffers, sems, leaf_of)
    target = target_ref[0]
    dims = target.shape[-1]
    sources = source_buf[slot].reshape(count * rank, source_buf.shape[-1])
    kernel = scaled_kernel(target, target_square_of(target), sources[:, :dims], norm_buf[slot])
    out_ref[0] = jnp.dot(kernel, sources[:, dims:], preferred_element_type=jnp.float32)


def far_field(leaf_coords, own_rows, own_norms, far_local, halo_inputs=None, previous=None):
    leaves, rank, dims = leaf_coords.shape
    width = own_rows.shape[-1]
    count = far_local.shape[1]
    halo = halo_inputs is not None
    leaf_of, steps, _ = leaf_order(leaves, halo)
    anywhere = pl.BlockSpec(memory_space=pl.ANY)
    if halo:
        left_rows, right_rows, left_norms, right_norms = halo_inputs
        inputs = (left_rows, own_rows, right_rows, left_norms, own_norms, right_norms, previous)
    else:
        inputs = (own_rows, own_norms)
    aliases = {len(inputs) + 1: 0} if previous is not None else {}
    by_leaf = lambda step, index: (leaf_of(step), 0, 0)
    return pl.pallas_call(
        lambda *refs: far_kernel(leaf_of, halo, *refs),
        grid_spec=pltpu.PrefetchScalarGridSpec(
            num_scalar_prefetch=1,
            grid=(steps,),
            in_specs=[pl.BlockSpec((1, rank, dims), by_leaf)] + [anywhere] * len(inputs),
            out_specs=pl.BlockSpec((1, rank, width - dims), by_leaf),
            scratch_shapes=[
                pltpu.VMEM((2, count, rank, width), own_rows.dtype),
                pltpu.VMEM((2, 1, count * rank), jnp.float32),
                pltpu.SemaphoreType.DMA((2, 2, count)),
            ],
        ),
        out_shape=jax.ShapeDtypeStruct((leaves, rank, width - dims), jnp.float32),
        input_output_aliases=aliases,
        compiler_params=pltpu.CompilerParams(dimension_semantics=("arbitrary",)),
    )(far_local.reshape(-1), leaf_coords, *inputs)


def final_kernel(rank_ref, basis_ref, down_ref, far_ref, leaf_base_ref, near_ref, out_ref):
    block = basis_ref.shape[0]
    step = pl.program_id(0)
    down = down_ref[...]
    for inside in range(block):
        total = jnp.dot(basis_ref[inside], down, preferred_element_type=jnp.float32) + far_ref[inside]
        rows = lax.broadcasted_iota(jnp.int32, total.shape, 0)
        leaf_down = jnp.where(rows < rank_ref[step * block + inside], total, 0.0).astype(jnp.bfloat16)
        result = (
            jnp.dot(leaf_base_ref[inside], leaf_down, preferred_element_type=jnp.float32)
            + near_ref[inside]
        )
        out_ref[inside] = result.astype(out_ref.dtype)


def final_field(leaf_rank, bases, node_down, far_total, leaf_bases, near_total):
    leaves, rank, width = bases.shape
    size = leaf_bases.shape[1]
    rhs = near_total.shape[-1]
    block = max(b for b in (1, 2, 3, 4) if leaves % b == 0)

    def own(l, ranks):
        return (l, 0, 0)

    return pl.pallas_call(
        final_kernel,
        grid_spec=pltpu.PrefetchScalarGridSpec(
            num_scalar_prefetch=1,
            grid=(leaves // block,),
            in_specs=[
                pl.BlockSpec((block, rank, width), own),
                pl.BlockSpec(node_down.shape, lambda l, ranks: (0, 0)),
                pl.BlockSpec((block, rank, rhs), own),
                pl.BlockSpec((block, size, rank), own),
                pl.BlockSpec((block, size, rhs), own),
            ],
            out_specs=pl.BlockSpec((block, size, rhs), own),
        ),
        out_shape=jax.ShapeDtypeStruct((leaves, size, rhs), jnp.bfloat16),
    )(leaf_rank, bases, node_down, far_total, leaf_bases, near_total)


def select_rows(table, index):
    count = table.shape[0]
    onehot = (index[:, None] == jnp.arange(count, dtype=jnp.int32)[None, :]).astype(table.dtype)
    picked = jnp.dot(onehot, table.reshape(count, -1), preferred_element_type=jnp.float32).astype(
        table.dtype
    )
    return picked.reshape(index.shape + table.shape[1:])


def select_within(table, index):
    count = table.shape[1]
    onehot = (index[:, :, None] == jnp.arange(count, dtype=jnp.int32)[None, None, :]).astype(
        table.dtype
    )
    return jnp.einsum("bkp,bpc->bkc", onehot, table, preferred_element_type=jnp.float32).astype(
        table.dtype
    )


def body(
    points,
    weights,
    leaf_basis,
    leaf_rank,
    leaf_skeleton,
    near_list,
    far_list,
    node_basis,
    node_rank,
    node_skeleton,
    node_far,
    group_basis,
    group_rank,
    group_skeleton,
    group_far,
):
    leaf_count = leaf_rank.shape[0]
    leaf_size = points.shape[0] // leaf_count
    dim_count = points.shape[1]
    rhs_count = weights.shape[1]
    rank_count = leaf_basis.shape[1]
    node_width = node_basis.shape[1]
    group_width = group_basis.shape[1]
    local_points = points.reshape(leaf_count, leaf_size, dim_count)
    local_bases = leaf_basis.reshape(leaf_count, leaf_size, rank_count)
    local_weights = weights.reshape(leaf_count, leaf_size, rhs_count)
    first_leaf = lax.axis_index(FLAT) * leaf_count
    offset = first_leaf - REACH

    left_pairs, right_pairs = halos((points, weights), REACH * leaf_size)
    left_pairs = left_pairs.reshape(REACH, leaf_size, dim_count + rhs_count)
    right_pairs = right_pairs.reshape(REACH, leaf_size, dim_count + rhs_count)

    leaf_mask = (
        lax.broadcasted_iota(jnp.int32, (leaf_count, rank_count), 1) < leaf_rank[:, None]
    ).astype(jnp.float32)
    leaf_up = (
        jnp.einsum("lpk,lpr->lkr", local_bases, local_weights, preferred_element_type=jnp.float32)
        * leaf_mask[:, :, None]
    ).astype(jnp.bfloat16)
    leaf_coords = select_within(local_points, leaf_skeleton)
    own_rows = jnp.concatenate([leaf_coords, leaf_up], axis=-1)
    skeleton_width = dim_count + rhs_count
    left_rows, right_rows = halos(
        (own_rows.reshape(leaf_count * rank_count, skeleton_width),), REACH * rank_count
    )

    node_mask = (jnp.arange(node_width, dtype=jnp.int32) < node_rank[0]).astype(jnp.float32)
    node_up = (
        jnp.einsum(
            "ak,ar->kr",
            node_basis,
            leaf_up.reshape(leaf_count * rank_count, rhs_count),
            preferred_element_type=jnp.float32,
        )
        * node_mask[:, None]
    ).astype(jnp.bfloat16)
    node_coords = select_rows(
        leaf_coords.reshape(leaf_count * rank_count, dim_count), node_skeleton[0]
    )
    columns = lax.axis_size("col")
    source_columns = node_far[0] % columns
    node_pack = jnp.concatenate([node_coords, node_up, group_basis], axis=1)
    gathered = doubling_gather(node_pack[None], "col")

    near_local = near_list - offset
    local_norms = scaled_norms(local_points)
    near_inner = near_field(local_points, local_weights, local_norms, near_local)
    all_coords = gathered[:, :, :dim_count]
    all_up = gathered[:, :, dim_count : dim_count + rhs_count]
    all_parts = gathered[:, :, dim_count + rhs_count :]
    picked_coords = select_rows(all_coords, source_columns)
    picked_up = select_rows(all_up, source_columns)
    kernel = kernel_block(jnp.broadcast_to(node_coords, picked_coords.shape), picked_coords)
    node_side = jnp.einsum("fab,fbr->ar", kernel, picked_up, preferred_element_type=jnp.float32)
    group_mask = (jnp.arange(group_width, dtype=jnp.int32) < group_rank[0]).astype(jnp.float32)
    group_up = (
        jnp.einsum("nag,nar->gr", all_parts, all_up, preferred_element_type=jnp.float32)
        * group_mask[:, None]
    ).astype(jnp.bfloat16)
    group_coords = select_rows(all_coords.reshape(columns * node_width, dim_count), group_skeleton[0])
    group_pack = jnp.concatenate([group_coords, group_up], axis=1)
    near_total = near_field(
        local_points,
        local_weights,
        local_norms,
        near_local,
        (
            left_pairs,
            right_pairs,
            scaled_norms(left_pairs[:, :, :dim_count]),
            scaled_norms(right_pairs[:, :, :dim_count]),
        ),
        near_inner,
        group_pack,
    )
    near_total, left_rows, right_rows = lax.optimization_barrier((near_total, left_rows, right_rows))

    left_rows = left_rows.reshape(REACH, rank_count, skeleton_width)
    right_rows = right_rows.reshape(REACH, rank_count, skeleton_width)
    far_local = far_list - offset
    coord_norms = scaled_norms(leaf_coords)
    far_inner = far_field(leaf_coords, own_rows, coord_norms, far_local)
    far_total = far_field(
        leaf_coords,
        own_rows,
        coord_norms,
        far_local,
        (
            left_rows,
            right_rows,
            scaled_norms(left_rows[:, :, :dim_count]),
            scaled_norms(right_rows[:, :, :dim_count]),
        ),
        far_inner,
    )
    rows = lax.axis_size("row")
    received = [group_pack] + [
        lax.ppermute(group_pack, "row", [(r, (r + shift) % rows) for r in range(rows)])
        for shift in range(1, rows)
    ]
    shifts = (lax.axis_index("row") - group_far[0]) % rows
    picked_group = select_rows(jnp.stack(received), shifts)
    picked_group_coords = picked_group[:, :, :dim_count]
    picked_group_up = picked_group[:, :, dim_count:]
    group_kernel = kernel_block(
        jnp.broadcast_to(group_coords, picked_group_coords.shape), picked_group_coords
    )
    group_down = (
        jnp.einsum("fab,fbr->ar", group_kernel, picked_group_up, preferred_element_type=jnp.float32)
        * group_mask[:, None]
    ).astype(jnp.bfloat16)
    node_down = (
        (jnp.dot(group_basis, group_down, preferred_element_type=jnp.float32) + node_side)
        * node_mask[:, None]
    ).astype(jnp.bfloat16)
    result = final_field(
        leaf_rank,
        node_basis.reshape(leaf_count, rank_count, node_width),
        node_down,
        far_total,
        local_bases,
        near_total,
    )
    return result.reshape(leaf_count * leaf_size, rhs_count)


def solution(mesh):
    in_specs = (
        P(FLAT, None),
        P(FLAT, None),
        P(FLAT, None),
        P(FLAT),
        P(FLAT, None),
        P(FLAT, None),
        P(FLAT, None),
        P(FLAT, None),
        P(FLAT),
        P(FLAT, None),
        P(FLAT, None),
        P(FLAT, None),
        P("row"),
        P("row", None),
        P("row", None),
    )
    out_specs = P(FLAT, None)

    return jax.shard_map(body, mesh=mesh, in_specs=in_specs, out_specs=out_specs, check_vma=False)
```

```python
import jax
import jax.numpy as jnp
from jax import lax
from jax.experimental import pallas as pl
from jax.experimental.pallas import tpu as pltpu
from jax.sharding import PartitionSpec as P


REACH = 8
FLAT = ("row", "col")


def halos(cells, width):
    count = lax.axis_size(FLAT)
    ends = count - 1
    head = jnp.concatenate([cell[:width] for cell in cells], axis=1)
    tail = jnp.concatenate([cell[cell.shape[0] - width :] for cell in cells], axis=1)
    left = lax.ppermute(tail, FLAT, [(i, i + 1) for i in range(ends)])
    right = lax.ppermute(head, FLAT, [(i + 1, i) for i in range(ends)])
    return left, right


def kernel_block(left, right):
    left_square = jnp.sum(jnp.square(left.astype(jnp.float32)), axis=-1)
    right_square = jnp.sum(jnp.square(right.astype(jnp.float32)), axis=-1)
    inner = jnp.einsum("...md,...nd->...mn", left, right, preferred_element_type=jnp.float32)
    distance = left_square[..., :, None] + right_square[..., None, :] - 2.0 * inner
    return jnp.exp(distance * (-2.0 / left.shape[-1])).astype(jnp.bfloat16)


def contract_last(a, b):
    return lax.dot_general(a, b, (((1,), (1,)), ((), ())), preferred_element_type=jnp.float32)


def scaled_kernel(target, target_square, source, source_square=None):
    dims = target.shape[-1]
    if source_square is None:
        wide = source.astype(jnp.float32)
        square = wide * wide
        high = square.astype(jnp.bfloat16)
        low = (square - high.astype(jnp.float32)).astype(jnp.bfloat16)
        ones = jnp.ones((8, dims), jnp.bfloat16)
        summed = contract_last(ones, high) + contract_last(ones, low)
        source_square = summed[0:1] * (-2.0 / dims)
    inner = contract_last(target * jnp.asarray(4.0 / dims, target.dtype), source)
    return jnp.exp((target_square + source_square) + inner).astype(jnp.bfloat16)


def scaled_norms(cells):
    factor = (2.0 / cells.shape[-1]) ** 0.5
    assert factor * factor == 2.0 / cells.shape[-1]
    wide = cells.astype(jnp.float32) * factor
    return jnp.sum(wide * -wide, axis=-1)


def target_square_of(target):
    wide = target.astype(jnp.float32)
    return jnp.sum(wide * wide, axis=-1, keepdims=True) * (-2.0 / target.shape[-1])


def fetch_sources(index_ref, row, count, parts, buffers, sems, slot):
    for position in range(count):
        source = index_ref[row * count + position]
        for which, (halo, mine, left, own, right) in enumerate(parts):
            target = buffers[which](slot, position)
            sem = sems.at[which, slot, position]
            if left is None:
                pltpu.make_async_copy(own(source - halo), target, sem).start()
                continue

            @pl.when(source < halo)
            def _():
                pltpu.make_async_copy(left(source), target, sem).start()

            @pl.when((source >= halo) & (source < halo + mine))
            def _():
                pltpu.make_async_copy(own(source - halo), target, sem).start()

            @pl.when(source >= halo + mine)
            def _():
                pltpu.make_async_copy(right(source - halo - mine), target, sem).start()


def wait_sources(count, parts, buffers, sems, slot):
    for position in range(count):
        for which, (halo, mine, left, own, right) in enumerate(parts):
            pltpu.make_async_copy(
                own(0), buffers[which](slot, position), sems.at[which, slot, position]
            ).wait()


def rows_of(ref):
    return lambda index: ref.at[index]


def row_of(ref):
    return lambda index: ref.at[pl.ds(index, 1)]


def own_norms_only(own):
    return (REACH, own.shape[0], None, row_of(own), None)


def whole_rows(left, own, right):
    return (left.shape[0], own.shape[0], rows_of(left), rows_of(own), rows_of(right))


def own_rows_only(own):
    return (REACH, own.shape[0], None, rows_of(own), None)


def lane_rows(left, own, right, start, width):
    def halo_at(ref):
        return lambda index: ref.at[index, :, pl.ds(start, width)]

    return (left.shape[0], own.shape[0], halo_at(left), rows_of(own), halo_at(right))


def pipelined_sources(index_ref, count, parts, buffers, sems, leaf_of):
    step = pl.program_id(0)
    steps = pl.num_programs(0)
    slot = step % 2

    @pl.when(step == 0)
    def _():
        fetch_sources(index_ref, leaf_of(0), count, parts, buffers, sems, 0)

    @pl.when(step + 1 < steps)
    def _():
        fetch_sources(index_ref, leaf_of(step + 1), count, parts, buffers, sems, 1 - slot)

    wait_sources(count, parts, buffers, sems, slot)
    return slot


def leaf_order(leaves, edges):
    low, high = REACH, leaves - REACH
    if high <= low:
        return (lambda step: step), leaves, None
    if not edges:
        return (lambda step: step + low), high - low, None
    gap = high - low
    return (lambda step: step + gap * jnp.asarray(step >= low, jnp.int32)), leaves - gap, gap


def near_kernel(leaf_of, halo, index_ref, target_ref, *refs):
    inputs = 6 if halo else 3
    out_ref = refs[inputs]
    point_buf, weight_buf, norm_buf, sems = refs[inputs + 1 :]
    count, size, dims = point_buf.shape[1], point_buf.shape[2], point_buf.shape[3]
    buffers = [
        lambda slot, position: point_buf.at[slot, position],
        lambda slot, position: weight_buf.at[slot, position],
    ]
    if halo:
        lpw, op, rpw, ow = refs[:4]
        parts = (
            lane_rows(lpw, op, rpw, 0, dims),
            lane_rows(lpw, ow, rpw, dims, weight_buf.shape[-1]),
        )
    else:
        parts = (own_rows_only(refs[0]), own_rows_only(refs[1]), own_norms_only(refs[2]))
        buffers.append(lambda slot, position: norm_buf.at[slot, :, pl.ds(position * size, size)])
    slot = pipelined_sources(index_ref, count, parts, buffers, sems, leaf_of)
    target = target_ref[0]
    sources = point_buf[slot].reshape(count * size, dims)
    values = weight_buf[slot].reshape(count * size, weight_buf.shape[-1])
    kernel = scaled_kernel(target, target_square_of(target), sources, None if halo else norm_buf[slot])
    out_ref[0] = jnp.dot(kernel, values, preferred_element_type=jnp.float32)


def near_field(local_points, local_weights, local_norms, near_local, halo_inputs=None, previous=None, after=None):
    leaves, size, dims = local_points.shape
    rhs = local_weights.shape[-1]
    count = near_local.shape[1]
    halo = halo_inputs is not None
    leaf_of, steps, _ = leaf_order(leaves, halo)
    anywhere = pl.BlockSpec(memory_space=pl.ANY)
    if halo:
        left_pairs, right_pairs = halo_inputs
        inputs = (left_pairs, local_points, right_pairs, local_weights, after, previous)
    else:
        inputs = (local_points, local_weights, local_norms)
    aliases = {len(inputs) + 1: 0} if previous is not None else {}
    by_leaf = lambda step, index: (leaf_of(step), 0, 0)
    return pl.pallas_call(
        lambda *refs: near_kernel(leaf_of, halo, *refs),
        grid_spec=pltpu.PrefetchScalarGridSpec(
            num_scalar_prefetch=1,
            grid=(steps,),
            in_specs=[pl.BlockSpec((1, size, dims), by_leaf)] + [anywhere] * len(inputs),
            out_specs=pl.BlockSpec((1, size, rhs), by_leaf),
            scratch_shapes=[
                pltpu.VMEM((2, count, size, dims), local_points.dtype),
                pltpu.VMEM((2, count, size, rhs), local_weights.dtype),
                pltpu.VMEM((2, 1, count * size), jnp.float32),
                pltpu.SemaphoreType.DMA((3, 2, count)),
            ],
        ),
        out_shape=jax.ShapeDtypeStruct((leaves, size, rhs), jnp.float32),
        input_output_aliases=aliases,
        compiler_params=pltpu.CompilerParams(dimension_semantics=("arbitrary",)),
    )(near_local.reshape(-1), local_points, *inputs)


def far_kernel(leaf_of, halo, index_ref, target_ref, *refs):
    inputs = 4 if halo else 2
    out_ref = refs[inputs]
    source_buf, norm_buf, sems = refs[inputs + 1 :]
    count, rank = source_buf.shape[1], source_buf.shape[2]
    buffers = [lambda slot, position: source_buf.at[slot, position]]
    if halo:
        ls, os, rs = refs[:3]
        parts = (whole_rows(ls, os, rs),)
    else:
        parts = (own_rows_only(refs[0]), own_norms_only(refs[1]))
        buffers.append(lambda slot, position: norm_buf.at[slot, :, pl.ds(position * rank, rank)])
    slot = pipelined_sources(index_ref, count, parts, buffers, sems, leaf_of)
    target = target_ref[0]
    dims = target.shape[-1]
    sources = source_buf[slot].reshape(count * rank, source_buf.shape[-1])
    kernel = scaled_kernel(
        target, target_square_of(target), sources[:, :dims], None if halo else norm_buf[slot]
    )
    out_ref[0] = jnp.dot(kernel, sources[:, dims:], preferred_element_type=jnp.float32)


def far_field(leaf_coords, own_rows, own_norms, far_local, halo_inputs=None, previous=None):
    leaves, rank, dims = leaf_coords.shape
    width = own_rows.shape[-1]
    count = far_local.shape[1]
    halo = halo_inputs is not None
    leaf_of, steps, _ = leaf_order(leaves, halo)
    anywhere = pl.BlockSpec(memory_space=pl.ANY)
    if halo:
        left_rows, right_rows = halo_inputs
        inputs = (left_rows, own_rows, right_rows, previous)
    else:
        inputs = (own_rows, own_norms)
    aliases = {len(inputs) + 1: 0} if previous is not None else {}
    by_leaf = lambda step, index: (leaf_of(step), 0, 0)
    return pl.pallas_call(
        lambda *refs: far_kernel(leaf_of, halo, *refs),
        grid_spec=pltpu.PrefetchScalarGridSpec(
            num_scalar_prefetch=1,
            grid=(steps,),
            in_specs=[pl.BlockSpec((1, rank, dims), by_leaf)] + [anywhere] * len(inputs),
            out_specs=pl.BlockSpec((1, rank, width - dims), by_leaf),
            scratch_shapes=[
                pltpu.VMEM((2, count, rank, width), own_rows.dtype),
                pltpu.VMEM((2, 1, count * rank), jnp.float32),
                pltpu.SemaphoreType.DMA((2, 2, count)),
            ],
        ),
        out_shape=jax.ShapeDtypeStruct((leaves, rank, width - dims), jnp.float32),
        input_output_aliases=aliases,
        compiler_params=pltpu.CompilerParams(dimension_semantics=("arbitrary",)),
    )(far_local.reshape(-1), leaf_coords, *inputs)


def final_kernel(rank_ref, basis_ref, down_ref, far_ref, leaf_base_ref, near_ref, out_ref):
    block = basis_ref.shape[0]
    step = pl.program_id(0)
    down = down_ref[...]
    for inside in range(block):
        total = jnp.dot(basis_ref[inside], down, preferred_element_type=jnp.float32) + far_ref[inside]
        rows = lax.broadcasted_iota(jnp.int32, total.shape, 0)
        leaf_down = jnp.where(rows < rank_ref[step * block + inside], total, 0.0).astype(jnp.bfloat16)
        result = (
            jnp.dot(leaf_base_ref[inside], leaf_down, preferred_element_type=jnp.float32)
            + near_ref[inside]
        )
        out_ref[inside] = result.astype(out_ref.dtype)


def final_field(leaf_rank, bases, node_down, far_total, leaf_bases, near_total):
    leaves, rank, width = bases.shape
    size = leaf_bases.shape[1]
    rhs = near_total.shape[-1]
    block = max(b for b in (1, 2, 3, 4) if leaves % b == 0)

    def own(l, ranks):
        return (l, 0, 0)

    return pl.pallas_call(
        final_kernel,
        grid_spec=pltpu.PrefetchScalarGridSpec(
            num_scalar_prefetch=1,
            grid=(leaves // block,),
            in_specs=[
                pl.BlockSpec((block, rank, width), own),
                pl.BlockSpec(node_down.shape, lambda l, ranks: (0, 0)),
                pl.BlockSpec((block, rank, rhs), own),
                pl.BlockSpec((block, size, rank), own),
                pl.BlockSpec((block, size, rhs), own),
            ],
            out_specs=pl.BlockSpec((block, size, rhs), own),
        ),
        out_shape=jax.ShapeDtypeStruct((leaves, size, rhs), jnp.bfloat16),
    )(leaf_rank, bases, node_down, far_total, leaf_bases, near_total)


def select_rows(table, index):
    count = table.shape[0]
    onehot = (index[:, None] == jnp.arange(count, dtype=jnp.int32)[None, :]).astype(table.dtype)
    picked = jnp.dot(onehot, table.reshape(count, -1), preferred_element_type=jnp.float32).astype(
        table.dtype
    )
    return picked.reshape(index.shape + table.shape[1:])


def select_within(table, index):
    count = table.shape[1]
    onehot = (index[:, :, None] == jnp.arange(count, dtype=jnp.int32)[None, None, :]).astype(
        table.dtype
    )
    return jnp.einsum("bkp,bpc->bkc", onehot, table, preferred_element_type=jnp.float32).astype(
        table.dtype
    )


def body(
    points,
    weights,
    leaf_basis,
    leaf_rank,
    leaf_skeleton,
    near_list,
    far_list,
    node_basis,
    node_rank,
    node_skeleton,
    node_far,
    group_basis,
    group_rank,
    group_skeleton,
    group_far,
):
    leaf_count = leaf_rank.shape[0]
    leaf_size = points.shape[0] // leaf_count
    dim_count = points.shape[1]
    rhs_count = weights.shape[1]
    rank_count = leaf_basis.shape[1]
    node_width = node_basis.shape[1]
    group_width = group_basis.shape[1]
    local_points = points.reshape(leaf_count, leaf_size, dim_count)
    local_bases = leaf_basis.reshape(leaf_count, leaf_size, rank_count)
    local_weights = weights.reshape(leaf_count, leaf_size, rhs_count)
    first_leaf = lax.axis_index(FLAT) * leaf_count
    offset = first_leaf - REACH

    left_pairs, right_pairs = halos((points, weights), REACH * leaf_size)
    left_pairs = left_pairs.reshape(REACH, leaf_size, dim_count + rhs_count)
    right_pairs = right_pairs.reshape(REACH, leaf_size, dim_count + rhs_count)

    leaf_mask = (
        lax.broadcasted_iota(jnp.int32, (leaf_count, rank_count), 1) < leaf_rank[:, None]
    ).astype(jnp.float32)
    leaf_up = (
        jnp.einsum("lpk,lpr->lkr", local_bases, local_weights, preferred_element_type=jnp.float32)
        * leaf_mask[:, :, None]
    ).astype(jnp.bfloat16)
    leaf_coords = select_within(local_points, leaf_skeleton)
    own_rows = jnp.concatenate([leaf_coords, leaf_up], axis=-1)
    skeleton_width = dim_count + rhs_count
    left_rows, right_rows = halos(
        (own_rows.reshape(leaf_count * rank_count, skeleton_width),), REACH * rank_count
    )

    node_mask = (jnp.arange(node_width, dtype=jnp.int32) < node_rank[0]).astype(jnp.float32)
    node_up = (
        jnp.einsum(
            "ak,ar->kr",
            node_basis,
            leaf_up.reshape(leaf_count * rank_count, rhs_count),
            preferred_element_type=jnp.float32,
        )
        * node_mask[:, None]
    ).astype(jnp.bfloat16)
    node_coords = select_rows(
        leaf_coords.reshape(leaf_count * rank_count, dim_count), node_skeleton[0]
    )
    columns = lax.axis_size("col")
    source_columns = node_far[0] % columns
    node_pack = jnp.concatenate([node_coords, node_up, group_basis], axis=1)
    gathered = lax.all_gather(node_pack[None], "col", axis=0, tiled=True)

    near_local = near_list - offset
    local_norms = scaled_norms(local_points)
    near_inner = near_field(local_points, local_weights, local_norms, near_local)
    all_coords = gathered[:, :, :dim_count]
    all_up = gathered[:, :, dim_count : dim_count + rhs_count]
    all_parts = gathered[:, :, dim_count + rhs_count :]
    picked_coords = select_rows(all_coords, source_columns)
    picked_up = select_rows(all_up, source_columns)
    kernel = kernel_block(jnp.broadcast_to(node_coords, picked_coords.shape), picked_coords)
    node_side = jnp.einsum("fab,fbr->ar", kernel, picked_up, preferred_element_type=jnp.float32)
    group_mask = (jnp.arange(group_width, dtype=jnp.int32) < group_rank[0]).astype(jnp.float32)
    group_up = (
        jnp.einsum("nag,nar->gr", all_parts, all_up, preferred_element_type=jnp.float32)
        * group_mask[:, None]
    ).astype(jnp.bfloat16)
    group_coords = select_rows(all_coords.reshape(columns * node_width, dim_count), group_skeleton[0])
    group_pack = jnp.concatenate([group_coords, group_up], axis=1)
    near_total = near_field(
        local_points,
        local_weights,
        local_norms,
        near_local,
        (left_pairs, right_pairs),
        near_inner,
        group_pack,
    )
    near_total, left_rows, right_rows = lax.optimization_barrier((near_total, left_rows, right_rows))

    left_rows = left_rows.reshape(REACH, rank_count, skeleton_width)
    right_rows = right_rows.reshape(REACH, rank_count, skeleton_width)
    far_local = far_list - offset
    coord_norms = scaled_norms(leaf_coords)
    far_inner = far_field(leaf_coords, own_rows, coord_norms, far_local)
    far_total = far_field(
        leaf_coords,
        own_rows,
        coord_norms,
        far_local,
        (left_rows, right_rows),
        far_inner,
    )
    rows = lax.axis_size("row")
    received = [group_pack] + [
        lax.ppermute(group_pack, "row", [(r, (r + shift) % rows) for r in range(rows)])
        for shift in range(1, rows)
    ]
    shifts = (lax.axis_index("row") - group_far[0]) % rows
    picked_group = select_rows(jnp.stack(received), shifts)
    picked_group_coords = picked_group[:, :, :dim_count]
    picked_group_up = picked_group[:, :, dim_count:]
    group_kernel = kernel_block(
        jnp.broadcast_to(group_coords, picked_group_coords.shape), picked_group_coords
    )
    group_down = (
        jnp.einsum("fab,fbr->ar", group_kernel, picked_group_up, preferred_element_type=jnp.float32)
        * group_mask[:, None]
    ).astype(jnp.bfloat16)
    node_down = (
        (jnp.dot(group_basis, group_down, preferred_element_type=jnp.float32) + node_side)
        * node_mask[:, None]
    ).astype(jnp.bfloat16)
    result = final_field(
        leaf_rank,
        node_basis.reshape(leaf_count, rank_count, node_width),
        node_down,
        far_total,
        local_bases,
        near_total,
    )
    return result.reshape(leaf_count * leaf_size, rhs_count)


def solution(mesh):
    in_specs = (
        P(FLAT, None),
        P(FLAT, None),
        P(FLAT, None),
        P(FLAT),
        P(FLAT, None),
        P(FLAT, None),
        P(FLAT, None),
        P(FLAT, None),
        P(FLAT),
        P(FLAT, None),
        P(FLAT, None),
        P(FLAT, None),
        P("row"),
        P("row", None),
        P("row", None),
    )
    out_specs = P(FLAT, None)

    return jax.shard_map(body, mesh=mesh, in_specs=in_specs, out_specs=out_specs, check_vma=False)
```

```python
import jax
import jax.numpy as jnp
from jax import lax
from jax.experimental import pallas as pl
from jax.experimental.pallas import tpu as pltpu
from jax.sharding import PartitionSpec as P


REACH = 8
FLAT = ("row", "col")


def halos(cells, width):
    count = lax.axis_size(FLAT)
    ends = count - 1
    head = jnp.concatenate([cell[:width] for cell in cells], axis=1)
    tail = jnp.concatenate([cell[cell.shape[0] - width :] for cell in cells], axis=1)
    left = lax.ppermute(tail, FLAT, [(i, i + 1) for i in range(ends)])
    right = lax.ppermute(head, FLAT, [(i + 1, i) for i in range(ends)])
    return left, right


def kernel_block(left, right):
    left_square = jnp.sum(jnp.square(left.astype(jnp.float32)), axis=-1)
    right_square = jnp.sum(jnp.square(right.astype(jnp.float32)), axis=-1)
    inner = jnp.einsum("...md,...nd->...mn", left, right, preferred_element_type=jnp.float32)
    distance = left_square[..., :, None] + right_square[..., None, :] - 2.0 * inner
    return jnp.exp(distance * (-2.0 / left.shape[-1])).astype(jnp.bfloat16)


def contract_last(a, b):
    return lax.dot_general(a, b, (((1,), (1,)), ((), ())), preferred_element_type=jnp.float32)


def scaled_kernel(target, target_square, source, source_square=None):
    dims = target.shape[-1]
    if source_square is None:
        wide = source.astype(jnp.float32)
        square = wide * wide
        high = square.astype(jnp.bfloat16)
        low = (square - high.astype(jnp.float32)).astype(jnp.bfloat16)
        ones = jnp.ones((8, dims), jnp.bfloat16)
        summed = contract_last(ones, high) + contract_last(ones, low)
        source_square = summed[0:1] * (-2.0 / dims)
    inner = contract_last(target * jnp.asarray(4.0 / dims, target.dtype), source)
    return jnp.exp((target_square + source_square) + inner).astype(jnp.bfloat16)


def scaled_norms(cells):
    factor = (2.0 / cells.shape[-1]) ** 0.5
    assert factor * factor == 2.0 / cells.shape[-1]
    wide = cells.astype(jnp.float32) * factor
    return jnp.sum(wide * -wide, axis=-1)


def target_square_of(target):
    wide = target.astype(jnp.float32)
    return jnp.sum(wide * wide, axis=-1, keepdims=True) * (-2.0 / target.shape[-1])


def fetch_sources(index_ref, row, count, parts, buffers, sems, slot):
    for position in range(count):
        source = index_ref[row * count + position]
        for which, (halo, mine, left, own, right) in enumerate(parts):
            target = buffers[which](slot, position)
            sem = sems.at[which, slot, position]
            if left is None:
                pltpu.make_async_copy(own(source - halo), target, sem).start()
                continue

            @pl.when(source < halo)
            def _():
                pltpu.make_async_copy(left(source), target, sem).start()

            @pl.when((source >= halo) & (source < halo + mine))
            def _():
                pltpu.make_async_copy(own(source - halo), target, sem).start()

            @pl.when(source >= halo + mine)
            def _():
                pltpu.make_async_copy(right(source - halo - mine), target, sem).start()


def wait_sources(count, parts, buffers, sems, slot):
    for position in range(count):
        for which, (halo, mine, left, own, right) in enumerate(parts):
            pltpu.make_async_copy(
                own(0), buffers[which](slot, position), sems.at[which, slot, position]
            ).wait()


def rows_of(ref):
    return lambda index: ref.at[index]


def row_of(ref):
    return lambda index: ref.at[pl.ds(index, 1)]


def own_norms_only(own):
    return (REACH, own.shape[0], None, row_of(own), None)


def whole_rows(left, own, right):
    return (left.shape[0], own.shape[0], rows_of(left), rows_of(own), rows_of(right))


def own_rows_only(own):
    return (REACH, own.shape[0], None, rows_of(own), None)


def lane_rows(left, own, right, start, width):
    def halo_at(ref):
        return lambda index: ref.at[index, :, pl.ds(start, width)]

    return (left.shape[0], own.shape[0], halo_at(left), rows_of(own), halo_at(right))


def pipelined_sources(index_ref, count, parts, buffers, sems, leaf_of):
    step = pl.program_id(0)
    steps = pl.num_programs(0)
    slot = step % 2

    @pl.when(step == 0)
    def _():
        fetch_sources(index_ref, leaf_of(0), count, parts, buffers, sems, 0)

    @pl.when(step + 1 < steps)
    def _():
        fetch_sources(index_ref, leaf_of(step + 1), count, parts, buffers, sems, 1 - slot)

    wait_sources(count, parts, buffers, sems, slot)
    return slot


def leaf_order(leaves, edges):
    low, high = REACH, leaves - REACH
    if high <= low:
        return (lambda step: step), leaves, None
    if not edges:
        return (lambda step: step + low), high - low, None
    gap = high - low
    return (lambda step: step + gap * jnp.asarray(step >= low, jnp.int32)), leaves - gap, gap


def near_kernel(leaf_of, halo, index_ref, target_ref, *refs):
    inputs = 5 if halo else 3
    out_ref = refs[inputs]
    point_buf, weight_buf, norm_buf, sems = refs[inputs + 1 :]
    count, size, dims = point_buf.shape[1], point_buf.shape[2], point_buf.shape[3]
    buffers = [
        lambda slot, position: point_buf.at[slot, position],
        lambda slot, position: weight_buf.at[slot, position],
    ]
    if halo:
        lpw, op, rpw, ow = refs[:4]
        parts = (
            lane_rows(lpw, op, rpw, 0, dims),
            lane_rows(lpw, ow, rpw, dims, weight_buf.shape[-1]),
        )
    else:
        parts = (own_rows_only(refs[0]), own_rows_only(refs[1]), own_norms_only(refs[2]))
        buffers.append(lambda slot, position: norm_buf.at[slot, :, pl.ds(position * size, size)])
    slot = pipelined_sources(index_ref, count, parts, buffers, sems, leaf_of)
    target = target_ref[0]
    sources = point_buf[slot].reshape(count * size, dims)
    values = weight_buf[slot].reshape(count * size, weight_buf.shape[-1])
    kernel = scaled_kernel(target, target_square_of(target), sources, None if halo else norm_buf[slot])
    out_ref[0] = jnp.dot(kernel, values, preferred_element_type=jnp.float32)


def near_field(local_points, local_weights, local_norms, near_local, halo_inputs=None, previous=None):
    leaves, size, dims = local_points.shape
    rhs = local_weights.shape[-1]
    count = near_local.shape[1]
    halo = halo_inputs is not None
    leaf_of, steps, _ = leaf_order(leaves, halo)
    anywhere = pl.BlockSpec(memory_space=pl.ANY)
    if halo:
        left_pairs, right_pairs = halo_inputs
        inputs = (left_pairs, local_points, right_pairs, local_weights, previous)
    else:
        inputs = (local_points, local_weights, local_norms)
    aliases = {len(inputs) + 1: 0} if previous is not None else {}
    by_leaf = lambda step, index: (leaf_of(step), 0, 0)
    return pl.pallas_call(
        lambda *refs: near_kernel(leaf_of, halo, *refs),
        grid_spec=pltpu.PrefetchScalarGridSpec(
            num_scalar_prefetch=1,
            grid=(steps,),
            in_specs=[pl.BlockSpec((1, size, dims), by_leaf)] + [anywhere] * len(inputs),
            out_specs=pl.BlockSpec((1, size, rhs), by_leaf),
            scratch_shapes=[
                pltpu.VMEM((2, count, size, dims), local_points.dtype),
                pltpu.VMEM((2, count, size, rhs), local_weights.dtype),
                pltpu.VMEM((2, 1, count * size), jnp.float32),
                pltpu.SemaphoreType.DMA((3, 2, count)),
            ],
        ),
        out_shape=jax.ShapeDtypeStruct((leaves, size, rhs), jnp.float32),
        input_output_aliases=aliases,
        compiler_params=pltpu.CompilerParams(dimension_semantics=("arbitrary",)),
    )(near_local.reshape(-1), local_points, *inputs)


def far_kernel(leaf_of, halo, index_ref, target_ref, *refs):
    inputs = 5 if halo else 2
    out_ref = refs[inputs]
    source_buf, norm_buf, sems = refs[inputs + 1 :]
    count, rank = source_buf.shape[1], source_buf.shape[2]
    buffers = [lambda slot, position: source_buf.at[slot, position]]
    if halo:
        ls, os, rs = refs[:3]
        parts = (whole_rows(ls, os, rs),)
    else:
        parts = (own_rows_only(refs[0]), own_norms_only(refs[1]))
        buffers.append(lambda slot, position: norm_buf.at[slot, :, pl.ds(position * rank, rank)])
    slot = pipelined_sources(index_ref, count, parts, buffers, sems, leaf_of)
    target = target_ref[0]
    dims = target.shape[-1]
    sources = source_buf[slot].reshape(count * rank, source_buf.shape[-1])
    kernel = scaled_kernel(
        target, target_square_of(target), sources[:, :dims], None if halo else norm_buf[slot]
    )
    out_ref[0] = jnp.dot(kernel, sources[:, dims:], preferred_element_type=jnp.float32)


def far_field(leaf_coords, own_rows, own_norms, far_local, halo_inputs=None, previous=None, after=None):
    leaves, rank, dims = leaf_coords.shape
    width = own_rows.shape[-1]
    count = far_local.shape[1]
    halo = halo_inputs is not None
    leaf_of, steps, _ = leaf_order(leaves, halo)
    anywhere = pl.BlockSpec(memory_space=pl.ANY)
    if halo:
        left_rows, right_rows = halo_inputs
        inputs = (left_rows, own_rows, right_rows, after, previous)
    else:
        inputs = (own_rows, own_norms)
    aliases = {len(inputs) + 1: 0} if previous is not None else {}
    by_leaf = lambda step, index: (leaf_of(step), 0, 0)
    return pl.pallas_call(
        lambda *refs: far_kernel(leaf_of, halo, *refs),
        grid_spec=pltpu.PrefetchScalarGridSpec(
            num_scalar_prefetch=1,
            grid=(steps,),
            in_specs=[pl.BlockSpec((1, rank, dims), by_leaf)] + [anywhere] * len(inputs),
            out_specs=pl.BlockSpec((1, rank, width - dims), by_leaf),
            scratch_shapes=[
                pltpu.VMEM((2, count, rank, width), own_rows.dtype),
                pltpu.VMEM((2, 1, count * rank), jnp.float32),
                pltpu.SemaphoreType.DMA((2, 2, count)),
            ],
        ),
        out_shape=jax.ShapeDtypeStruct((leaves, rank, width - dims), jnp.float32),
        input_output_aliases=aliases,
        compiler_params=pltpu.CompilerParams(dimension_semantics=("arbitrary",)),
    )(far_local.reshape(-1), leaf_coords, *inputs)


def final_kernel(rank_ref, basis_ref, down_ref, far_ref, leaf_base_ref, near_ref, out_ref):
    block = basis_ref.shape[0]
    step = pl.program_id(0)
    down = down_ref[...]
    for inside in range(block):
        total = jnp.dot(basis_ref[inside], down, preferred_element_type=jnp.float32) + far_ref[inside]
        rows = lax.broadcasted_iota(jnp.int32, total.shape, 0)
        leaf_down = jnp.where(rows < rank_ref[step * block + inside], total, 0.0).astype(jnp.bfloat16)
        result = (
            jnp.dot(leaf_base_ref[inside], leaf_down, preferred_element_type=jnp.float32)
            + near_ref[inside]
        )
        out_ref[inside] = result.astype(out_ref.dtype)


def final_field(leaf_rank, bases, node_down, far_total, leaf_bases, near_total):
    leaves, rank, width = bases.shape
    size = leaf_bases.shape[1]
    rhs = near_total.shape[-1]
    block = max(b for b in (1, 2, 3, 4) if leaves % b == 0)

    def own(l, ranks):
        return (l, 0, 0)

    return pl.pallas_call(
        final_kernel,
        grid_spec=pltpu.PrefetchScalarGridSpec(
            num_scalar_prefetch=1,
            grid=(leaves // block,),
            in_specs=[
                pl.BlockSpec((block, rank, width), own),
                pl.BlockSpec(node_down.shape, lambda l, ranks: (0, 0)),
                pl.BlockSpec((block, rank, rhs), own),
                pl.BlockSpec((block, size, rank), own),
                pl.BlockSpec((block, size, rhs), own),
            ],
            out_specs=pl.BlockSpec((block, size, rhs), own),
        ),
        out_shape=jax.ShapeDtypeStruct((leaves, size, rhs), jnp.bfloat16),
    )(leaf_rank, bases, node_down, far_total, leaf_bases, near_total)


def select_rows(table, index):
    count = table.shape[0]
    onehot = (index[:, None] == jnp.arange(count, dtype=jnp.int32)[None, :]).astype(table.dtype)
    picked = jnp.dot(onehot, table.reshape(count, -1), preferred_element_type=jnp.float32).astype(
        table.dtype
    )
    return picked.reshape(index.shape + table.shape[1:])


def select_within(table, index):
    count = table.shape[1]
    onehot = (index[:, :, None] == jnp.arange(count, dtype=jnp.int32)[None, None, :]).astype(
        table.dtype
    )
    return jnp.einsum("bkp,bpc->bkc", onehot, table, preferred_element_type=jnp.float32).astype(
        table.dtype
    )


def body(
    points,
    weights,
    leaf_basis,
    leaf_rank,
    leaf_skeleton,
    near_list,
    far_list,
    node_basis,
    node_rank,
    node_skeleton,
    node_far,
    group_basis,
    group_rank,
    group_skeleton,
    group_far,
):
    leaf_count = leaf_rank.shape[0]
    leaf_size = points.shape[0] // leaf_count
    dim_count = points.shape[1]
    rhs_count = weights.shape[1]
    rank_count = leaf_basis.shape[1]
    node_width = node_basis.shape[1]
    group_width = group_basis.shape[1]
    local_points = points.reshape(leaf_count, leaf_size, dim_count)
    local_bases = leaf_basis.reshape(leaf_count, leaf_size, rank_count)
    local_weights = weights.reshape(leaf_count, leaf_size, rhs_count)
    first_leaf = lax.axis_index(FLAT) * leaf_count
    offset = first_leaf - REACH

    left_pairs, right_pairs = halos((points, weights), REACH * leaf_size)
    left_pairs = left_pairs.reshape(REACH, leaf_size, dim_count + rhs_count)
    right_pairs = right_pairs.reshape(REACH, leaf_size, dim_count + rhs_count)

    leaf_mask = (lax.broadcasted_iota(jnp.int32, (leaf_count, rank_count), 1) < leaf_rank[:, None]).astype(jnp.float32)
    leaf_up = (
        jnp.einsum("lpk,lpr->lkr", local_bases, local_weights, preferred_element_type=jnp.float32)
        * leaf_mask[:, :, None]
    ).astype(jnp.bfloat16)
    leaf_coords = select_within(local_points, leaf_skeleton)
    own_rows = jnp.concatenate([leaf_coords, leaf_up], axis=-1)
    skeleton_width = dim_count + rhs_count
    left_rows, right_rows = halos(
        (own_rows.reshape(leaf_count * rank_count, skeleton_width),), REACH * rank_count
    )

    node_mask = (jnp.arange(node_width, dtype=jnp.int32) < node_rank[0]).astype(jnp.float32)
    node_up = (
        jnp.einsum(
            "ak,ar->kr",
            node_basis,
            leaf_up.reshape(leaf_count * rank_count, rhs_count),
            preferred_element_type=jnp.float32,
        )
        * node_mask[:, None]
    ).astype(jnp.bfloat16)
    node_coords = select_rows(
        leaf_coords.reshape(leaf_count * rank_count, dim_count), node_skeleton[0]
    )
    columns = lax.axis_size("col")
    source_columns = node_far[0] % columns
    node_pack = jnp.concatenate([node_coords, node_up, group_basis], axis=1)
    gathered = lax.all_gather(node_pack[None], "col", axis=0, tiled=True)

    near_local = near_list - offset
    local_norms = scaled_norms(local_points)
    near_inner = near_field(local_points, local_weights, local_norms, near_local)
    all_coords = gathered[:, :, :dim_count]
    all_up = gathered[:, :, dim_count : dim_count + rhs_count]
    all_parts = gathered[:, :, dim_count + rhs_count :]
    picked_coords = select_rows(all_coords, source_columns)
    picked_up = select_rows(all_up, source_columns)
    kernel = kernel_block(jnp.broadcast_to(node_coords, picked_coords.shape), picked_coords)
    node_side = jnp.einsum("fab,fbr->ar", kernel, picked_up, preferred_element_type=jnp.float32)
    group_mask = (jnp.arange(group_width, dtype=jnp.int32) < group_rank[0]).astype(jnp.float32)
    group_up = (
        jnp.einsum("nag,nar->gr", all_parts, all_up, preferred_element_type=jnp.float32)
        * group_mask[:, None]
    ).astype(jnp.bfloat16)
    group_coords = select_rows(all_coords.reshape(columns * node_width, dim_count), group_skeleton[0])
    group_pack = jnp.concatenate([group_coords, group_up], axis=1)
    near_total = near_field(
        local_points,
        local_weights,
        local_norms,
        near_local,
        (left_pairs, right_pairs),
        near_inner,
    )
    near_total, left_rows, right_rows = lax.optimization_barrier((near_total, left_rows, right_rows))

    left_rows = left_rows.reshape(REACH, rank_count, skeleton_width)
    right_rows = right_rows.reshape(REACH, rank_count, skeleton_width)
    far_local = far_list - offset
    coord_norms = scaled_norms(leaf_coords)
    far_inner = far_field(leaf_coords, own_rows, coord_norms, far_local)
    far_total = far_field(
        leaf_coords,
        own_rows,
        coord_norms,
        far_local,
        (left_rows, right_rows),
        far_inner,
        group_pack,
    )
    rows = lax.axis_size("row")
    mine = lax.axis_index("row")
    slots = jnp.where(
        (jnp.arange(rows, dtype=jnp.int32) == mine)[:, None, None], group_pack[None], jnp.zeros_like(group_pack)[None]
    )
    every_group = lax.psum(slots, "row")
    picked_group = select_rows(every_group, group_far[0])
    picked_group_coords = picked_group[:, :, :dim_count]
    picked_group_up = picked_group[:, :, dim_count:]
    group_kernel = kernel_block(
        jnp.broadcast_to(group_coords, picked_group_coords.shape), picked_group_coords
    )
    group_down = (
        jnp.einsum("fab,fbr->ar", group_kernel, picked_group_up, preferred_element_type=jnp.float32)
        * group_mask[:, None]
    ).astype(jnp.bfloat16)
    node_down = (
        (jnp.dot(group_basis, group_down, preferred_element_type=jnp.float32) + node_side)
        * node_mask[:, None]
    ).astype(jnp.bfloat16)
    result = final_field(
        leaf_rank,
        node_basis.reshape(leaf_count, rank_count, node_width),
        node_down,
        far_total,
        local_bases,
        near_total,
    )
    return result.reshape(leaf_count * leaf_size, rhs_count)


def solution(mesh):
    in_specs = (
        P(FLAT, None),
        P(FLAT, None),
        P(FLAT, None),
        P(FLAT),
        P(FLAT, None),
        P(FLAT, None),
        P(FLAT, None),
        P(FLAT, None),
        P(FLAT),
        P(FLAT, None),
        P(FLAT, None),
        P(FLAT, None),
        P("row"),
        P("row", None),
        P("row", None),
    )
    out_specs = P(FLAT, None)

    return jax.shard_map(body, mesh=mesh, in_specs=in_specs, out_specs=out_specs, check_vma=False)
```

```python
import jax
import jax.numpy as jnp
from jax import lax
from jax.experimental import pallas as pl
from jax.experimental.pallas import tpu as pltpu
from jax.sharding import PartitionSpec as P


REACH = 8
FLAT = ("row", "col")


def halos(cells, width):
    count = lax.axis_size(FLAT)
    ends = count - 1
    head = jnp.concatenate([cell[:width] for cell in cells], axis=1)
    tail = jnp.concatenate([cell[cell.shape[0] - width :] for cell in cells], axis=1)
    left = lax.ppermute(tail, FLAT, [(i, i + 1) for i in range(ends)])
    right = lax.ppermute(head, FLAT, [(i + 1, i) for i in range(ends)])
    return left, right


def kernel_block(left, right):
    left_square = jnp.sum(jnp.square(left.astype(jnp.float32)), axis=-1)
    right_square = jnp.sum(jnp.square(right.astype(jnp.float32)), axis=-1)
    inner = jnp.einsum("...md,...nd->...mn", left, right, preferred_element_type=jnp.float32)
    distance = left_square[..., :, None] + right_square[..., None, :] - 2.0 * inner
    return jnp.exp(distance * (-2.0 / left.shape[-1])).astype(jnp.bfloat16)


def contract_last(a, b):
    return lax.dot_general(a, b, (((1,), (1,)), ((), ())), preferred_element_type=jnp.float32)


def scaled_kernel(target, target_square, source, source_square=None):
    dims = target.shape[-1]
    if source_square is None:
        wide = source.astype(jnp.float32)
        square = wide * wide
        high = square.astype(jnp.bfloat16)
        low = (square - high.astype(jnp.float32)).astype(jnp.bfloat16)
        ones = jnp.ones((8, dims), jnp.bfloat16)
        summed = contract_last(ones, high) + contract_last(ones, low)
        source_square = summed[0:1] * (-2.0 / dims)
    inner = contract_last(target * jnp.asarray(4.0 / dims, target.dtype), source)
    return jnp.exp((target_square + source_square) + inner).astype(jnp.bfloat16)


def scaled_norms(cells):
    factor = (2.0 / cells.shape[-1]) ** 0.5
    assert factor * factor == 2.0 / cells.shape[-1]
    wide = cells.astype(jnp.float32) * factor
    return jnp.sum(wide * -wide, axis=-1)


def target_square_of(target):
    wide = target.astype(jnp.float32)
    return jnp.sum(wide * wide, axis=-1, keepdims=True) * (-2.0 / target.shape[-1])


def fetch_sources(index_ref, row, count, parts, buffers, sems, slot):
    for position in range(count):
        source = index_ref[row * count + position]
        for which, (halo, mine, left, own, right) in enumerate(parts):
            target = buffers[which](slot, position)
            sem = sems.at[which, slot, position]
            if left is None:
                pltpu.make_async_copy(own(source - halo), target, sem).start()
                continue

            @pl.when(source < halo)
            def _():
                pltpu.make_async_copy(left(source), target, sem).start()

            @pl.when((source >= halo) & (source < halo + mine))
            def _():
                pltpu.make_async_copy(own(source - halo), target, sem).start()

            @pl.when(source >= halo + mine)
            def _():
                pltpu.make_async_copy(right(source - halo - mine), target, sem).start()


def wait_sources(count, parts, buffers, sems, slot):
    for position in range(count):
        for which, (halo, mine, left, own, right) in enumerate(parts):
            pltpu.make_async_copy(
                own(0), buffers[which](slot, position), sems.at[which, slot, position]
            ).wait()


def rows_of(ref):
    return lambda index: ref.at[index]


def row_of(ref):
    return lambda index: ref.at[pl.ds(index, 1)]


def own_norms_only(own):
    return (REACH, own.shape[0], None, row_of(own), None)


def whole_rows(left, own, right):
    return (left.shape[0], own.shape[0], rows_of(left), rows_of(own), rows_of(right))


def own_rows_only(own):
    return (REACH, own.shape[0], None, rows_of(own), None)


def lane_rows(left, own, right, start, width):
    def halo_at(ref):
        return lambda index: ref.at[index, :, pl.ds(start, width)]

    return (left.shape[0], own.shape[0], halo_at(left), rows_of(own), halo_at(right))


def pipelined_sources(index_ref, count, parts, buffers, sems, leaf_of):
    step = pl.program_id(0)
    steps = pl.num_programs(0)
    slot = step % 2

    @pl.when(step == 0)
    def _():
        fetch_sources(index_ref, leaf_of(0), count, parts, buffers, sems, 0)

    @pl.when(step + 1 < steps)
    def _():
        fetch_sources(index_ref, leaf_of(step + 1), count, parts, buffers, sems, 1 - slot)

    wait_sources(count, parts, buffers, sems, slot)
    return slot


def leaf_order(leaves, edges):
    low, high = REACH, leaves - REACH
    if high <= low:
        return (lambda step: step), leaves, None
    if not edges:
        return (lambda step: step + low), high - low, None
    gap = high - low
    return (lambda step: step + gap * jnp.asarray(step >= low, jnp.int32)), leaves - gap, gap


def near_kernel(leaf_of, halo, index_ref, target_ref, *refs):
    inputs = 5 if halo else 3
    out_ref = refs[inputs]
    point_buf, weight_buf, norm_buf, sems = refs[inputs + 1 :]
    count, size, dims = point_buf.shape[1], point_buf.shape[2], point_buf.shape[3]
    buffers = [
        lambda slot, position: point_buf.at[slot, position],
        lambda slot, position: weight_buf.at[slot, position],
    ]
    if halo:
        lpw, op, rpw, ow = refs[:4]
        parts = (
            lane_rows(lpw, op, rpw, 0, dims),
            lane_rows(lpw, ow, rpw, dims, weight_buf.shape[-1]),
        )
    else:
        parts = (own_rows_only(refs[0]), own_rows_only(refs[1]), own_norms_only(refs[2]))
        buffers.append(lambda slot, position: norm_buf.at[slot, :, pl.ds(position * size, size)])
    slot = pipelined_sources(index_ref, count, parts, buffers, sems, leaf_of)
    target = target_ref[0]
    sources = point_buf[slot].reshape(count * size, dims)
    values = weight_buf[slot].reshape(count * size, weight_buf.shape[-1])
    kernel = scaled_kernel(target, target_square_of(target), sources, None if halo else norm_buf[slot])
    out_ref[0] = jnp.dot(kernel, values, preferred_element_type=jnp.float32)


def near_field(local_points, local_weights, local_norms, near_local, halo_inputs=None, previous=None):
    leaves, size, dims = local_points.shape
    rhs = local_weights.shape[-1]
    count = near_local.shape[1]
    halo = halo_inputs is not None
    leaf_of, steps, _ = leaf_order(leaves, halo)
    anywhere = pl.BlockSpec(memory_space=pl.ANY)
    if halo:
        left_pairs, right_pairs = halo_inputs
        inputs = (left_pairs, local_points, right_pairs, local_weights, previous)
    else:
        inputs = (local_points, local_weights, local_norms)
    aliases = {len(inputs) + 1: 0} if previous is not None else {}
    by_leaf = lambda step, index: (leaf_of(step), 0, 0)
    return pl.pallas_call(
        lambda *refs: near_kernel(leaf_of, halo, *refs),
        grid_spec=pltpu.PrefetchScalarGridSpec(
            num_scalar_prefetch=1,
            grid=(steps,),
            in_specs=[pl.BlockSpec((1, size, dims), by_leaf)] + [anywhere] * len(inputs),
            out_specs=pl.BlockSpec((1, size, rhs), by_leaf),
            scratch_shapes=[
                pltpu.VMEM((2, count, size, dims), local_points.dtype),
                pltpu.VMEM((2, count, size, rhs), local_weights.dtype),
                pltpu.VMEM((2, 1, count * size), jnp.float32),
                pltpu.SemaphoreType.DMA((3, 2, count)),
            ],
        ),
        out_shape=jax.ShapeDtypeStruct((leaves, size, rhs), jnp.float32),
        input_output_aliases=aliases,
        compiler_params=pltpu.CompilerParams(dimension_semantics=("arbitrary",)),
    )(near_local.reshape(-1), local_points, *inputs)


def far_kernel(leaf_of, halo, index_ref, target_ref, *refs):
    inputs = 5 if halo else 2
    out_ref = refs[inputs]
    source_buf, norm_buf, sems = refs[inputs + 1 :]
    count, rank = source_buf.shape[1], source_buf.shape[2]
    buffers = [lambda slot, position: source_buf.at[slot, position]]
    if halo:
        ls, os, rs = refs[:3]
        parts = (whole_rows(ls, os, rs),)
    else:
        parts = (own_rows_only(refs[0]), own_norms_only(refs[1]))
        buffers.append(lambda slot, position: norm_buf.at[slot, :, pl.ds(position * rank, rank)])
    slot = pipelined_sources(index_ref, count, parts, buffers, sems, leaf_of)
    target = target_ref[0]
    dims = target.shape[-1]
    sources = source_buf[slot].reshape(count * rank, source_buf.shape[-1])
    kernel = scaled_kernel(
        target, target_square_of(target), sources[:, :dims], None if halo else norm_buf[slot]
    )
    out_ref[0] = jnp.dot(kernel, sources[:, dims:], preferred_element_type=jnp.float32)


def far_field(leaf_coords, own_rows, own_norms, far_local, halo_inputs=None, previous=None, after=None):
    leaves, rank, dims = leaf_coords.shape
    width = own_rows.shape[-1]
    count = far_local.shape[1]
    halo = halo_inputs is not None
    leaf_of, steps, _ = leaf_order(leaves, halo)
    anywhere = pl.BlockSpec(memory_space=pl.ANY)
    if halo:
        left_rows, right_rows = halo_inputs
        inputs = (left_rows, own_rows, right_rows, after, previous)
    else:
        inputs = (own_rows, own_norms)
    aliases = {len(inputs) + 1: 0} if previous is not None else {}
    by_leaf = lambda step, index: (leaf_of(step), 0, 0)
    return pl.pallas_call(
        lambda *refs: far_kernel(leaf_of, halo, *refs),
        grid_spec=pltpu.PrefetchScalarGridSpec(
            num_scalar_prefetch=1,
            grid=(steps,),
            in_specs=[pl.BlockSpec((1, rank, dims), by_leaf)] + [anywhere] * len(inputs),
            out_specs=pl.BlockSpec((1, rank, width - dims), by_leaf),
            scratch_shapes=[
                pltpu.VMEM((2, count, rank, width), own_rows.dtype),
                pltpu.VMEM((2, 1, count * rank), jnp.float32),
                pltpu.SemaphoreType.DMA((2, 2, count)),
            ],
        ),
        out_shape=jax.ShapeDtypeStruct((leaves, rank, width - dims), jnp.float32),
        input_output_aliases=aliases,
        compiler_params=pltpu.CompilerParams(dimension_semantics=("arbitrary",)),
    )(far_local.reshape(-1), leaf_coords, *inputs)


def final_kernel(rank_ref, basis_ref, down_ref, far_ref, leaf_base_ref, near_ref, out_ref):
    block = basis_ref.shape[0]
    step = pl.program_id(0)
    down = down_ref[...]
    for inside in range(block):
        total = jnp.dot(basis_ref[inside], down, preferred_element_type=jnp.float32) + far_ref[inside]
        rows = lax.broadcasted_iota(jnp.int32, total.shape, 0)
        leaf_down = jnp.where(rows < rank_ref[step * block + inside], total, 0.0).astype(jnp.bfloat16)
        result = (
            jnp.dot(leaf_base_ref[inside], leaf_down, preferred_element_type=jnp.float32)
            + near_ref[inside]
        )
        out_ref[inside] = result.astype(out_ref.dtype)


def final_field(leaf_rank, bases, node_down, far_total, leaf_bases, near_total):
    leaves, rank, width = bases.shape
    size = leaf_bases.shape[1]
    rhs = near_total.shape[-1]
    block = max(b for b in (1, 2, 3, 4) if leaves % b == 0)

    def own(l, ranks):
        return (l, 0, 0)

    return pl.pallas_call(
        final_kernel,
        grid_spec=pltpu.PrefetchScalarGridSpec(
            num_scalar_prefetch=1,
            grid=(leaves // block,),
            in_specs=[
                pl.BlockSpec((block, rank, width), own),
                pl.BlockSpec(node_down.shape, lambda l, ranks: (0, 0)),
                pl.BlockSpec((block, rank, rhs), own),
                pl.BlockSpec((block, size, rank), own),
                pl.BlockSpec((block, size, rhs), own),
            ],
            out_specs=pl.BlockSpec((block, size, rhs), own),
        ),
        out_shape=jax.ShapeDtypeStruct((leaves, size, rhs), jnp.bfloat16),
    )(leaf_rank, bases, node_down, far_total, leaf_bases, near_total)


def select_rows(table, index):
    count = table.shape[0]
    onehot = (index[:, None] == jnp.arange(count, dtype=jnp.int32)[None, :]).astype(table.dtype)
    picked = jnp.dot(onehot, table.reshape(count, -1), preferred_element_type=jnp.float32).astype(
        table.dtype
    )
    return picked.reshape(index.shape + table.shape[1:])


def select_within(table, index):
    count = table.shape[1]
    onehot = (index[:, :, None] == jnp.arange(count, dtype=jnp.int32)[None, None, :]).astype(
        table.dtype
    )
    return jnp.einsum("bkp,bpc->bkc", onehot, table, preferred_element_type=jnp.float32).astype(
        table.dtype
    )


def body(
    points,
    weights,
    leaf_basis,
    leaf_rank,
    leaf_skeleton,
    near_list,
    far_list,
    node_basis,
    node_rank,
    node_skeleton,
    node_far,
    group_basis,
    group_rank,
    group_skeleton,
    group_far,
):
    leaf_count = leaf_rank.shape[0]
    leaf_size = points.shape[0] // leaf_count
    dim_count = points.shape[1]
    rhs_count = weights.shape[1]
    rank_count = leaf_basis.shape[1]
    node_width = node_basis.shape[1]
    group_width = group_basis.shape[1]
    local_points = points.reshape(leaf_count, leaf_size, dim_count)
    local_bases = leaf_basis.reshape(leaf_count, leaf_size, rank_count)
    local_weights = weights.reshape(leaf_count, leaf_size, rhs_count)
    first_leaf = lax.axis_index(FLAT) * leaf_count
    offset = first_leaf - REACH

    left_pairs, right_pairs = halos((points, weights), REACH * leaf_size)
    left_pairs = left_pairs.reshape(REACH, leaf_size, dim_count + rhs_count)
    right_pairs = right_pairs.reshape(REACH, leaf_size, dim_count + rhs_count)

    leaf_mask = (
        lax.broadcasted_iota(jnp.int32, (leaf_count, rank_count), 1) < leaf_rank[:, None]
    ).astype(jnp.float32)
    leaf_up = (
        jnp.einsum("lpk,lpr->lkr", local_bases, local_weights, preferred_element_type=jnp.float32)
        * leaf_mask[:, :, None]
    ).astype(jnp.bfloat16)
    leaf_coords = select_within(local_points, leaf_skeleton)
    own_rows = jnp.concatenate([leaf_coords, leaf_up], axis=-1)
    skeleton_width = dim_count + rhs_count
    left_rows, right_rows = halos(
        (own_rows.reshape(leaf_count * rank_count, skeleton_width),), REACH * rank_count
    )

    node_mask = (jnp.arange(node_width, dtype=jnp.int32) < node_rank[0]).astype(jnp.float32)
    node_up = (
        jnp.einsum(
            "ak,ar->kr",
            node_basis,
            leaf_up.reshape(leaf_count * rank_count, rhs_count),
            preferred_element_type=jnp.float32,
        )
        * node_mask[:, None]
    ).astype(jnp.bfloat16)
    node_coords = select_rows(
        leaf_coords.reshape(leaf_count * rank_count, dim_count), node_skeleton[0]
    )
    columns = lax.axis_size("col")
    source_columns = node_far[0] % columns
    node_pack = jnp.concatenate([node_coords, node_up, group_basis], axis=1)
    received = [node_pack] + [
        lax.ppermute(node_pack, "col", [(c, (c + shift) % columns) for c in range(columns)])
        for shift in range(1, columns)
    ]
    origins = (lax.axis_index("col") - jnp.arange(columns, dtype=jnp.int32)) % columns
    gathered = select_rows(jnp.stack(received), origins)

    near_local = near_list - offset
    local_norms = scaled_norms(local_points)
    near_inner = near_field(local_points, local_weights, local_norms, near_local)
    all_coords = gathered[:, :, :dim_count]
    all_up = gathered[:, :, dim_count : dim_count + rhs_count]
    all_parts = gathered[:, :, dim_count + rhs_count :]
    picked_coords = select_rows(all_coords, source_columns)
    picked_up = select_rows(all_up, source_columns)
    kernel = kernel_block(jnp.broadcast_to(node_coords, picked_coords.shape), picked_coords)
    node_side = jnp.einsum("fab,fbr->ar", kernel, picked_up, preferred_element_type=jnp.float32)
    group_mask = (jnp.arange(group_width, dtype=jnp.int32) < group_rank[0]).astype(jnp.float32)
    group_up = (
        jnp.einsum("nag,nar->gr", all_parts, all_up, preferred_element_type=jnp.float32)
        * group_mask[:, None]
    ).astype(jnp.bfloat16)
    group_coords = select_rows(all_coords.reshape(columns * node_width, dim_count), group_skeleton[0])
    group_pack = jnp.concatenate([group_coords, group_up], axis=1)
    near_total = near_field(
        local_points,
        local_weights,
        local_norms,
        near_local,
        (left_pairs, right_pairs),
        near_inner,
    )
    near_total, left_rows, right_rows = lax.optimization_barrier((near_total, left_rows, right_rows))

    left_rows = left_rows.reshape(REACH, rank_count, skeleton_width)
    right_rows = right_rows.reshape(REACH, rank_count, skeleton_width)
    far_local = far_list - offset
    coord_norms = scaled_norms(leaf_coords)
    far_inner = far_field(leaf_coords, own_rows, coord_norms, far_local)
    far_total = far_field(
        leaf_coords,
        own_rows,
        coord_norms,
        far_local,
        (left_rows, right_rows),
        far_inner,
        group_pack,
    )
    rows = lax.axis_size("row")
    received = [group_pack] + [
        lax.ppermute(group_pack, "row", [(r, (r + shift) % rows) for r in range(rows)])
        for shift in range(1, rows)
    ]
    shifts = (lax.axis_index("row") - group_far[0]) % rows
    picked_group = select_rows(jnp.stack(received), shifts)
    picked_group_coords = picked_group[:, :, :dim_count]
    picked_group_up = picked_group[:, :, dim_count:]
    group_kernel = kernel_block(
        jnp.broadcast_to(group_coords, picked_group_coords.shape), picked_group_coords
    )
    group_down = (
        jnp.einsum("fab,fbr->ar", group_kernel, picked_group_up, preferred_element_type=jnp.float32)
        * group_mask[:, None]
    ).astype(jnp.bfloat16)
    node_down = (
        (jnp.dot(group_basis, group_down, preferred_element_type=jnp.float32) + node_side)
        * node_mask[:, None]
    ).astype(jnp.bfloat16)
    result = final_field(
        leaf_rank,
        node_basis.reshape(leaf_count, rank_count, node_width),
        node_down,
        far_total,
        local_bases,
        near_total,
    )
    return result.reshape(leaf_count * leaf_size, rhs_count)


def solution(mesh):
    in_specs = (
        P(FLAT, None),
        P(FLAT, None),
        P(FLAT, None),
        P(FLAT),
        P(FLAT, None),
        P(FLAT, None),
        P(FLAT, None),
        P(FLAT, None),
        P(FLAT),
        P(FLAT, None),
        P(FLAT, None),
        P(FLAT, None),
        P("row"),
        P("row", None),
        P("row", None),
    )
    out_specs = P(FLAT, None)

    return jax.shard_map(body, mesh=mesh, in_specs=in_specs, out_specs=out_specs, check_vma=False)
```

```python
import jax
import jax.numpy as jnp
from jax import lax
from jax.experimental import pallas as pl
from jax.experimental.pallas import tpu as pltpu
from jax.sharding import PartitionSpec as P


REACH = 8
FLAT = ("row", "col")


def halos(cells, width):
    count = lax.axis_size(FLAT)
    ends = count - 1
    head = jnp.concatenate([cell[:width] for cell in cells], axis=1)
    tail = jnp.concatenate([cell[cell.shape[0] - width :] for cell in cells], axis=1)
    left = lax.ppermute(tail, FLAT, [(i, i + 1) for i in range(ends)])
    right = lax.ppermute(head, FLAT, [(i + 1, i) for i in range(ends)])
    return left, right


def kernel_block(left, right):
    left_square = jnp.sum(jnp.square(left.astype(jnp.float32)), axis=-1)
    right_square = jnp.sum(jnp.square(right.astype(jnp.float32)), axis=-1)
    inner = jnp.einsum("...md,...nd->...mn", left, right, preferred_element_type=jnp.float32)
    distance = left_square[..., :, None] + right_square[..., None, :] - 2.0 * inner
    return jnp.exp(distance * (-2.0 / left.shape[-1])).astype(jnp.bfloat16)


def contract_last(a, b):
    return lax.dot_general(a, b, (((1,), (1,)), ((), ())), preferred_element_type=jnp.float32)


def scaled_kernel(target, target_square, source, source_square=None):
    dims = target.shape[-1]
    if source_square is None:
        wide = source.astype(jnp.float32)
        square = wide * wide
        high = square.astype(jnp.bfloat16)
        low = (square - high.astype(jnp.float32)).astype(jnp.bfloat16)
        ones = jnp.ones((8, dims), jnp.bfloat16)
        summed = contract_last(ones, high) + contract_last(ones, low)
        source_square = summed[0:1] * (-2.0 / dims)
    inner = contract_last(target * jnp.asarray(4.0 / dims, target.dtype), source)
    return jnp.exp((target_square + source_square) + inner).astype(jnp.bfloat16)


def scaled_norms(cells):
    factor = (2.0 / cells.shape[-1]) ** 0.5
    assert factor * factor == 2.0 / cells.shape[-1]
    wide = cells.astype(jnp.float32) * factor
    return jnp.sum(wide * -wide, axis=-1)


def target_square_of(target):
    wide = target.astype(jnp.float32)
    return jnp.sum(wide * wide, axis=-1, keepdims=True) * (-2.0 / target.shape[-1])


def fetch_sources(index_ref, row, count, parts, buffers, sems, slot):
    for position in range(count):
        source = index_ref[row * count + position]
        for which, (halo, mine, left, own, right) in enumerate(parts):
            target = buffers[which](slot, position)
            sem = sems.at[which, slot, position]
            if left is None:
                pltpu.make_async_copy(own(source - halo), target, sem).start()
                continue

            @pl.when(source < halo)
            def _():
                pltpu.make_async_copy(left(source), target, sem).start()

            @pl.when((source >= halo) & (source < halo + mine))
            def _():
                pltpu.make_async_copy(own(source - halo), target, sem).start()

            @pl.when(source >= halo + mine)
            def _():
                pltpu.make_async_copy(right(source - halo - mine), target, sem).start()


def wait_sources(count, parts, buffers, sems, slot):
    for position in range(count):
        for which, (halo, mine, left, own, right) in enumerate(parts):
            pltpu.make_async_copy(
                own(0), buffers[which](slot, position), sems.at[which, slot, position]
            ).wait()


def rows_of(ref):
    return lambda index: ref.at[index]


def row_of(ref):
    return lambda index: ref.at[pl.ds(index, 1)]


def own_norms_only(own):
    return (REACH, own.shape[0], None, row_of(own), None)


def whole_rows(left, own, right):
    return (left.shape[0], own.shape[0], rows_of(left), rows_of(own), rows_of(right))


def own_rows_only(own):
    return (REACH, own.shape[0], None, rows_of(own), None)


def lane_rows(left, own, right, start, width):
    def halo_at(ref):
        return lambda index: ref.at[index, :, pl.ds(start, width)]

    return (left.shape[0], own.shape[0], halo_at(left), rows_of(own), halo_at(right))


def pipelined_sources(index_ref, count, parts, buffers, sems, leaf_of):
    step = pl.program_id(0)
    steps = pl.num_programs(0)
    slot = step % 2

    @pl.when(step == 0)
    def _():
        fetch_sources(index_ref, leaf_of(0), count, parts, buffers, sems, 0)

    @pl.when(step + 1 < steps)
    def _():
        fetch_sources(index_ref, leaf_of(step + 1), count, parts, buffers, sems, 1 - slot)

    wait_sources(count, parts, buffers, sems, slot)
    return slot


def leaf_order(leaves, edges):
    low, high = REACH, leaves - REACH
    if high <= low:
        return (lambda step: step), leaves, None
    if not edges:
        return (lambda step: step + low), high - low, None
    gap = high - low
    return (lambda step: step + gap * jnp.asarray(step >= low, jnp.int32)), leaves - gap, gap


def near_kernel(leaf_of, halo, index_ref, target_ref, *refs):
    inputs = 5 if halo else 3
    out_ref = refs[inputs]
    point_buf, weight_buf, norm_buf, sems = refs[inputs + 1 :]
    count, size, dims = point_buf.shape[1], point_buf.shape[2], point_buf.shape[3]
    buffers = [
        lambda slot, position: point_buf.at[slot, position],
        lambda slot, position: weight_buf.at[slot, position],
    ]
    if halo:
        lpw, op, rpw, ow = refs[:4]
        parts = (
            lane_rows(lpw, op, rpw, 0, dims),
            lane_rows(lpw, ow, rpw, dims, weight_buf.shape[-1]),
        )
    else:
        parts = (own_rows_only(refs[0]), own_rows_only(refs[1]), own_norms_only(refs[2]))
        buffers.append(lambda slot, position: norm_buf.at[slot, :, pl.ds(position * size, size)])
    slot = pipelined_sources(index_ref, count, parts, buffers, sems, leaf_of)
    target = target_ref[0]
    sources = point_buf[slot].reshape(count * size, dims)
    values = weight_buf[slot].reshape(count * size, weight_buf.shape[-1])
    kernel = scaled_kernel(target, target_square_of(target), sources, None if halo else norm_buf[slot])
    out_ref[0] = jnp.dot(kernel, values, preferred_element_type=jnp.float32)


def near_field(local_points, local_weights, local_norms, near_local, halo_inputs=None, previous=None):
    leaves, size, dims = local_points.shape
    rhs = local_weights.shape[-1]
    count = near_local.shape[1]
    halo = halo_inputs is not None
    leaf_of, steps, _ = leaf_order(leaves, halo)
    anywhere = pl.BlockSpec(memory_space=pl.ANY)
    if halo:
        left_pairs, right_pairs = halo_inputs
        inputs = (left_pairs, local_points, right_pairs, local_weights, previous)
    else:
        inputs = (local_points, local_weights, local_norms)
    aliases = {len(inputs) + 1: 0} if previous is not None else {}
    by_leaf = lambda step, index: (leaf_of(step), 0, 0)
    return pl.pallas_call(
        lambda *refs: near_kernel(leaf_of, halo, *refs),
        grid_spec=pltpu.PrefetchScalarGridSpec(
            num_scalar_prefetch=1,
            grid=(steps,),
            in_specs=[pl.BlockSpec((1, size, dims), by_leaf)] + [anywhere] * len(inputs),
            out_specs=pl.BlockSpec((1, size, rhs), by_leaf),
            scratch_shapes=[
                pltpu.VMEM((2, count, size, dims), local_points.dtype),
                pltpu.VMEM((2, count, size, rhs), local_weights.dtype),
                pltpu.VMEM((2, 1, count * size), jnp.float32),
                pltpu.SemaphoreType.DMA((3, 2, count)),
            ],
        ),
        out_shape=jax.ShapeDtypeStruct((leaves, size, rhs), jnp.float32),
        input_output_aliases=aliases,
        compiler_params=pltpu.CompilerParams(dimension_semantics=("arbitrary",)),
    )(near_local.reshape(-1), local_points, *inputs)


def far_kernel(leaf_of, halo, index_ref, target_ref, *refs):
    inputs = 5 if halo else 2
    out_ref = refs[inputs]
    source_buf, norm_buf, sems = refs[inputs + 1 :]
    count, rank = source_buf.shape[1], source_buf.shape[2]
    buffers = [lambda slot, position: source_buf.at[slot, position]]
    if halo:
        ls, os, rs = refs[:3]
        parts = (whole_rows(ls, os, rs),)
    else:
        parts = (own_rows_only(refs[0]), own_norms_only(refs[1]))
        buffers.append(lambda slot, position: norm_buf.at[slot, :, pl.ds(position * rank, rank)])
    slot = pipelined_sources(index_ref, count, parts, buffers, sems, leaf_of)
    target = target_ref[0]
    dims = target.shape[-1]
    sources = source_buf[slot].reshape(count * rank, source_buf.shape[-1])
    kernel = scaled_kernel(
        target, target_square_of(target), sources[:, :dims], None if halo else norm_buf[slot]
    )
    out_ref[0] = jnp.dot(kernel, sources[:, dims:], preferred_element_type=jnp.float32)


def far_field(leaf_coords, own_rows, own_norms, far_local, halo_inputs=None, previous=None, after=None):
    leaves, rank, dims = leaf_coords.shape
    width = own_rows.shape[-1]
    count = far_local.shape[1]
    halo = halo_inputs is not None
    leaf_of, steps, _ = leaf_order(leaves, halo)
    anywhere = pl.BlockSpec(memory_space=pl.ANY)
    if halo:
        left_rows, right_rows = halo_inputs
        inputs = (left_rows, own_rows, right_rows, after, previous)
    else:
        inputs = (own_rows, own_norms)
    aliases = {len(inputs) + 1: 0} if previous is not None else {}
    by_leaf = lambda step, index: (leaf_of(step), 0, 0)
    return pl.pallas_call(
        lambda *refs: far_kernel(leaf_of, halo, *refs),
        grid_spec=pltpu.PrefetchScalarGridSpec(
            num_scalar_prefetch=1,
            grid=(steps,),
            in_specs=[pl.BlockSpec((1, rank, dims), by_leaf)] + [anywhere] * len(inputs),
            out_specs=pl.BlockSpec((1, rank, width - dims), by_leaf),
            scratch_shapes=[
                pltpu.VMEM((2, count, rank, width), own_rows.dtype),
                pltpu.VMEM((2, 1, count * rank), jnp.float32),
                pltpu.SemaphoreType.DMA((2, 2, count)),
            ],
        ),
        out_shape=jax.ShapeDtypeStruct((leaves, rank, width - dims), jnp.float32),
        input_output_aliases=aliases,
        compiler_params=pltpu.CompilerParams(dimension_semantics=("arbitrary",)),
    )(far_local.reshape(-1), leaf_coords, *inputs)


def final_kernel(rank_ref, basis_ref, down_ref, far_ref, leaf_base_ref, near_ref, out_ref):
    block = basis_ref.shape[0]
    step = pl.program_id(0)
    down = down_ref[...]
    for inside in range(block):
        total = jnp.dot(basis_ref[inside], down, preferred_element_type=jnp.float32) + far_ref[inside]
        rows = lax.broadcasted_iota(jnp.int32, total.shape, 0)
        leaf_down = jnp.where(rows < rank_ref[step * block + inside], total, 0.0).astype(jnp.bfloat16)
        result = (
            jnp.dot(leaf_base_ref[inside], leaf_down, preferred_element_type=jnp.float32)
            + near_ref[inside]
        )
        out_ref[inside] = result.astype(out_ref.dtype)


def final_field(leaf_rank, bases, node_down, far_total, leaf_bases, near_total):
    leaves, rank, width = bases.shape
    size = leaf_bases.shape[1]
    rhs = near_total.shape[-1]
    block = max(b for b in (1, 2, 3, 4) if leaves % b == 0)

    def own(l, ranks):
        return (l, 0, 0)

    return pl.pallas_call(
        final_kernel,
        grid_spec=pltpu.PrefetchScalarGridSpec(
            num_scalar_prefetch=1,
            grid=(leaves // block,),
            in_specs=[
                pl.BlockSpec((block, rank, width), own),
                pl.BlockSpec(node_down.shape, lambda l, ranks: (0, 0)),
                pl.BlockSpec((block, rank, rhs), own),
                pl.BlockSpec((block, size, rank), own),
                pl.BlockSpec((block, size, rhs), own),
            ],
            out_specs=pl.BlockSpec((block, size, rhs), own),
        ),
        out_shape=jax.ShapeDtypeStruct((leaves, size, rhs), jnp.bfloat16),
    )(leaf_rank, bases, node_down, far_total, leaf_bases, near_total)


def select_rows(table, index):
    count = table.shape[0]
    onehot = (index[:, None] == jnp.arange(count, dtype=jnp.int32)[None, :]).astype(table.dtype)
    picked = jnp.dot(onehot, table.reshape(count, -1), preferred_element_type=jnp.float32).astype(
        table.dtype
    )
    return picked.reshape(index.shape + table.shape[1:])


def select_within(table, index):
    count = table.shape[1]
    onehot = (index[:, :, None] == jnp.arange(count, dtype=jnp.int32)[None, None, :]).astype(
        table.dtype
    )
    return jnp.einsum("bkp,bpc->bkc", onehot, table, preferred_element_type=jnp.float32).astype(
        table.dtype
    )


def body(
    points,
    weights,
    leaf_basis,
    leaf_rank,
    leaf_skeleton,
    near_list,
    far_list,
    node_basis,
    node_rank,
    node_skeleton,
    node_far,
    group_basis,
    group_rank,
    group_skeleton,
    group_far,
):
    leaf_count = leaf_rank.shape[0]
    leaf_size = points.shape[0] // leaf_count
    dim_count = points.shape[1]
    rhs_count = weights.shape[1]
    rank_count = leaf_basis.shape[1]
    node_width = node_basis.shape[1]
    group_width = group_basis.shape[1]
    local_points = points.reshape(leaf_count, leaf_size, dim_count)
    local_bases = leaf_basis.reshape(leaf_count, leaf_size, rank_count)
    local_weights = weights.reshape(leaf_count, leaf_size, rhs_count)
    first_leaf = lax.axis_index(FLAT) * leaf_count
    offset = first_leaf - REACH

    left_pairs, right_pairs = halos((points, weights), REACH * leaf_size)
    left_pairs = left_pairs.reshape(REACH, leaf_size, dim_count + rhs_count)
    right_pairs = right_pairs.reshape(REACH, leaf_size, dim_count + rhs_count)

    leaf_mask = (
        lax.broadcasted_iota(jnp.int32, (leaf_count, rank_count), 1) < leaf_rank[:, None]
    ).astype(jnp.float32)
    leaf_up = (
        jnp.einsum("lpk,lpr->lkr", local_bases, local_weights, preferred_element_type=jnp.float32)
        * leaf_mask[:, :, None]
    ).astype(jnp.bfloat16)
    leaf_coords = select_within(local_points, leaf_skeleton)
    own_rows = jnp.concatenate([leaf_coords, leaf_up], axis=-1)
    skeleton_width = dim_count + rhs_count
    left_rows, right_rows = halos(
        (own_rows.reshape(leaf_count * rank_count, skeleton_width),), REACH * rank_count
    )

    node_mask = (jnp.arange(node_width, dtype=jnp.int32) < node_rank[0]).astype(jnp.float32)
    node_up = (
        jnp.einsum(
            "ak,ar->kr",
            node_basis,
            leaf_up.reshape(leaf_count * rank_count, rhs_count),
            preferred_element_type=jnp.float32,
        )
        * node_mask[:, None]
    ).astype(jnp.bfloat16)
    node_coords = select_rows(
        leaf_coords.reshape(leaf_count * rank_count, dim_count), node_skeleton[0]
    )
    columns = lax.axis_size("col")
    source_columns = node_far[0] % columns
    node_pack = jnp.concatenate([node_coords, node_up, group_basis], axis=1)
    gathered = lax.all_gather(node_pack[None], "col", axis=0, tiled=True)

    near_local = near_list - offset
    local_norms = scaled_norms(local_points)
    near_inner = near_field(local_points, local_weights, local_norms, near_local)
    all_coords = gathered[:, :, :dim_count]
    all_up = gathered[:, :, dim_count : dim_count + rhs_count]
    all_parts = gathered[:, :, dim_count + rhs_count :]
    picked_coords = select_rows(all_coords, source_columns)
    picked_up = select_rows(all_up, source_columns)
    kernel = kernel_block(jnp.broadcast_to(node_coords, picked_coords.shape), picked_coords)
    node_side = jnp.einsum("fab,fbr->ar", kernel, picked_up, preferred_element_type=jnp.float32)
    group_mask = (jnp.arange(group_width, dtype=jnp.int32) < group_rank[0]).astype(jnp.float32)
    group_up = (
        jnp.einsum("nag,nar->gr", all_parts, all_up, preferred_element_type=jnp.float32)
        * group_mask[:, None]
    ).astype(jnp.bfloat16)
    group_coords = select_rows(all_coords.reshape(columns * node_width, dim_count), group_skeleton[0])
    group_pack = jnp.concatenate([group_coords, group_up], axis=1)
    near_total = near_field(
        local_points,
        local_weights,
        local_norms,
        near_local,
        (left_pairs, right_pairs),
        near_inner,
    )
    near_total, left_rows, right_rows = lax.optimization_barrier((near_total, left_rows, right_rows))

    left_rows = left_rows.reshape(REACH, rank_count, skeleton_width)
    right_rows = right_rows.reshape(REACH, rank_count, skeleton_width)
    far_local = far_list - offset
    coord_norms = scaled_norms(leaf_coords)
    far_inner = far_field(leaf_coords, own_rows, coord_norms, far_local)
    far_total = far_field(
        leaf_coords,
        own_rows,
        coord_norms,
        far_local,
        (left_rows, right_rows),
        far_inner,
        group_pack,
    )
    rows = lax.axis_size("row")
    received = [group_pack] + [
        lax.ppermute(group_pack, "row", [(r, (r + shift) % rows) for r in range(rows)])
        for shift in range(1, rows)
    ]
    shifts = (lax.axis_index("row") - group_far[0]) % rows
    picked_group = select_rows(jnp.stack(received), shifts)
    picked_group_coords = picked_group[:, :, :dim_count]
    picked_group_up = picked_group[:, :, dim_count:]
    group_kernel = kernel_block(
        jnp.broadcast_to(group_coords, picked_group_coords.shape), picked_group_coords
    )
    group_down = (
        jnp.einsum("fab,fbr->ar", group_kernel, picked_group_up, preferred_element_type=jnp.float32)
        * group_mask[:, None]
    ).astype(jnp.bfloat16)
    node_down = (
        (jnp.dot(group_basis, group_down, preferred_element_type=jnp.float32) + node_side)
        * node_mask[:, None]
    ).astype(jnp.bfloat16)
    result = final_field(
        leaf_rank,
        node_basis.reshape(leaf_count, rank_count, node_width),
        node_down,
        far_total,
        local_bases,
        near_total,
    )
    return result.reshape(leaf_count * leaf_size, rhs_count)


def solution(mesh):
    in_specs = (
        P(FLAT, None),
        P(FLAT, None),
        P(FLAT, None),
        P(FLAT),
        P(FLAT, None),
        P(FLAT, None),
        P(FLAT, None),
        P(FLAT, None),
        P(FLAT),
        P(FLAT, None),
        P(FLAT, None),
        P(FLAT, None),
        P("row"),
        P("row", None),
        P("row", None),
    )
    out_specs = P(FLAT, None)

    return jax.shard_map(body, mesh=mesh, in_specs=in_specs, out_specs=out_specs, check_vma=False)
```

```python
import jax
import jax.numpy as jnp
from jax import lax
from jax.experimental import pallas as pl
from jax.experimental.pallas import tpu as pltpu
from jax.sharding import PartitionSpec as P


REACH = 8
FLAT = ("row", "col")
DEPTH = 4


def halos(cells, width):
    count = lax.axis_size(FLAT)
    ends = count - 1
    head = jnp.concatenate([cell[:width] for cell in cells], axis=1)
    tail = jnp.concatenate([cell[cell.shape[0] - width :] for cell in cells], axis=1)
    left = lax.ppermute(tail, FLAT, [(i, i + 1) for i in range(ends)])
    right = lax.ppermute(head, FLAT, [(i + 1, i) for i in range(ends)])
    return left, right


def kernel_block(left, right):
    left_square = jnp.sum(jnp.square(left.astype(jnp.float32)), axis=-1)
    right_square = jnp.sum(jnp.square(right.astype(jnp.float32)), axis=-1)
    inner = jnp.einsum("...md,...nd->...mn", left, right, preferred_element_type=jnp.float32)
    distance = left_square[..., :, None] + right_square[..., None, :] - 2.0 * inner
    return jnp.exp(distance * (-2.0 / left.shape[-1])).astype(jnp.bfloat16)


def contract_last(a, b):
    return lax.dot_general(a, b, (((1,), (1,)), ((), ())), preferred_element_type=jnp.float32)


def scaled_kernel(target, target_square, source, source_square=None):
    dims = target.shape[-1]
    if source_square is None:
        wide = source.astype(jnp.float32)
        square = wide * wide
        high = square.astype(jnp.bfloat16)
        low = (square - high.astype(jnp.float32)).astype(jnp.bfloat16)
        ones = jnp.ones((8, dims), jnp.bfloat16)
        summed = contract_last(ones, high) + contract_last(ones, low)
        source_square = summed[0:1] * (-2.0 / dims)
    inner = contract_last(target * jnp.asarray(4.0 / dims, target.dtype), source)
    return jnp.exp((target_square + source_square) + inner).astype(jnp.bfloat16)


def scaled_norms(cells):
    factor = (2.0 / cells.shape[-1]) ** 0.5
    assert factor * factor == 2.0 / cells.shape[-1]
    wide = cells.astype(jnp.float32) * factor
    return jnp.sum(wide * -wide, axis=-1)


def target_square_of(target):
    wide = target.astype(jnp.float32)
    return jnp.sum(wide * wide, axis=-1, keepdims=True) * (-2.0 / target.shape[-1])


def fetch_sources(index_ref, row, count, parts, buffers, sems, slot):
    for position in range(count):
        source = index_ref[row * count + position]
        for which, (halo, mine, left, own, right) in enumerate(parts):
            target = buffers[which](slot, position)
            sem = sems.at[which, slot, position]
            if left is None:
                pltpu.make_async_copy(own(source - halo), target, sem).start()
                continue

            @pl.when(source < halo)
            def _():
                pltpu.make_async_copy(left(source), target, sem).start()

            @pl.when((source >= halo) & (source < halo + mine))
            def _():
                pltpu.make_async_copy(own(source - halo), target, sem).start()

            @pl.when(source >= halo + mine)
            def _():
                pltpu.make_async_copy(right(source - halo - mine), target, sem).start()


def wait_sources(count, parts, buffers, sems, slot):
    for position in range(count):
        for which, (halo, mine, left, own, right) in enumerate(parts):
            pltpu.make_async_copy(
                own(0), buffers[which](slot, position), sems.at[which, slot, position]
            ).wait()


def rows_of(ref):
    return lambda index: ref.at[index]


def row_of(ref):
    return lambda index: ref.at[pl.ds(index, 1)]


def own_norms_only(own):
    return (REACH, own.shape[0], None, row_of(own), None)


def whole_rows(left, own, right):
    return (left.shape[0], own.shape[0], rows_of(left), rows_of(own), rows_of(right))


def own_rows_only(own):
    return (REACH, own.shape[0], None, rows_of(own), None)


def lane_rows(left, own, right, start, width):
    def halo_at(ref):
        return lambda index: ref.at[index, :, pl.ds(start, width)]

    return (left.shape[0], own.shape[0], halo_at(left), rows_of(own), halo_at(right))


def pipelined_sources(index_ref, count, parts, buffers, sems, leaf_of):
    step = pl.program_id(0)
    steps = pl.num_programs(0)
    slot = step % DEPTH

    @pl.when(step == 0)
    def _():
        for ahead in range(DEPTH - 1):

            @pl.when(ahead < steps)
            def _():
                fetch_sources(index_ref, leaf_of(ahead), count, parts, buffers, sems, ahead)

    @pl.when(step + DEPTH - 1 < steps)
    def _():
        fetch_sources(
            index_ref, leaf_of(step + DEPTH - 1), count, parts, buffers, sems, (step + DEPTH - 1) % DEPTH
        )

    wait_sources(count, parts, buffers, sems, slot)
    return slot


def leaf_order(leaves, edges):
    low, high = REACH, leaves - REACH
    if high <= low:
        return (lambda step: step), leaves, None
    if not edges:
        return (lambda step: step + low), high - low, None
    gap = high - low
    return (lambda step: step + gap * jnp.asarray(step >= low, jnp.int32)), leaves - gap, gap


def near_kernel(leaf_of, halo, index_ref, target_ref, *refs):
    inputs = 5 if halo else 3
    out_ref = refs[inputs]
    point_buf, weight_buf, norm_buf, sems = refs[inputs + 1 :]
    count, size, dims = point_buf.shape[1], point_buf.shape[2], point_buf.shape[3]
    buffers = [
        lambda slot, position: point_buf.at[slot, position],
        lambda slot, position: weight_buf.at[slot, position],
    ]
    if halo:
        lpw, op, rpw, ow = refs[:4]
        parts = (
            lane_rows(lpw, op, rpw, 0, dims),
            lane_rows(lpw, ow, rpw, dims, weight_buf.shape[-1]),
        )
    else:
        parts = (own_rows_only(refs[0]), own_rows_only(refs[1]), own_norms_only(refs[2]))
        buffers.append(lambda slot, position: norm_buf.at[slot, :, pl.ds(position * size, size)])
    slot = pipelined_sources(index_ref, count, parts, buffers, sems, leaf_of)
    target = target_ref[0]
    sources = point_buf[slot].reshape(count * size, dims)
    values = weight_buf[slot].reshape(count * size, weight_buf.shape[-1])
    kernel = scaled_kernel(target, target_square_of(target), sources, None if halo else norm_buf[slot])
    out_ref[0] = jnp.dot(kernel, values, preferred_element_type=jnp.float32)


def near_field(local_points, local_weights, local_norms, near_local, halo_inputs=None, previous=None):
    leaves, size, dims = local_points.shape
    rhs = local_weights.shape[-1]
    count = near_local.shape[1]
    halo = halo_inputs is not None
    leaf_of, steps, _ = leaf_order(leaves, halo)
    anywhere = pl.BlockSpec(memory_space=pl.ANY)
    if halo:
        left_pairs, right_pairs = halo_inputs
        inputs = (left_pairs, local_points, right_pairs, local_weights, previous)
    else:
        inputs = (local_points, local_weights, local_norms)
    aliases = {len(inputs) + 1: 0} if previous is not None else {}
    by_leaf = lambda step, index: (leaf_of(step), 0, 0)
    return pl.pallas_call(
        lambda *refs: near_kernel(leaf_of, halo, *refs),
        grid_spec=pltpu.PrefetchScalarGridSpec(
            num_scalar_prefetch=1,
            grid=(steps,),
            in_specs=[pl.BlockSpec((1, size, dims), by_leaf)] + [anywhere] * len(inputs),
            out_specs=pl.BlockSpec((1, size, rhs), by_leaf),
            scratch_shapes=[
                pltpu.VMEM((DEPTH, count, size, dims), local_points.dtype),
                pltpu.VMEM((DEPTH, count, size, rhs), local_weights.dtype),
                pltpu.VMEM((DEPTH, 1, count * size), jnp.float32),
                pltpu.SemaphoreType.DMA((3, DEPTH, count)),
            ],
        ),
        out_shape=jax.ShapeDtypeStruct((leaves, size, rhs), jnp.float32),
        input_output_aliases=aliases,
        compiler_params=pltpu.CompilerParams(dimension_semantics=("arbitrary",)),
    )(near_local.reshape(-1), local_points, *inputs)


def far_kernel(leaf_of, halo, index_ref, target_ref, *refs):
    inputs = 5 if halo else 2
    out_ref = refs[inputs]
    source_buf, norm_buf, sems = refs[inputs + 1 :]
    count, rank = source_buf.shape[1], source_buf.shape[2]
    buffers = [lambda slot, position: source_buf.at[slot, position]]
    if halo:
        ls, os, rs = refs[:3]
        parts = (whole_rows(ls, os, rs),)
    else:
        parts = (own_rows_only(refs[0]), own_norms_only(refs[1]))
        buffers.append(lambda slot, position: norm_buf.at[slot, :, pl.ds(position * rank, rank)])
    slot = pipelined_sources(index_ref, count, parts, buffers, sems, leaf_of)
    target = target_ref[0]
    dims = target.shape[-1]
    sources = source_buf[slot].reshape(count * rank, source_buf.shape[-1])
    kernel = scaled_kernel(
        target, target_square_of(target), sources[:, :dims], None if halo else norm_buf[slot]
    )
    out_ref[0] = jnp.dot(kernel, sources[:, dims:], preferred_element_type=jnp.float32)


def far_field(leaf_coords, own_rows, own_norms, far_local, halo_inputs=None, previous=None, after=None):
    leaves, rank, dims = leaf_coords.shape
    width = own_rows.shape[-1]
    count = far_local.shape[1]
    halo = halo_inputs is not None
    leaf_of, steps, _ = leaf_order(leaves, halo)
    anywhere = pl.BlockSpec(memory_space=pl.ANY)
    if halo:
        left_rows, right_rows = halo_inputs
        inputs = (left_rows, own_rows, right_rows, after, previous)
    else:
        inputs = (own_rows, own_norms)
    aliases = {len(inputs) + 1: 0} if previous is not None else {}
    by_leaf = lambda step, index: (leaf_of(step), 0, 0)
    return pl.pallas_call(
        lambda *refs: far_kernel(leaf_of, halo, *refs),
        grid_spec=pltpu.PrefetchScalarGridSpec(
            num_scalar_prefetch=1,
            grid=(steps,),
            in_specs=[pl.BlockSpec((1, rank, dims), by_leaf)] + [anywhere] * len(inputs),
            out_specs=pl.BlockSpec((1, rank, width - dims), by_leaf),
            scratch_shapes=[
                pltpu.VMEM((DEPTH, count, rank, width), own_rows.dtype),
                pltpu.VMEM((DEPTH, 1, count * rank), jnp.float32),
                pltpu.SemaphoreType.DMA((2, DEPTH, count)),
            ],
        ),
        out_shape=jax.ShapeDtypeStruct((leaves, rank, width - dims), jnp.float32),
        input_output_aliases=aliases,
        compiler_params=pltpu.CompilerParams(dimension_semantics=("arbitrary",)),
    )(far_local.reshape(-1), leaf_coords, *inputs)


def final_kernel(rank_ref, basis_ref, down_ref, far_ref, leaf_base_ref, near_ref, out_ref):
    block = basis_ref.shape[0]
    step = pl.program_id(0)
    down = down_ref[...]
    for inside in range(block):
        total = jnp.dot(basis_ref[inside], down, preferred_element_type=jnp.float32) + far_ref[inside]
        rows = lax.broadcasted_iota(jnp.int32, total.shape, 0)
        leaf_down = jnp.where(rows < rank_ref[step * block + inside], total, 0.0).astype(jnp.bfloat16)
        result = (
            jnp.dot(leaf_base_ref[inside], leaf_down, preferred_element_type=jnp.float32)
            + near_ref[inside]
        )
        out_ref[inside] = result.astype(out_ref.dtype)


def final_field(leaf_rank, bases, node_down, far_total, leaf_bases, near_total):
    leaves, rank, width = bases.shape
    size = leaf_bases.shape[1]
    rhs = near_total.shape[-1]
    block = max(b for b in (1, 2, 3, 4) if leaves % b == 0)

    def own(l, ranks):
        return (l, 0, 0)

    return pl.pallas_call(
        final_kernel,
        grid_spec=pltpu.PrefetchScalarGridSpec(
            num_scalar_prefetch=1,
            grid=(leaves // block,),
            in_specs=[
                pl.BlockSpec((block, rank, width), own),
                pl.BlockSpec(node_down.shape, lambda l, ranks: (0, 0)),
                pl.BlockSpec((block, rank, rhs), own),
                pl.BlockSpec((block, size, rank), own),
                pl.BlockSpec((block, size, rhs), own),
            ],
            out_specs=pl.BlockSpec((block, size, rhs), own),
        ),
        out_shape=jax.ShapeDtypeStruct((leaves, size, rhs), jnp.bfloat16),
    )(leaf_rank, bases, node_down, far_total, leaf_bases, near_total)


def select_rows(table, index):
    count = table.shape[0]
    onehot = (index[:, None] == jnp.arange(count, dtype=jnp.int32)[None, :]).astype(table.dtype)
    picked = jnp.dot(onehot, table.reshape(count, -1), preferred_element_type=jnp.float32).astype(
        table.dtype
    )
    return picked.reshape(index.shape + table.shape[1:])


def select_within(table, index):
    count = table.shape[1]
    onehot = (index[:, :, None] == jnp.arange(count, dtype=jnp.int32)[None, None, :]).astype(
        table.dtype
    )
    return jnp.einsum("bkp,bpc->bkc", onehot, table, preferred_element_type=jnp.float32).astype(
        table.dtype
    )


def body(
    points,
    weights,
    leaf_basis,
    leaf_rank,
    leaf_skeleton,
    near_list,
    far_list,
    node_basis,
    node_rank,
    node_skeleton,
    node_far,
    group_basis,
    group_rank,
    group_skeleton,
    group_far,
):
    leaf_count = leaf_rank.shape[0]
    leaf_size = points.shape[0] // leaf_count
    dim_count = points.shape[1]
    rhs_count = weights.shape[1]
    rank_count = leaf_basis.shape[1]
    node_width = node_basis.shape[1]
    group_width = group_basis.shape[1]
    local_points = points.reshape(leaf_count, leaf_size, dim_count)
    local_bases = leaf_basis.reshape(leaf_count, leaf_size, rank_count)
    local_weights = weights.reshape(leaf_count, leaf_size, rhs_count)
    first_leaf = lax.axis_index(FLAT) * leaf_count
    offset = first_leaf - REACH

    left_pairs, right_pairs = halos((points, weights), REACH * leaf_size)
    left_pairs = left_pairs.reshape(REACH, leaf_size, dim_count + rhs_count)
    right_pairs = right_pairs.reshape(REACH, leaf_size, dim_count + rhs_count)

    leaf_mask = (lax.broadcasted_iota(jnp.int32, (leaf_count, rank_count), 1) < leaf_rank[:, None]).astype(jnp.float32)
    leaf_up = (
        jnp.einsum("lpk,lpr->lkr", local_bases, local_weights, preferred_element_type=jnp.float32)
        * leaf_mask[:, :, None]
    ).astype(jnp.bfloat16)
    leaf_coords = select_within(local_points, leaf_skeleton)
    own_rows = jnp.concatenate([leaf_coords, leaf_up], axis=-1)
    skeleton_width = dim_count + rhs_count
    left_rows, right_rows = halos((own_rows.reshape(leaf_count * rank_count, skeleton_width),), REACH * rank_count)

    node_mask = (jnp.arange(node_width, dtype=jnp.int32) < node_rank[0]).astype(jnp.float32)
    node_up = (
        jnp.einsum(
            "ak,ar->kr",
            node_basis,
            leaf_up.reshape(leaf_count * rank_count, rhs_count),
            preferred_element_type=jnp.float32,
        )
        * node_mask[:, None]
    ).astype(jnp.bfloat16)
    node_coords = select_rows(
        leaf_coords.reshape(leaf_count * rank_count, dim_count), node_skeleton[0]
    )
    columns = lax.axis_size("col")
    source_columns = node_far[0] % columns
    node_pack = jnp.concatenate([node_coords, node_up, group_basis], axis=1)
    gathered = lax.all_gather(node_pack[None], "col", axis=0, tiled=True)

    near_local = near_list - offset
    local_norms = scaled_norms(local_points)
    near_inner = near_field(local_points, local_weights, local_norms, near_local)
    all_coords = gathered[:, :, :dim_count]
    all_up = gathered[:, :, dim_count : dim_count + rhs_count]
    all_parts = gathered[:, :, dim_count + rhs_count :]
    picked_coords = select_rows(all_coords, source_columns)
    picked_up = select_rows(all_up, source_columns)
    kernel = kernel_block(jnp.broadcast_to(node_coords, picked_coords.shape), picked_coords)
    node_side = jnp.einsum("fab,fbr->ar", kernel, picked_up, preferred_element_type=jnp.float32)
    group_mask = (jnp.arange(group_width, dtype=jnp.int32) < group_rank[0]).astype(jnp.float32)
    group_up = (
        jnp.einsum("nag,nar->gr", all_parts, all_up, preferred_element_type=jnp.float32)
        * group_mask[:, None]
    ).astype(jnp.bfloat16)
    group_coords = select_rows(all_coords.reshape(columns * node_width, dim_count), group_skeleton[0])
    group_pack = jnp.concatenate([group_coords, group_up], axis=1)
    near_total = near_field(
        local_points,
        local_weights,
        local_norms,
        near_local,
        (left_pairs, right_pairs),
        near_inner,
    )
    near_total, left_rows, right_rows = lax.optimization_barrier((near_total, left_rows, right_rows))

    left_rows = left_rows.reshape(REACH, rank_count, skeleton_width)
    right_rows = right_rows.reshape(REACH, rank_count, skeleton_width)
    far_local = far_list - offset
    coord_norms = scaled_norms(leaf_coords)
    far_inner = far_field(leaf_coords, own_rows, coord_norms, far_local)
    far_total = far_field(leaf_coords, own_rows, coord_norms, far_local, (left_rows, right_rows), far_inner, group_pack)
    rows = lax.axis_size("row")
    received = [group_pack] + [
        lax.ppermute(group_pack, "row", [(r, (r + shift) % rows) for r in range(rows)])
        for shift in range(1, rows)
    ]
    shifts = (lax.axis_index("row") - group_far[0]) % rows
    picked_group = select_rows(jnp.stack(received), shifts)
    picked_group_coords = picked_group[:, :, :dim_count]
    picked_group_up = picked_group[:, :, dim_count:]
    group_kernel = kernel_block(
        jnp.broadcast_to(group_coords, picked_group_coords.shape), picked_group_coords
    )
    group_down = (
        jnp.einsum("fab,fbr->ar", group_kernel, picked_group_up, preferred_element_type=jnp.float32)
        * group_mask[:, None]
    ).astype(jnp.bfloat16)
    node_down = (
        (jnp.dot(group_basis, group_down, preferred_element_type=jnp.float32) + node_side)
        * node_mask[:, None]
    ).astype(jnp.bfloat16)
    result = final_field(
        leaf_rank,
        node_basis.reshape(leaf_count, rank_count, node_width),
        node_down,
        far_total,
        local_bases,
        near_total,
    )
    return result.reshape(leaf_count * leaf_size, rhs_count)


def solution(mesh):
    in_specs = (
        P(FLAT, None),
        P(FLAT, None),
        P(FLAT, None),
        P(FLAT),
        P(FLAT, None),
        P(FLAT, None),
        P(FLAT, None),
        P(FLAT, None),
        P(FLAT),
        P(FLAT, None),
        P(FLAT, None),
        P(FLAT, None),
        P("row"),
        P("row", None),
        P("row", None),
    )
    out_specs = P(FLAT, None)

    return jax.shard_map(body, mesh=mesh, in_specs=in_specs, out_specs=out_specs, check_vma=False)
```
